128 devices in a mesh: tm: 64 (over x, y_hi, z, core), mp: 2 (over y_lo).
Axes of the slice: x: 4, y: 4 (y_hi: 2, y_lo: 2; y = y_hi * 2 + y_lo), z: 4, core: 2. Of those that a mesh axis runs over, the one named last changes fastest.
Arguments:
- frames: bfloat16 [32768, 1024], P('tm'), may hold values from -24 to 24
- cotangent: bfloat16 [32768, 1024], P('tm'), may hold values from -20 to 20
- weights: bfloat16 [1024, 4, 1024], P(None, None, 'mp'), may hold values from -4 to 4
- summary: bfloat16 [64, 1024], replicated, may hold values from -5 to 5
- owners: int32 [64], replicated, may hold values from 0 to 63, as said below
Outputs:
- grad_frames: bfloat16 [32768, 1024], P(('tm', 'mp'))
- grad_weights: float32 [1024, 4, 1024], P('tm', None, 'mp')
- grad_summary: float32 [64, 1024], replicated
The draws below stay inside these ranges and needn't reach their ends.
Inputs may be any that keep to these rules, and one draw needn't show every extreme that they name: owners[g] is the index of the block of 512 frames that global token g summarizes.
All inputs are finite; a program needn't handle non-finite values.
Results may differ from the reference program's by a relative error of at most 0.04.
Values may be sent and summed in bfloat16 or wider, within the bound.
No kernel may reach another device: no remote copies, remote signals or barrier semaphores. Data moves between devices by JAX's collectives and lax.ppermute only.
A program may use at most 128 MiB of HBM per device.

```python
import math
import jax
import jax.numpy as jnp
from jax import lax

D = 1024
HEAD_DIM = 64
WINDOW = 512
GLOBALS = 64
TOK_DEV = 512
TOKENS = 32768
N_TM = 64


def draw_frames(key, part):
    streams = jax.random.split(key, 3)
    row_scale = jnp.exp(jax.random.uniform(streams[0], (TOKENS, 1), jnp.float32, math.log(0.3), math.log(3.0)))
    col_scale = jnp.exp(jax.random.uniform(streams[1], (1, D), jnp.float32, math.log(0.5), math.log(2.0)))
    result = jnp.clip(jax.random.normal(streams[2], (TOKENS, D), jnp.float32), -4.0, 4.0)
    return (result * row_scale * col_scale).astype(jnp.bfloat16)


def draw_cotangent(key, part):
    streams = jax.random.split(key, 1)
    ramp = jnp.arange(TOKENS, dtype=jnp.float32)[:, None] / TOKENS
    result = jnp.clip(jax.random.normal(streams[0], (TOKENS, D), jnp.float32), -5.0, 5.0)
    result = result * jnp.exp(ramp * math.log(3.0))
    return result.astype(jnp.bfloat16)


def draw_weights(key, part):
    streams = jax.random.split(key, 1)
    result = jnp.clip(jax.random.normal(streams[0], (D, 4, D), jnp.float32), -4.0, 4.0) / math.sqrt(D)
    return result.astype(jnp.bfloat16)


def draw_owners(key, part):
    streams = jax.random.split(key, 3)
    result = jax.random.randint(streams[0], (GLOBALS,), 0, N_TM)
    top_slot = jax.random.randint(streams[1], (), 0, GLOBALS)
    low_slot = (top_slot + 1 + jax.random.randint(streams[2], (), 0, GLOBALS - 1)) % GLOBALS
    slots = jnp.arange(GLOBALS)
    result = jnp.where(slots == top_slot, N_TM - 1, result)
    result = jnp.where(slots == low_slot, 0, result)
    return result.astype(jnp.int32)


def centred(rng, extent, width, most, kind=jnp.bfloat16):
    drawn = width * jax.random.normal(rng, extent, jnp.float32)
    return jnp.clip(drawn, min=-most, max=most).astype(kind)


def setup_inputs(seed: int = 0) -> dict:
    streams_of = jax.random.split(jax.random.key(seed), 6)
    frames = draw_frames(jax.random.fold_in(streams_of[5], 71), 0)
    cotangent = draw_cotangent(jax.random.fold_in(streams_of[5], 71), 0)
    weights = draw_weights(jax.random.fold_in(streams_of[5], 71), 0)
    summary = centred(streams_of[3], (GLOBALS, D), 1.0, 5.0)
    owners = draw_owners(jax.random.fold_in(streams_of[5], 71), 0)
    return dict(frames=frames, cotangent=cotangent, weights=weights, summary=summary, owners=owners)


EPSILON = 1e-05
PRECISE = lax.Precision.HIGHEST

def normalize(rows_in):
    inverse = lax.rsqrt(lax.optimization_barrier(jnp.mean(rows_in * rows_in, axis=-1, keepdims=True)) + EPSILON)
    return (rows_in * inverse, inverse)

def norm_back(gradient, unit_rows, inverse):
    return (gradient - unit_rows * lax.optimization_barrier(jnp.mean(gradient * unit_rows, axis=-1, keepdims=True))) * inverse

def product(form, left, right):
    return jnp.einsum(form, left.astype(jnp.float32), right.astype(jnp.float32), precision=PRECISE)

def window_mask(row_count, lead, root):
    query_pos = lax.broadcasted_iota(jnp.int32, (row_count, row_count + lead), 0)
    key_pos = lax.broadcasted_iota(jnp.int32, (row_count, row_count + lead), 1)
    inside = (key_pos > query_pos) & (key_pos <= query_pos + lead)
    return inside & (root - lead + key_pos >= 0)

def block_pass(queries, keys_ext, values_ext, keys_glob, values_glob, grad_rows, allowed):
    scaling = HEAD_DIM ** (-0.5)
    near_scores = product('qhe,khe->hqk', queries, keys_ext) * scaling
    far_scores = product('qhe,khe->hqk', queries, keys_glob) * scaling
    near_scores = jnp.where(allowed[None, :, :], near_scores, -jnp.inf)
    row_top = jnp.maximum(lax.optimization_barrier(jnp.max(near_scores, axis=-1, keepdims=True)), lax.optimization_barrier(jnp.max(far_scores, axis=-1, keepdims=True)))
    near_exp = jnp.exp(near_scores - row_top)
    far_exp = jnp.exp(far_scores - row_top)
    row_total = lax.optimization_barrier(jnp.sum(near_exp, axis=-1, keepdims=True)) + lax.optimization_barrier(jnp.sum(far_exp, axis=-1, keepdims=True))
    near_prob = (near_exp / row_total).astype(jnp.bfloat16)
    far_prob = (far_exp / row_total).astype(jnp.bfloat16)
    attended = (product('hqk,khe->qhe', near_prob, values_ext) + product('hqk,khe->qhe', far_prob, values_glob)).astype(jnp.bfloat16)
    near_dot = product('qhe,khe->hqk', grad_rows, values_ext)
    far_dot = product('qhe,khe->hqk', grad_rows, values_glob)
    near_p32 = near_prob.astype(jnp.float32)
    far_p32 = far_prob.astype(jnp.float32)
    row_delta = lax.optimization_barrier(jnp.sum(near_p32 * near_dot, axis=-1, keepdims=True)) + lax.optimization_barrier(jnp.sum(far_p32 * far_dot, axis=-1, keepdims=True))
    near_grad = (near_p32 * (near_dot - row_delta) * scaling).astype(jnp.bfloat16)
    far_grad = (far_p32 * (far_dot - row_delta) * scaling).astype(jnp.bfloat16)
    query_grad = (product('hqk,khe->qhe', near_grad, keys_ext) + product('hqk,khe->qhe', far_grad, keys_glob)).astype(jnp.bfloat16)
    key_grad = product('hqk,qhe->khe', near_grad, queries)
    value_grad = product('hqk,qhe->khe', near_prob, grad_rows)
    glob_key_grad = product('hqk,qhe->khe', far_grad, queries)
    glob_value_grad = product('hqk,qhe->khe', far_prob, grad_rows)
    return (attended, query_grad, key_grad, value_grad, glob_key_grad, glob_value_grad)

def reference(frames, cotangent, weights, summary, owners):
    heads = D // HEAD_DIM
    frames32 = frames.astype(jnp.float32)
    unit_rows, inverse = normalize(frames32)
    normed = unit_rows.astype(jnp.bfloat16)
    block_mean = lax.optimization_barrier(jnp.mean(frames32.reshape(N_TM, TOK_DEV, D), axis=1))
    pool_unit, pool_inv = normalize(block_mean)
    pooled = pool_unit.astype(jnp.bfloat16)
    choose = (owners[:, None] == jnp.arange(N_TM, dtype=jnp.int32)[None, :]).astype(jnp.float32)
    anchor = summary.astype(jnp.float32) + jnp.dot(choose, pooled.astype(jnp.float32), precision=PRECISE)
    glob_unit, glob_inv = normalize(anchor)
    glob_normed = glob_unit.astype(jnp.bfloat16)
    project = weights[:, :3, :].reshape(D, 3 * D)
    kv_weights = weights[:, 1:3, :].reshape(D, 2 * D)
    qkv = jnp.dot(normed, project, preferred_element_type=jnp.float32).astype(jnp.bfloat16)
    queries = qkv[:, :D].reshape(TOKENS, heads, HEAD_DIM)
    zeros_pad = jnp.zeros((WINDOW, D), jnp.bfloat16)
    keys_pad = jnp.concatenate([zeros_pad, qkv[:, D:2 * D]], 0).reshape(TOKENS + WINDOW, heads, HEAD_DIM)
    values_pad = jnp.concatenate([zeros_pad, qkv[:, 2 * D:]], 0).reshape(TOKENS + WINDOW, heads, HEAD_DIM)
    glob_kv = jnp.dot(glob_normed, kv_weights, preferred_element_type=jnp.float32).astype(jnp.bfloat16)
    keys_glob = glob_kv[:, :D].reshape(GLOBALS, heads, HEAD_DIM)
    values_glob = glob_kv[:, D:].reshape(GLOBALS, heads, HEAD_DIM)
    grad_attended = jnp.dot(cotangent, weights[:, 3, :], preferred_element_type=jnp.float32).astype(jnp.bfloat16)
    grad_attended = grad_attended.reshape(TOKENS, heads, HEAD_DIM)

    def block_step(index, carry):
        attended_all, grad_q_all, grad_kp, grad_vp, grad_kg, grad_vg = carry
        first_row = (index * WINDOW).astype(jnp.int32)
        allowed = window_mask(WINDOW, WINDOW, first_row)
        results = block_pass(lax.dynamic_slice_in_dim(queries, first_row, WINDOW, 0), lax.dynamic_slice_in_dim(keys_pad, first_row, 2 * WINDOW, 0), lax.dynamic_slice_in_dim(values_pad, first_row, 2 * WINDOW, 0), keys_glob, values_glob, lax.dynamic_slice_in_dim(grad_attended, first_row, WINDOW, 0), allowed)
        attended_all = lax.dynamic_update_slice_in_dim(attended_all, results[0], first_row, 0)
        grad_q_all = lax.dynamic_update_slice_in_dim(grad_q_all, results[1], first_row, 0)
        grad_kp = lax.dynamic_update_slice_in_dim(grad_kp, lax.dynamic_slice_in_dim(grad_kp, first_row, 2 * WINDOW, 0) + results[2], first_row, 0)
        grad_vp = lax.dynamic_update_slice_in_dim(grad_vp, lax.dynamic_slice_in_dim(grad_vp, first_row, 2 * WINDOW, 0) + results[3], first_row, 0)
        return (attended_all, grad_q_all, grad_kp, grad_vp, grad_kg + results[4], grad_vg + results[5])
    start_carry = (jnp.zeros((TOKENS, heads, HEAD_DIM), jnp.bfloat16), jnp.zeros((TOKENS, heads, HEAD_DIM), jnp.bfloat16), jnp.zeros((TOKENS + WINDOW, heads, HEAD_DIM), jnp.float32), jnp.zeros((TOKENS + WINDOW, heads, HEAD_DIM), jnp.float32), jnp.zeros((GLOBALS, heads, HEAD_DIM), jnp.float32), jnp.zeros((GLOBALS, heads, HEAD_DIM), jnp.float32))
    attended_all, grad_q_all, grad_kp, grad_vp, grad_kg, grad_vg = lax.fori_loop(0, TOKENS // WINDOW, block_step, start_carry)
    attended = attended_all.reshape(TOKENS, D)
    grad_cat = jnp.concatenate([grad_q_all.reshape(TOKENS, D), grad_kp[WINDOW:].reshape(TOKENS, D).astype(jnp.bfloat16), grad_vp[WINDOW:].reshape(TOKENS, D).astype(jnp.bfloat16)], 1)
    feature_grads = lax.dot_general(grad_cat, project, (((1,), (1,)), ((), ())), preferred_element_type=jnp.float32)
    glob_grads = jnp.concatenate([grad_kg.reshape(GLOBALS, D), grad_vg.reshape(GLOBALS, D)], 1)
    summary_features = lax.dot_general(glob_grads, kv_weights.astype(jnp.float32), (((1,), (1,)), ((), ())), precision=PRECISE)
    grad_summary = norm_back(summary_features, glob_unit, glob_inv)
    pool_grads = lax.dot_general(choose, grad_summary, (((0,), (0,)), ((), ())), precision=PRECISE)
    mean_grads = norm_back(pool_grads, pool_unit, pool_inv) / TOK_DEV
    grad_frames = cotangent.astype(jnp.float32) + norm_back(feature_grads, unit_rows, inverse) + jnp.repeat(mean_grads, TOK_DEV, axis=0)
    inner = lax.dot_general(normed, grad_cat, (((0,), (0,)), ((), ())), preferred_element_type=jnp.float32)
    glob_term = lax.dot_general(glob_normed.astype(jnp.float32), glob_grads, (((0,), (0,)), ((), ())), precision=PRECISE)
    inner = inner + jnp.concatenate([jnp.zeros((D, D), jnp.float32), glob_term], 1)
    last_term = lax.dot_general(cotangent, attended, (((0,), (0,)), ((), ())), preferred_element_type=jnp.float32)
    grad_weights = jnp.concatenate([inner.reshape(D, 3, D), last_term.reshape(D, 1, D)], 1)
    return (grad_frames.astype(jnp.bfloat16), grad_weights, grad_summary)
```

```python
import jax
import jax.numpy as jnp
from jax import lax
from jax.sharding import PartitionSpec as P

HEAD_DIM = 64
WINDOW = 512


EPSILON = 1e-05
PRECISE = lax.Precision.HIGHEST


def from_behind(shard, axis, by):
    devices = lax.axis_size(axis)
    pairs = [(i, i + by) for i in range(devices) if 0 <= i + by < devices]
    return lax.ppermute(shard, axis, pairs)


def normalize(rows_in):
    inverse = lax.rsqrt(jnp.mean(rows_in * rows_in, axis=-1, keepdims=True) + EPSILON)
    return (rows_in * inverse, inverse)


def norm_back(gradient, unit_rows, inverse):
    return (gradient - unit_rows * jnp.mean(gradient * unit_rows, axis=-1, keepdims=True)) * inverse


def product(form, left, right):
    return jnp.einsum(form, left, right, preferred_element_type=jnp.float32)


def window_mask(row_count, lead, root):
    query_pos = lax.broadcasted_iota(jnp.int32, (row_count, row_count + lead), 0)
    key_pos = lax.broadcasted_iota(jnp.int32, (row_count, row_count + lead), 1)
    inside = (key_pos > query_pos) & (key_pos <= query_pos + lead)
    return inside & (root - lead + key_pos >= 0)


def block_pass(queries, keys_ext, values_ext, keys_glob, values_glob, grad_rows, allowed):
    scaling = HEAD_DIM ** (-0.5)
    near_scores = product("qhe,khe->hqk", queries, keys_ext) * scaling
    far_scores = product("qhe,khe->hqk", queries, keys_glob) * scaling
    near_scores = jnp.where(allowed[None, :, :], near_scores, -jnp.inf)
    row_top = jnp.maximum(
        jnp.max(near_scores, axis=-1, keepdims=True), jnp.max(far_scores, axis=-1, keepdims=True)
    )
    near_exp = jnp.exp(near_scores - row_top)
    far_exp = jnp.exp(far_scores - row_top)
    row_total = jnp.sum(near_exp, axis=-1, keepdims=True) + jnp.sum(far_exp, axis=-1, keepdims=True)
    near_prob = (near_exp / row_total).astype(jnp.bfloat16)
    far_prob = (far_exp / row_total).astype(jnp.bfloat16)
    attended = (
        product("hqk,khe->qhe", near_prob, values_ext)
        + product("hqk,khe->qhe", far_prob, values_glob)
    ).astype(jnp.bfloat16)
    near_dot = product("qhe,khe->hqk", grad_rows, values_ext)
    far_dot = product("qhe,khe->hqk", grad_rows, values_glob)
    near_p32 = near_prob.astype(jnp.float32)
    far_p32 = far_prob.astype(jnp.float32)
    row_delta = jnp.sum(near_p32 * near_dot, axis=-1, keepdims=True) + jnp.sum(
        far_p32 * far_dot, axis=-1, keepdims=True
    )
    near_grad = (near_p32 * (near_dot - row_delta) * scaling).astype(jnp.bfloat16)
    far_grad = (far_p32 * (far_dot - row_delta) * scaling).astype(jnp.bfloat16)
    query_grad = (
        product("hqk,khe->qhe", near_grad, keys_ext) + product("hqk,khe->qhe", far_grad, keys_glob)
    ).astype(jnp.bfloat16)
    key_grad = product("hqk,qhe->khe", near_grad, queries)
    value_grad = product("hqk,qhe->khe", near_prob, grad_rows)
    glob_key_grad = product("hqk,qhe->khe", far_grad, queries)
    glob_value_grad = product("hqk,qhe->khe", far_prob, grad_rows)
    return (attended, query_grad, key_grad, value_grad, glob_key_grad, glob_value_grad)


def shards(frames, cotangent, weights, summary, owners):
    rows_here = frames.shape[0]
    width = frames.shape[1]
    local_width = weights.shape[2]
    heads_here = local_width // HEAD_DIM
    glob_count = summary.shape[0]
    shard_index = lax.axis_index("tm")
    shard_total = lax.axis_size("tm")
    mp_index = lax.axis_index("mp")
    mp_total = lax.axis_size("mp")
    frames32 = frames.astype(jnp.float32)
    unit_rows, inverse = normalize(frames32)
    normed = unit_rows.astype(jnp.bfloat16)
    block_mean = jnp.mean(frames32, axis=0, keepdims=True)
    pool_unit, pool_inv = normalize(block_mean)
    pooled = pool_unit.astype(jnp.bfloat16)
    pooled_rows = jnp.concatenate([pooled, frames[1:8]], 0)
    pooled_all = lax.all_gather(pooled_rows, "tm", axis=0, tiled=False)[:, 0, :]
    owned_mask = (owners == shard_index).astype(jnp.float32)[:, None]
    anchor = summary.astype(jnp.float32) + jnp.take(pooled_all, owners, axis=0).astype(jnp.float32)
    glob_unit, glob_inv = normalize(anchor)
    glob_normed = glob_unit.astype(jnp.bfloat16)
    kv_weights = weights[:, 1:3, :].reshape(width, 2 * local_width)
    glob_kv = jnp.dot(glob_normed, kv_weights, preferred_element_type=jnp.float32).astype(jnp.bfloat16)
    project = weights[:, :3, :].reshape(width, 3 * local_width)
    qkv = jnp.dot(normed, project, preferred_element_type=jnp.float32).astype(jnp.bfloat16)
    keys_local = qkv[:, local_width : 2 * local_width]
    values_local = qkv[:, 2 * local_width :]
    queries = qkv[:, :local_width].reshape(rows_here, heads_here, HEAD_DIM)
    grad_attended = jnp.dot(cotangent, weights[:, 3, :], preferred_element_type=jnp.float32).astype(
        jnp.bfloat16
    )
    grad_attended = grad_attended.reshape(rows_here, heads_here, HEAD_DIM)
    edge_keys, edge_values = from_behind((keys_local, values_local), "tm", 1)
    keys_ext = jnp.concatenate([edge_keys, keys_local], 0).reshape(
        rows_here + WINDOW, heads_here, HEAD_DIM
    )
    values_ext = jnp.concatenate([edge_values, values_local], 0).reshape(
        rows_here + WINDOW, heads_here, HEAD_DIM
    )
    keys_glob = glob_kv[:, :local_width].reshape(glob_count, heads_here, HEAD_DIM)
    values_glob = glob_kv[:, local_width:].reshape(glob_count, heads_here, HEAD_DIM)
    allowed = window_mask(WINDOW, WINDOW, shard_index * rows_here + 0)
    results = block_pass(
        queries, keys_ext, values_ext, keys_glob, values_glob, grad_attended, allowed
    )
    attended = results[0].reshape(rows_here, local_width)
    grad_queries = results[1].reshape(rows_here, local_width)
    grad_kp = results[2].reshape(rows_here + WINDOW, local_width)
    grad_vp = results[3].reshape(rows_here + WINDOW, local_width)
    grad_kg = results[4].reshape(glob_count, local_width)
    grad_vg = results[5].reshape(glob_count, local_width)
    back_keys, back_values = from_behind(
        (grad_kp[:WINDOW].astype(jnp.bfloat16), grad_vp[:WINDOW].astype(jnp.bfloat16)), "tm", -1
    )
    grad_keys = grad_kp[WINDOW:].at[rows_here - WINDOW :].add(back_keys.astype(jnp.float32))
    grad_values = grad_vp[WINDOW:].at[rows_here - WINDOW :].add(back_values.astype(jnp.float32))
    grad_cat = jnp.concatenate(
        [grad_queries, grad_keys.astype(jnp.bfloat16), grad_values.astype(jnp.bfloat16)], 1
    )
    glob_grads = jnp.concatenate([grad_kg, grad_vg], 1)
    kv_weights32 = kv_weights.astype(jnp.float32)
    local_features = lax.dot_general(
        glob_grads, kv_weights32, (((1,), (1,)), ((), ())), precision=PRECISE
    )
    summary_features = lax.psum(local_features, ("tm", "mp"))
    grad_summary = norm_back(summary_features, glob_unit, glob_inv)
    pool_grads = lax.dot_general(
        owned_mask, grad_summary, (((0,), (0,)), ((), ())), precision=PRECISE
    )
    mean_grads = norm_back(pool_grads, pool_unit, pool_inv) / rows_here
    half_rows = rows_here // mp_total
    start_row = mp_index * half_rows
    other_row = (1 - mp_index) * half_rows
    feature_all = lax.dot_general(
        grad_cat, project, (((1,), (1,)), ((), ())), preferred_element_type=jnp.float32
    )
    mine = lax.dynamic_slice_in_dim(feature_all, start_row, half_rows, 0)
    theirs = lax.dynamic_slice_in_dim(feature_all, other_row, half_rows, 0).astype(jnp.bfloat16)
    received = lax.ppermute(theirs, "mp", [(0, 1), (1, 0)])
    feature_grads = mine + received.astype(jnp.float32)
    my_unit = lax.dynamic_slice_in_dim(unit_rows, start_row, half_rows, 0)
    my_inverse = lax.dynamic_slice_in_dim(inverse, start_row, half_rows, 0)
    my_cotangent = lax.dynamic_slice_in_dim(cotangent, start_row, half_rows, 0).astype(jnp.float32)
    grad_frames = (
        my_cotangent + norm_back(feature_grads, my_unit, my_inverse) + mean_grads
    ).astype(jnp.bfloat16)
    glob_cols = glob_normed.astype(jnp.float32)
    inner = lax.dot_general(
        normed, grad_cat, (((0,), (0,)), ((), ())), preferred_element_type=jnp.float32
    )
    glob_term = lax.dot_general(glob_cols, glob_grads, (((0,), (0,)), ((), ())), precision=PRECISE)
    inner = inner + jnp.concatenate([jnp.zeros((width, local_width), jnp.float32), glob_term], 1)
    last_term = lax.dot_general(
        cotangent, attended, (((0,), (0,)), ((), ())), preferred_element_type=jnp.float32
    )
    weight_parts = jnp.concatenate(
        [inner.reshape(width, 3, local_width), last_term.reshape(width, 1, local_width)], 1
    )
    grad_weights = lax.psum_scatter(
        weight_parts.reshape(width, 4 * local_width), "tm", scatter_dimension=0, tiled=True
    ).reshape(width // shard_total, 4, local_width)
    return (grad_frames, grad_weights, grad_summary)


def solution(mesh):
    in_specs = (P("tm", None), P("tm", None), P(None, None, "mp"), P(), P())
    out_specs = (P(("tm", "mp"), None), P("tm", None, "mp"), P())
    return jax.shard_map(shards, mesh=mesh, in_specs=in_specs, out_specs=out_specs, check_vma=False)
```

```python
import numpy as np
import jax
import jax.numpy as jnp
from jax import lax
from jax.sharding import PartitionSpec as P

HEAD_DIM = 64
WINDOW = 512


EPSILON = 1e-05
PRECISE = lax.Precision.HIGHEST


def from_behind(shard, axis, by):
    devices = lax.axis_size(axis)
    pairs = [(i, i + by) for i in range(devices) if 0 <= i + by < devices]
    return lax.ppermute(shard, axis, pairs)


def tm_coords(i):
    return (i >> 4) & 3, (i >> 3) & 1, (i >> 1) & 3, i & 1


def tm_index(x, y_half, z, core):
    return ((x * 2 + y_half) * 4 + z) * 2 + core


def butterfly_plan():
    pairs, bits = [], np.zeros((64, 6), np.int32)
    flips = [("z", 1), ("x", 1), ("z", 2), ("x", 2), ("y", 1)]
    round_pairs = [[(i, i ^ 1) for i in range(64)]]
    for i in range(64):
        bits[i, 0] = i & 1
    for r, (axis, mask) in enumerate(flips):
        these = []
        for i in range(64):
            x, y_half, z, core = tm_coords(i)
            zl, xl = (z + core) % 4, (x + core) % 4
            label = {"z": zl, "x": xl, "y": y_half}[axis]
            bits[i, r + 1] = 1 if label & mask else 0
            if axis == "z":
                z = ((zl ^ mask) - core) % 4
            elif axis == "x":
                x = ((xl ^ mask) - core) % 4
            else:
                y_half ^= 1
            these.append((i, tm_index(x, y_half, z, core)))
        round_pairs.append(these)
    pairs = round_pairs
    return pairs, bits


def to_positions(a):
    rows = a.shape[0]
    r = a.reshape(rows, 4, 2, 4, 2, 16)
    first = r[:, :, :, :, 0, :]
    second = jnp.roll(jnp.roll(r[:, :, :, :, 1, :], 1, axis=1), 1, axis=3)
    g = jnp.stack([first, second], axis=1).reshape(rows, 2, 2, 2, 2, 2, 2, 16)
    g = g.transpose(0, 1, 6, 3, 5, 2, 4, 7)
    return g.reshape(rows, 1024)


def butterfly(parts, glob, shard_index):
    pairs, bits = butterfly_plan()
    my_bits = jnp.asarray(bits)[shard_index]
    for r in range(6):
        half = parts.shape[0] // 2
        b = my_bits[r]
        keep = lax.dynamic_slice_in_dim(parts, b * half, half, 0)
        send = lax.dynamic_slice_in_dim(parts, (1 - b) * half, half, 0)
        got, got_glob = lax.ppermute((send, glob), "tm", pairs[r])
        parts = keep + got
        glob = glob + got_glob
    return parts, glob


def normalize(rows_in):
    inverse = lax.rsqrt(jnp.mean(rows_in * rows_in, axis=-1, keepdims=True) + EPSILON)
    return (rows_in * inverse, inverse)


def norm_back(gradient, unit_rows, inverse):
    return (gradient - unit_rows * jnp.mean(gradient * unit_rows, axis=-1, keepdims=True)) * inverse


def product(form, left, right):
    return jnp.einsum(form, left, right, preferred_element_type=jnp.float32)


def window_mask(row_count, lead, root):
    query_pos = lax.broadcasted_iota(jnp.int32, (row_count, row_count + lead), 0)
    key_pos = lax.broadcasted_iota(jnp.int32, (row_count, row_count + lead), 1)
    inside = (key_pos > query_pos) & (key_pos <= query_pos + lead)
    return inside & (root - lead + key_pos >= 0)


def block_pass(queries, keys_ext, values_ext, keys_glob, values_glob, grad_rows, allowed):
    scaling = HEAD_DIM ** (-0.5)
    near_scores = product("qhe,khe->hqk", queries, keys_ext) * scaling
    far_scores = product("qhe,khe->hqk", queries, keys_glob) * scaling
    near_scores = jnp.where(allowed[None, :, :], near_scores, -jnp.inf)
    row_top = jnp.maximum(
        jnp.max(near_scores, axis=-1, keepdims=True), jnp.max(far_scores, axis=-1, keepdims=True)
    )
    near_exp = jnp.exp(near_scores - row_top)
    far_exp = jnp.exp(far_scores - row_top)
    row_total = jnp.sum(near_exp, axis=-1, keepdims=True) + jnp.sum(far_exp, axis=-1, keepdims=True)
    near_prob = (near_exp / row_total).astype(jnp.bfloat16)
    far_prob = (far_exp / row_total).astype(jnp.bfloat16)
    attended = (
        product("hqk,khe->qhe", near_prob, values_ext)
        + product("hqk,khe->qhe", far_prob, values_glob)
    ).astype(jnp.bfloat16)
    near_dot = product("qhe,khe->hqk", grad_rows, values_ext)
    far_dot = product("qhe,khe->hqk", grad_rows, values_glob)
    near_p32 = near_prob.astype(jnp.float32)
    far_p32 = far_prob.astype(jnp.float32)
    row_delta = jnp.sum(near_p32 * near_dot, axis=-1, keepdims=True) + jnp.sum(
        far_p32 * far_dot, axis=-1, keepdims=True
    )
    near_grad = (near_p32 * (near_dot - row_delta) * scaling).astype(jnp.bfloat16)
    far_grad = (far_p32 * (far_dot - row_delta) * scaling).astype(jnp.bfloat16)
    query_grad = (
        product("hqk,khe->qhe", near_grad, keys_ext) + product("hqk,khe->qhe", far_grad, keys_glob)
    ).astype(jnp.bfloat16)
    key_grad = product("hqk,qhe->khe", near_grad, queries)
    value_grad = product("hqk,qhe->khe", near_prob, grad_rows)
    glob_key_grad = product("hqk,qhe->khe", far_grad, queries)
    glob_value_grad = product("hqk,qhe->khe", far_prob, grad_rows)
    return (attended, query_grad, key_grad, value_grad, glob_key_grad, glob_value_grad)


def shards(frames, cotangent, weights, summary, owners):
    rows_here = frames.shape[0]
    width = frames.shape[1]
    local_width = weights.shape[2]
    heads_here = local_width // HEAD_DIM
    glob_count = summary.shape[0]
    shard_index = lax.axis_index("tm")
    shard_total = lax.axis_size("tm")
    mp_index = lax.axis_index("mp")
    mp_total = lax.axis_size("mp")
    frames32 = frames.astype(jnp.float32)
    unit_rows, inverse = normalize(frames32)
    normed = unit_rows.astype(jnp.bfloat16)
    block_mean = jnp.mean(frames32, axis=0, keepdims=True)
    pool_unit, pool_inv = normalize(block_mean)
    pooled = pool_unit.astype(jnp.bfloat16)
    pooled_rows = jnp.concatenate([pooled, frames[1:8]], 0)
    pooled_all = lax.all_gather(pooled_rows, "tm", axis=0, tiled=False)[:, 0, :]
    owned_mask = (owners == shard_index).astype(jnp.float32)[:, None]
    anchor = summary.astype(jnp.float32) + jnp.take(pooled_all, owners, axis=0).astype(jnp.float32)
    glob_unit, glob_inv = normalize(anchor)
    glob_normed = glob_unit.astype(jnp.bfloat16)
    kv_weights = weights[:, 1:3, :].reshape(width, 2 * local_width)
    glob_kv = jnp.dot(glob_normed, kv_weights, preferred_element_type=jnp.float32).astype(jnp.bfloat16)
    project = weights[:, :3, :].reshape(width, 3 * local_width)
    qkv = jnp.dot(normed, project, preferred_element_type=jnp.float32).astype(jnp.bfloat16)
    keys_local = qkv[:, local_width : 2 * local_width]
    values_local = qkv[:, 2 * local_width :]
    queries = qkv[:, :local_width].reshape(rows_here, heads_here, HEAD_DIM)
    grad_attended = jnp.dot(cotangent, weights[:, 3, :], preferred_element_type=jnp.float32).astype(
        jnp.bfloat16
    )
    grad_attended = grad_attended.reshape(rows_here, heads_here, HEAD_DIM)
    edge_keys, edge_values = from_behind((keys_local, values_local), "tm", 1)
    keys_ext = jnp.concatenate([edge_keys, keys_local], 0).reshape(
        rows_here + WINDOW, heads_here, HEAD_DIM
    )
    values_ext = jnp.concatenate([edge_values, values_local], 0).reshape(
        rows_here + WINDOW, heads_here, HEAD_DIM
    )
    keys_glob = glob_kv[:, :local_width].reshape(glob_count, heads_here, HEAD_DIM)
    values_glob = glob_kv[:, local_width:].reshape(glob_count, heads_here, HEAD_DIM)
    allowed = window_mask(WINDOW, WINDOW, shard_index * rows_here + 0)
    results = block_pass(
        queries, keys_ext, values_ext, keys_glob, values_glob, grad_attended, allowed
    )
    attended = results[0].reshape(rows_here, local_width)
    grad_queries = results[1].reshape(rows_here, local_width)
    grad_kp = results[2].reshape(rows_here + WINDOW, local_width)
    grad_vp = results[3].reshape(rows_here + WINDOW, local_width)
    grad_kg = results[4].reshape(glob_count, local_width)
    grad_vg = results[5].reshape(glob_count, local_width)
    back_keys, back_values = from_behind(
        (grad_kp[:WINDOW].astype(jnp.bfloat16), grad_vp[:WINDOW].astype(jnp.bfloat16)), "tm", -1
    )
    grad_keys = grad_kp[WINDOW:].at[rows_here - WINDOW :].add(back_keys.astype(jnp.float32))
    grad_values = grad_vp[WINDOW:].at[rows_here - WINDOW :].add(back_values.astype(jnp.float32))
    grad_cat = jnp.concatenate(
        [grad_queries, grad_keys.astype(jnp.bfloat16), grad_values.astype(jnp.bfloat16)], 1
    )
    glob_grads = jnp.concatenate([grad_kg, grad_vg], 1)
    kv_weights32 = kv_weights.astype(jnp.float32)
    local_features = lax.dot_general(
        glob_grads, kv_weights32, (((1,), (1,)), ((), ())), precision=PRECISE
    )
    glob_cols = to_positions(glob_normed).astype(jnp.float32)
    inner = lax.dot_general(
        to_positions(normed), grad_cat, (((0,), (0,)), ((), ())), preferred_element_type=jnp.float32
    )
    glob_term = lax.dot_general(glob_cols, glob_grads, (((0,), (0,)), ((), ())), precision=PRECISE)
    inner = inner + jnp.concatenate([jnp.zeros((width, local_width), jnp.float32), glob_term], 1)
    last_term = lax.dot_general(
        to_positions(cotangent), attended, (((0,), (0,)), ((), ())), preferred_element_type=jnp.float32
    )
    weight_parts = jnp.concatenate(
        [inner.reshape(width, 3, local_width), last_term.reshape(width, 1, local_width)], 1
    )
    weight_rows, tm_features = butterfly(
        weight_parts.reshape(width, 4 * local_width), local_features, shard_index
    )
    grad_weights = weight_rows.reshape(width // shard_total, 4, local_width)
    summary_features = tm_features + lax.ppermute(tm_features, "mp", [(0, 1), (1, 0)])
    grad_summary = norm_back(summary_features, glob_unit, glob_inv)
    pool_grads = lax.dot_general(
        owned_mask, grad_summary, (((0,), (0,)), ((), ())), precision=PRECISE
    )
    mean_grads = norm_back(pool_grads, pool_unit, pool_inv) / rows_here
    half_rows = rows_here // mp_total
    start_row = mp_index * half_rows
    other_row = (1 - mp_index) * half_rows
    feature_all = lax.dot_general(
        grad_cat, project, (((1,), (1,)), ((), ())), preferred_element_type=jnp.float32
    )
    mine = lax.dynamic_slice_in_dim(feature_all, start_row, half_rows, 0)
    theirs = lax.dynamic_slice_in_dim(feature_all, other_row, half_rows, 0).astype(jnp.bfloat16)
    received = lax.ppermute(theirs, "mp", [(0, 1), (1, 0)])
    feature_grads = mine + received.astype(jnp.float32)
    my_unit = lax.dynamic_slice_in_dim(unit_rows, start_row, half_rows, 0)
    my_inverse = lax.dynamic_slice_in_dim(inverse, start_row, half_rows, 0)
    my_cotangent = lax.dynamic_slice_in_dim(cotangent, start_row, half_rows, 0).astype(jnp.float32)
    grad_frames = (
        my_cotangent + norm_back(feature_grads, my_unit, my_inverse) + mean_grads
    ).astype(jnp.bfloat16)
    return (grad_frames, grad_weights, grad_summary)


def solution(mesh):
    in_specs = (P("tm", None), P("tm", None), P(None, None, "mp"), P(), P())
    out_specs = (P(("tm", "mp"), None), P("tm", None, "mp"), P())
    return jax.shard_map(shards, mesh=mesh, in_specs=in_specs, out_specs=out_specs, check_vma=False)
```

```python
import numpy as np
import jax
import jax.numpy as jnp
from jax import lax
from jax.sharding import PartitionSpec as P

HEAD_DIM = 64
WINDOW = 512


EPSILON = 1e-05
PRECISE = lax.Precision.HIGHEST


def from_behind(shard, axis, by):
    devices = lax.axis_size(axis)
    pairs = [(i, i + by) for i in range(devices) if 0 <= i + by < devices]
    return lax.ppermute(shard, axis, pairs)


def tm_coords(i):
    return (i >> 4) & 3, (i >> 3) & 1, (i >> 1) & 3, i & 1


def tm_index(x, y_half, z, core):
    return ((x * 2 + y_half) * 4 + z) * 2 + core


Z_FIRST = (("z", 1), ("x", 1), ("z", 2), ("x", 2), ("y", 1))
X_FIRST = (("x", 1), ("z", 1), ("x", 2), ("z", 2), ("y", 1))


def butterfly_plan(flips):
    pairs, bits = [], np.zeros((64, 6), np.int32)
    round_pairs = [[(i, i ^ 1) for i in range(64)]]
    for i in range(64):
        bits[i, 0] = i & 1
    for r, (axis, mask) in enumerate(flips):
        these = []
        for i in range(64):
            x, y_half, z, core = tm_coords(i)
            zl, xl = (z + core) % 4, (x + core) % 4
            label = {"z": zl, "x": xl, "y": y_half}[axis]
            bits[i, r + 1] = 1 if label & mask else 0
            if axis == "z":
                z = ((zl ^ mask) - core) % 4
            elif axis == "x":
                x = ((xl ^ mask) - core) % 4
            else:
                y_half ^= 1
            these.append((i, tm_index(x, y_half, z, core)))
        round_pairs.append(these)
    pairs = round_pairs
    return pairs, bits


def to_positions(a, flips):
    rows = a.shape[0]
    r = a.reshape(rows, 4, 2, 4, 2, 16)
    first = r[:, :, :, :, 0, :]
    second = jnp.roll(jnp.roll(r[:, :, :, :, 1, :], 1, axis=1), 1, axis=3)
    g = jnp.stack([first, second], axis=1).reshape(rows, 2, 2, 2, 2, 2, 2, 16)
    axis_of = {("z", 1): 6, ("z", 2): 5, ("x", 1): 3, ("x", 2): 2, ("y", 1): 4}
    g = g.transpose(0, 1, *[axis_of[f] for f in flips], 7)
    return g.reshape(rows, 1024)


def butterfly(parts, glob, shard_index, flips=Z_FIRST):
    pairs, bits = butterfly_plan(flips)
    my_bits = jnp.asarray(bits)[shard_index]
    for r in range(6):
        if parts is not None:
            half = parts.shape[0] // 2
            b = my_bits[r]
            keep = lax.dynamic_slice_in_dim(parts, b * half, half, 0)
            send = lax.dynamic_slice_in_dim(parts, (1 - b) * half, half, 0)
            parts = keep + lax.ppermute(send, "tm", pairs[r])
        if glob is not None:
            glob = glob + lax.ppermute(glob, "tm", pairs[r])
    return parts, glob


def normalize(rows_in):
    inverse = lax.rsqrt(jnp.mean(rows_in * rows_in, axis=-1, keepdims=True) + EPSILON)
    return (rows_in * inverse, inverse)


def norm_back(gradient, unit_rows, inverse):
    return (gradient - unit_rows * jnp.mean(gradient * unit_rows, axis=-1, keepdims=True)) * inverse


def product(form, left, right):
    return jnp.einsum(form, left, right, preferred_element_type=jnp.float32)


def window_mask(row_count, lead, root):
    query_pos = lax.broadcasted_iota(jnp.int32, (row_count, row_count + lead), 0)
    key_pos = lax.broadcasted_iota(jnp.int32, (row_count, row_count + lead), 1)
    inside = (key_pos > query_pos) & (key_pos <= query_pos + lead)
    return inside & (root - lead + key_pos >= 0)


def block_pass(queries, keys_ext, values_ext, keys_glob, values_glob, grad_rows, allowed):
    scaling = HEAD_DIM ** (-0.5)
    near_scores = product("qhe,khe->hqk", queries, keys_ext) * scaling
    far_scores = product("qhe,khe->hqk", queries, keys_glob) * scaling
    near_scores = jnp.where(allowed[None, :, :], near_scores, -jnp.inf)
    row_top = jnp.maximum(
        jnp.max(near_scores, axis=-1, keepdims=True), jnp.max(far_scores, axis=-1, keepdims=True)
    )
    near_exp = jnp.exp(near_scores - row_top)
    far_exp = jnp.exp(far_scores - row_top)
    row_total = jnp.sum(near_exp, axis=-1, keepdims=True) + jnp.sum(far_exp, axis=-1, keepdims=True)
    near_prob = (near_exp / row_total).astype(jnp.bfloat16)
    far_prob = (far_exp / row_total).astype(jnp.bfloat16)
    attended = (
        product("hqk,khe->qhe", near_prob, values_ext)
        + product("hqk,khe->qhe", far_prob, values_glob)
    ).astype(jnp.bfloat16)
    near_dot = product("qhe,khe->hqk", grad_rows, values_ext)
    far_dot = product("qhe,khe->hqk", grad_rows, values_glob)
    near_p32 = near_prob.astype(jnp.float32)
    far_p32 = far_prob.astype(jnp.float32)
    row_delta = jnp.sum(near_p32 * near_dot, axis=-1, keepdims=True) + jnp.sum(
        far_p32 * far_dot, axis=-1, keepdims=True
    )
    near_grad = (near_p32 * (near_dot - row_delta) * scaling).astype(jnp.bfloat16)
    far_grad = (far_p32 * (far_dot - row_delta) * scaling).astype(jnp.bfloat16)
    query_grad = (
        product("hqk,khe->qhe", near_grad, keys_ext) + product("hqk,khe->qhe", far_grad, keys_glob)
    ).astype(jnp.bfloat16)
    key_grad = product("hqk,qhe->khe", near_grad, queries)
    value_grad = product("hqk,qhe->khe", near_prob, grad_rows)
    glob_key_grad = product("hqk,qhe->khe", far_grad, queries)
    glob_value_grad = product("hqk,qhe->khe", far_prob, grad_rows)
    return (attended, query_grad, key_grad, value_grad, glob_key_grad, glob_value_grad)


def shards(frames, cotangent, weights, summary, owners):
    rows_here = frames.shape[0]
    width = frames.shape[1]
    local_width = weights.shape[2]
    heads_here = local_width // HEAD_DIM
    glob_count = summary.shape[0]
    shard_index = lax.axis_index("tm")
    shard_total = lax.axis_size("tm")
    mp_index = lax.axis_index("mp")
    mp_total = lax.axis_size("mp")
    frames32 = frames.astype(jnp.float32)
    unit_rows, inverse = normalize(frames32)
    normed = unit_rows.astype(jnp.bfloat16)
    block_mean = jnp.mean(frames32, axis=0, keepdims=True)
    pool_unit, pool_inv = normalize(block_mean)
    pooled = pool_unit.astype(jnp.bfloat16)
    pooled_rows = jnp.concatenate([pooled, frames[1:8]], 0)
    pooled_all = lax.all_gather(pooled_rows, "tm", axis=0, tiled=False)[:, 0, :]
    owned_mask = (owners == shard_index).astype(jnp.float32)[:, None]
    anchor = summary.astype(jnp.float32) + jnp.take(pooled_all, owners, axis=0).astype(jnp.float32)
    glob_unit, glob_inv = normalize(anchor)
    glob_normed = glob_unit.astype(jnp.bfloat16)
    kv_weights = weights[:, 1:3, :].reshape(width, 2 * local_width)
    glob_kv = jnp.dot(glob_normed, kv_weights, preferred_element_type=jnp.float32).astype(jnp.bfloat16)
    project = weights[:, :3, :].reshape(width, 3 * local_width)
    qkv = jnp.dot(normed, project, preferred_element_type=jnp.float32).astype(jnp.bfloat16)
    keys_local = qkv[:, local_width : 2 * local_width]
    values_local = qkv[:, 2 * local_width :]
    queries = qkv[:, :local_width].reshape(rows_here, heads_here, HEAD_DIM)
    grad_attended = jnp.dot(cotangent, weights[:, 3, :], preferred_element_type=jnp.float32).astype(
        jnp.bfloat16
    )
    grad_attended = grad_attended.reshape(rows_here, heads_here, HEAD_DIM)
    edge_keys, edge_values = from_behind((keys_local, values_local), "tm", 1)
    keys_ext = jnp.concatenate([edge_keys, keys_local], 0).reshape(
        rows_here + WINDOW, heads_here, HEAD_DIM
    )
    values_ext = jnp.concatenate([edge_values, values_local], 0).reshape(
        rows_here + WINDOW, heads_here, HEAD_DIM
    )
    keys_glob = glob_kv[:, :local_width].reshape(glob_count, heads_here, HEAD_DIM)
    values_glob = glob_kv[:, local_width:].reshape(glob_count, heads_here, HEAD_DIM)
    allowed = window_mask(WINDOW, WINDOW, shard_index * rows_here + 0)
    groups = 2
    group_heads = heads_here // groups
    group_width = group_heads * HEAD_DIM
    orders = (Z_FIRST, X_FIRST)
    weight_rows = []
    grad_cats = []
    local_features = jnp.zeros((glob_count, width), jnp.float32)
    gate = None
    for g in range(groups):
        heads = slice(g * group_heads, (g + 1) * group_heads)
        cols = slice(g * group_width, (g + 1) * group_width)
        group_inputs = (
            queries[:, heads],
            keys_ext[:, heads],
            values_ext[:, heads],
            keys_glob[:, heads],
            values_glob[:, heads],
            grad_attended[:, heads],
        )
        if gate is not None:
            _, group_inputs = lax.optimization_barrier((gate, group_inputs))
        results = block_pass(*group_inputs, allowed)
        attended = results[0].reshape(rows_here, group_width)
        grad_queries = results[1].reshape(rows_here, group_width)
        grad_kp = results[2].reshape(rows_here + WINDOW, group_width)
        grad_vp = results[3].reshape(rows_here + WINDOW, group_width)
        grad_kg = results[4].reshape(glob_count, group_width)
        grad_vg = results[5].reshape(glob_count, group_width)
        back_keys, back_values = from_behind(
            (grad_kp[:WINDOW].astype(jnp.bfloat16), grad_vp[:WINDOW].astype(jnp.bfloat16)), "tm", -1
        )
        grad_keys = grad_kp[WINDOW:].at[rows_here - WINDOW :].add(back_keys.astype(jnp.float32))
        grad_values = grad_vp[WINDOW:].at[rows_here - WINDOW :].add(back_values.astype(jnp.float32))
        grad_cat = jnp.concatenate(
            [grad_queries, grad_keys.astype(jnp.bfloat16), grad_values.astype(jnp.bfloat16)], 1
        )
        grad_cats.append(grad_cat)
        glob_grads = jnp.concatenate([grad_kg, grad_vg], 1)
        normed_positions = to_positions(normed, orders[g])
        cotangent_positions = to_positions(cotangent, orders[g])
        glob_cols = to_positions(glob_normed, orders[g]).astype(jnp.float32)
        kv_group = weights[:, 1:3, cols].reshape(width, 2 * group_width).astype(jnp.float32)
        local_features = local_features + lax.dot_general(
            glob_grads, kv_group, (((1,), (1,)), ((), ())), precision=PRECISE
        )
        inner = lax.dot_general(
            normed_positions, grad_cat, (((0,), (0,)), ((), ())), preferred_element_type=jnp.float32
        )
        glob_term = lax.dot_general(
            glob_cols, glob_grads, (((0,), (0,)), ((), ())), precision=PRECISE
        )
        inner = inner + jnp.concatenate(
            [jnp.zeros((width, group_width), jnp.float32), glob_term], 1
        )
        last_term = lax.dot_general(
            cotangent_positions, attended, (((0,), (0,)), ((), ())), preferred_element_type=jnp.float32
        )
        weight_parts = jnp.concatenate(
            [inner.reshape(width, 3, group_width), last_term.reshape(width, 1, group_width)], 1
        )
        gate = weight_parts
        reduced, _ = butterfly(
            weight_parts.reshape(width, 4 * group_width), None, shard_index, orders[g]
        )
        weight_rows.append(reduced.reshape(width // shard_total, 4, group_width))
    grad_weights = jnp.concatenate(weight_rows, 2)
    _, tm_features = butterfly(None, local_features, shard_index)
    summary_features = tm_features + lax.ppermute(tm_features, "mp", [(0, 1), (1, 0)])
    grad_summary = norm_back(summary_features, glob_unit, glob_inv)
    pool_grads = lax.dot_general(
        owned_mask, grad_summary, (((0,), (0,)), ((), ())), precision=PRECISE
    )
    mean_grads = norm_back(pool_grads, pool_unit, pool_inv) / rows_here
    half_rows = rows_here // mp_total
    start_row = mp_index * half_rows
    other_row = (1 - mp_index) * half_rows
    feature_all = sum(
        lax.dot_general(
            grad_cats[g],
            weights[:, :3, g * group_width : (g + 1) * group_width].reshape(width, 3 * group_width),
            (((1,), (1,)), ((), ())),
            preferred_element_type=jnp.float32,
        )
        for g in range(groups)
    )
    mine = lax.dynamic_slice_in_dim(feature_all, start_row, half_rows, 0)
    theirs = lax.dynamic_slice_in_dim(feature_all, other_row, half_rows, 0).astype(jnp.bfloat16)
    received = lax.ppermute(theirs, "mp", [(0, 1), (1, 0)])
    feature_grads = mine + received.astype(jnp.float32)
    my_unit = lax.dynamic_slice_in_dim(unit_rows, start_row, half_rows, 0)
    my_inverse = lax.dynamic_slice_in_dim(inverse, start_row, half_rows, 0)
    my_cotangent = lax.dynamic_slice_in_dim(cotangent, start_row, half_rows, 0).astype(jnp.float32)
    grad_frames = (
        my_cotangent + norm_back(feature_grads, my_unit, my_inverse) + mean_grads
    ).astype(jnp.bfloat16)
    return (grad_frames, grad_weights, grad_summary)


def solution(mesh):
    in_specs = (P("tm", None), P("tm", None), P(None, None, "mp"), P(), P())
    out_specs = (P(("tm", "mp"), None), P("tm", None, "mp"), P())
    return jax.shard_map(shards, mesh=mesh, in_specs=in_specs, out_specs=out_specs, check_vma=False)
```

```python
import numpy as np
import jax
import jax.numpy as jnp
from jax import lax
from jax.sharding import PartitionSpec as P

HEAD_DIM = 64
WINDOW = 512


EPSILON = 1e-05
PRECISE = lax.Precision.HIGHEST


def from_behind(shard, axis, by):
    devices = lax.axis_size(axis)
    pairs = [(i, i + by) for i in range(devices) if 0 <= i + by < devices]
    return lax.ppermute(shard, axis, pairs)


def tm_coords(i):
    return (i >> 4) & 3, (i >> 3) & 1, (i >> 1) & 3, i & 1


def tm_index(x, y_half, z, core):
    return ((x * 2 + y_half) * 4 + z) * 2 + core


def butterfly_plan():
    pairs, bits = [], np.zeros((64, 6), np.int32)
    flips = [("z", 1), ("x", 1), ("z", 2), ("x", 2), ("y", 1)]
    round_pairs = [[(i, i ^ 1) for i in range(64)]]
    for i in range(64):
        bits[i, 0] = i & 1
    for r, (axis, mask) in enumerate(flips):
        these = []
        for i in range(64):
            x, y_half, z, core = tm_coords(i)
            zl, xl = (z + core) % 4, (x + core) % 4
            label = {"z": zl, "x": xl, "y": y_half}[axis]
            bits[i, r + 1] = 1 if label & mask else 0
            if axis == "z":
                z = ((zl ^ mask) - core) % 4
            elif axis == "x":
                x = ((xl ^ mask) - core) % 4
            else:
                y_half ^= 1
            these.append((i, tm_index(x, y_half, z, core)))
        round_pairs.append(these)
    pairs = round_pairs
    return pairs, bits


def to_positions(a):
    rows = a.shape[0]
    r = a.reshape(rows, 4, 2, 4, 2, 16)
    first = r[:, :, :, :, 0, :]
    second = jnp.roll(jnp.roll(r[:, :, :, :, 1, :], 1, axis=1), 1, axis=3)
    g = jnp.stack([first, second], axis=1).reshape(rows, 2, 2, 2, 2, 2, 2, 16)
    g = g.transpose(0, 1, 6, 3, 5, 2, 4, 7)
    return g.reshape(rows, 1024)


def butterfly(parts, glob, shard_index):
    pairs, bits = butterfly_plan()
    my_bits = jnp.asarray(bits)[shard_index]
    rows = parts.shape[0]
    glob_shape = glob.shape
    carried = glob.reshape(rows, glob.size // rows)
    for r in range(6):
        half = parts.shape[1] // 2
        b = my_bits[r]
        keep = lax.dynamic_slice_in_dim(parts, b * half, half, 1)
        send = lax.dynamic_slice_in_dim(parts, (1 - b) * half, half, 1)
        if r == 0:
            parts = keep + lax.ppermute(send, "tm", pairs[r])
            continue
        got = lax.ppermute(jnp.concatenate([send, carried], 1), "tm", pairs[r])
        parts = keep + got[:, :half]
        carried = carried + got[:, half:]
    carried = carried + lax.ppermute(carried, "tm", pairs[0])
    return parts, carried.reshape(glob_shape)


def normalize(rows_in):
    inverse = lax.rsqrt(jnp.mean(rows_in * rows_in, axis=-1, keepdims=True) + EPSILON)
    return (rows_in * inverse, inverse)


def norm_back(gradient, unit_rows, inverse):
    return (gradient - unit_rows * jnp.mean(gradient * unit_rows, axis=-1, keepdims=True)) * inverse


def product(form, left, right):
    return jnp.einsum(form, left, right, preferred_element_type=jnp.float32)


def window_mask(row_count, lead, root):
    query_pos = lax.broadcasted_iota(jnp.int32, (row_count, row_count + lead), 0)
    key_pos = lax.broadcasted_iota(jnp.int32, (row_count, row_count + lead), 1)
    inside = (key_pos > query_pos) & (key_pos <= query_pos + lead)
    return inside & (root - lead + key_pos >= 0)


def block_pass(queries, keys_ext, values_ext, keys_glob, values_glob, grad_rows, allowed):
    scaling = HEAD_DIM ** (-0.5)
    near_scores = product("qhe,khe->hqk", queries, keys_ext) * scaling
    far_scores = product("qhe,khe->hqk", queries, keys_glob) * scaling
    near_scores = jnp.where(allowed[None, :, :], near_scores, -jnp.inf)
    row_top = jnp.maximum(
        jnp.max(near_scores, axis=-1, keepdims=True), jnp.max(far_scores, axis=-1, keepdims=True)
    )
    near_exp = jnp.exp(near_scores - row_top)
    far_exp = jnp.exp(far_scores - row_top)
    row_total = jnp.sum(near_exp, axis=-1, keepdims=True) + jnp.sum(far_exp, axis=-1, keepdims=True)
    near_prob = (near_exp / row_total).astype(jnp.bfloat16)
    far_prob = (far_exp / row_total).astype(jnp.bfloat16)
    attended = (
        product("hqk,khe->qhe", near_prob, values_ext)
        + product("hqk,khe->qhe", far_prob, values_glob)
    ).astype(jnp.bfloat16)
    near_dot = product("qhe,khe->hqk", grad_rows, values_ext)
    far_dot = product("qhe,khe->hqk", grad_rows, values_glob)
    near_p32 = near_prob.astype(jnp.float32)
    far_p32 = far_prob.astype(jnp.float32)
    row_delta = jnp.sum(near_p32 * near_dot, axis=-1, keepdims=True) + jnp.sum(
        far_p32 * far_dot, axis=-1, keepdims=True
    )
    near_grad = (near_p32 * (near_dot - row_delta) * scaling).astype(jnp.bfloat16)
    far_grad = (far_p32 * (far_dot - row_delta) * scaling).astype(jnp.bfloat16)
    query_grad = (
        product("hqk,khe->qhe", near_grad, keys_ext) + product("hqk,khe->qhe", far_grad, keys_glob)
    ).astype(jnp.bfloat16)
    key_grad = product("hqk,qhe->khe", near_grad, queries)
    value_grad = product("hqk,qhe->khe", near_prob, grad_rows)
    glob_key_grad = product("hqk,qhe->khe", far_grad, queries)
    glob_value_grad = product("hqk,qhe->khe", far_prob, grad_rows)
    return (attended, query_grad, key_grad, value_grad, glob_key_grad, glob_value_grad)


def shards(frames, cotangent, weights, summary, owners):
    rows_here = frames.shape[0]
    width = frames.shape[1]
    local_width = weights.shape[2]
    heads_here = local_width // HEAD_DIM
    glob_count = summary.shape[0]
    shard_index = lax.axis_index("tm")
    shard_total = lax.axis_size("tm")
    mp_index = lax.axis_index("mp")
    mp_total = lax.axis_size("mp")
    frames32 = frames.astype(jnp.float32)
    unit_rows, inverse = normalize(frames32)
    normed = unit_rows.astype(jnp.bfloat16)
    block_mean = jnp.mean(frames32, axis=0, keepdims=True)
    pool_unit, pool_inv = normalize(block_mean)
    pooled = pool_unit.astype(jnp.bfloat16)
    pooled_rows = jnp.concatenate([pooled, frames[1:8]], 0)
    pooled_all = lax.all_gather(pooled_rows, "tm", axis=0, tiled=False)[:, 0, :]
    owned_mask = (owners == shard_index).astype(jnp.float32)[:, None]
    anchor = summary.astype(jnp.float32) + jnp.take(pooled_all, owners, axis=0).astype(jnp.float32)
    glob_unit, glob_inv = normalize(anchor)
    glob_normed = glob_unit.astype(jnp.bfloat16)
    kv_weights = weights[:, 1:3, :].reshape(width, 2 * local_width)
    glob_kv = jnp.dot(glob_normed, kv_weights, preferred_element_type=jnp.float32).astype(jnp.bfloat16)
    project = weights[:, :3, :].reshape(width, 3 * local_width)
    qkv = jnp.dot(normed, project, preferred_element_type=jnp.float32).astype(jnp.bfloat16)
    keys_local = qkv[:, local_width : 2 * local_width]
    values_local = qkv[:, 2 * local_width :]
    queries = qkv[:, :local_width].reshape(rows_here, heads_here, HEAD_DIM)
    grad_attended = jnp.dot(cotangent, weights[:, 3, :], preferred_element_type=jnp.float32).astype(
        jnp.bfloat16
    )
    grad_attended = grad_attended.reshape(rows_here, heads_here, HEAD_DIM)
    edge_keys, edge_values = from_behind((keys_local, values_local), "tm", 1)
    keys_ext = jnp.concatenate([edge_keys, keys_local], 0).reshape(
        rows_here + WINDOW, heads_here, HEAD_DIM
    )
    values_ext = jnp.concatenate([edge_values, values_local], 0).reshape(
        rows_here + WINDOW, heads_here, HEAD_DIM
    )
    keys_glob = glob_kv[:, :local_width].reshape(glob_count, heads_here, HEAD_DIM)
    values_glob = glob_kv[:, local_width:].reshape(glob_count, heads_here, HEAD_DIM)
    allowed = window_mask(WINDOW, WINDOW, shard_index * rows_here + 0)
    results = block_pass(
        queries, keys_ext, values_ext, keys_glob, values_glob, grad_attended, allowed
    )
    attended = results[0].reshape(rows_here, local_width)
    grad_queries = results[1].reshape(rows_here, local_width)
    grad_kp = results[2].reshape(rows_here + WINDOW, local_width)
    grad_vp = results[3].reshape(rows_here + WINDOW, local_width)
    grad_kg = results[4].reshape(glob_count, local_width)
    grad_vg = results[5].reshape(glob_count, local_width)
    back_keys, back_values = from_behind(
        (grad_kp[:WINDOW].astype(jnp.bfloat16), grad_vp[:WINDOW].astype(jnp.bfloat16)), "tm", -1
    )
    grad_keys = grad_kp[WINDOW:].at[rows_here - WINDOW :].add(back_keys.astype(jnp.float32))
    grad_values = grad_vp[WINDOW:].at[rows_here - WINDOW :].add(back_values.astype(jnp.float32))
    grad_cat = jnp.concatenate(
        [grad_queries, grad_keys.astype(jnp.bfloat16), grad_values.astype(jnp.bfloat16)], 1
    )
    glob_grads = jnp.concatenate([grad_kg, grad_vg], 1)
    kv_weights32 = kv_weights.astype(jnp.float32)
    local_features = lax.dot_general(
        glob_grads, kv_weights32, (((1,), (1,)), ((), ())), precision=PRECISE
    )
    glob_cols = to_positions(glob_normed).astype(jnp.float32)
    inner_t = lax.dot_general(
        grad_cat, to_positions(normed), (((0,), (0,)), ((), ())), preferred_element_type=jnp.float32
    )
    glob_term_t = lax.dot_general(
        glob_grads, glob_cols, (((0,), (0,)), ((), ())), precision=PRECISE
    )
    inner_t = inner_t + jnp.concatenate([jnp.zeros((local_width, width), jnp.float32), glob_term_t], 0)
    last_term_t = lax.dot_general(
        attended, to_positions(cotangent), (((0,), (0,)), ((), ())), preferred_element_type=jnp.float32
    )
    weight_parts_t = jnp.concatenate([inner_t, last_term_t], 0)
    weight_cols, tm_features = butterfly(weight_parts_t, local_features, shard_index)
    grad_weights = weight_cols.reshape(4, local_width, width // shard_total).transpose(2, 0, 1)
    summary_features = tm_features + lax.ppermute(tm_features, "mp", [(0, 1), (1, 0)])
    grad_summary = norm_back(summary_features, glob_unit, glob_inv)
    pool_grads = lax.dot_general(
        owned_mask, grad_summary, (((0,), (0,)), ((), ())), precision=PRECISE
    )
    mean_grads = norm_back(pool_grads, pool_unit, pool_inv) / rows_here
    half_rows = rows_here // mp_total
    start_row = mp_index * half_rows
    other_row = (1 - mp_index) * half_rows
    feature_all = lax.dot_general(
        grad_cat, project, (((1,), (1,)), ((), ())), preferred_element_type=jnp.float32
    )
    mine = lax.dynamic_slice_in_dim(feature_all, start_row, half_rows, 0)
    theirs = lax.dynamic_slice_in_dim(feature_all, other_row, half_rows, 0).astype(jnp.bfloat16)
    received = lax.ppermute(theirs, "mp", [(0, 1), (1, 0)])
    feature_grads = mine + received.astype(jnp.float32)
    my_unit = lax.dynamic_slice_in_dim(unit_rows, start_row, half_rows, 0)
    my_inverse = lax.dynamic_slice_in_dim(inverse, start_row, half_rows, 0)
    my_cotangent = lax.dynamic_slice_in_dim(cotangent, start_row, half_rows, 0).astype(jnp.float32)
    grad_frames = (
        my_cotangent + norm_back(feature_grads, my_unit, my_inverse) + mean_grads
    ).astype(jnp.bfloat16)
    return (grad_frames, grad_weights, grad_summary)


def solution(mesh):
    in_specs = (P("tm", None), P("tm", None), P(None, None, "mp"), P(), P())
    out_specs = (P(("tm", "mp"), None), P("tm", None, "mp"), P())
    return jax.shard_map(shards, mesh=mesh, in_specs=in_specs, out_specs=out_specs, check_vma=False)
```

```python
import numpy as np
import jax
import jax.numpy as jnp
from jax import lax
from jax.sharding import PartitionSpec as P

HEAD_DIM = 64
WINDOW = 512


EPSILON = 1e-05
PRECISE = lax.Precision.HIGHEST


def from_behind(shard, axis, by):
    devices = lax.axis_size(axis)
    pairs = [(i, i + by) for i in range(devices) if 0 <= i + by < devices]
    return lax.ppermute(shard, axis, pairs)


def tm_coords(i):
    return (i >> 4) & 3, (i >> 3) & 1, (i >> 1) & 3, i & 1


def tm_index(x, y_half, z, core):
    return ((x * 2 + y_half) * 4 + z) * 2 + core


def butterfly_plan():
    pairs, bits = [], np.zeros((64, 6), np.int32)
    flips = [("z", 1), ("x", 1), ("z", 2), ("x", 2), ("y", 1)]
    round_pairs = [[(i, i ^ 1) for i in range(64)]]
    for i in range(64):
        bits[i, 0] = i & 1
    for r, (axis, mask) in enumerate(flips):
        these = []
        for i in range(64):
            x, y_half, z, core = tm_coords(i)
            zl, xl = (z + core) % 4, (x + core) % 4
            label = {"z": zl, "x": xl, "y": y_half}[axis]
            bits[i, r + 1] = 1 if label & mask else 0
            if axis == "z":
                z = ((zl ^ mask) - core) % 4
            elif axis == "x":
                x = ((xl ^ mask) - core) % 4
            else:
                y_half ^= 1
            these.append((i, tm_index(x, y_half, z, core)))
        round_pairs.append(these)
    pairs = round_pairs
    return pairs, bits


def to_positions(a):
    rows = a.shape[0]
    r = a.reshape(rows, 4, 2, 4, 2, 16)
    first = r[:, :, :, :, 0, :]
    second = jnp.roll(jnp.roll(r[:, :, :, :, 1, :], 1, axis=1), 1, axis=3)
    g = jnp.stack([first, second], axis=1).reshape(rows, 2, 2, 2, 2, 2, 2, 16)
    g = g.transpose(0, 1, 6, 3, 5, 2, 4, 7)
    return g.reshape(rows, 1024)


def butterfly(parts, glob, shard_index):
    pairs, bits = butterfly_plan()
    my_bits = jnp.asarray(bits)[shard_index]
    glob_shape = glob.shape
    carried = glob.reshape(glob.size // parts.shape[1], parts.shape[1])
    for r in range(6):
        half = parts.shape[0] // 2
        b = my_bits[r]
        keep = lax.dynamic_slice_in_dim(parts, b * half, half, 0)
        send = lax.dynamic_slice_in_dim(parts, (1 - b) * half, half, 0)
        if r == 0:
            parts = keep + lax.ppermute(send, "tm", pairs[r])
            continue
        got = lax.ppermute(jnp.concatenate([send, carried], 0), "tm", pairs[r])
        parts = keep + got[:half]
        carried = carried + got[half:]
    carried = carried + lax.ppermute(carried, "tm", pairs[0])
    carried = carried + lax.ppermute(carried, "mp", [(0, 1), (1, 0)])
    return parts, carried.reshape(glob_shape)


def normalize(rows_in):
    inverse = lax.rsqrt(jnp.mean(rows_in * rows_in, axis=-1, keepdims=True) + EPSILON)
    return (rows_in * inverse, inverse)


def norm_back(gradient, unit_rows, inverse):
    return (gradient - unit_rows * jnp.mean(gradient * unit_rows, axis=-1, keepdims=True)) * inverse


def product(form, left, right):
    return jnp.einsum(form, left, right, preferred_element_type=jnp.float32)


def window_mask(row_count, lead, root):
    query_pos = lax.broadcasted_iota(jnp.int32, (row_count, row_count + lead), 0)
    key_pos = lax.broadcasted_iota(jnp.int32, (row_count, row_count + lead), 1)
    inside = (key_pos > query_pos) & (key_pos <= query_pos + lead)
    return inside & (root - lead + key_pos >= 0)


def block_pass(queries, keys_ext, values_ext, keys_glob, values_glob, grad_rows, allowed):
    scaling = HEAD_DIM ** (-0.5)
    near_scores = product("qhe,khe->hqk", queries, keys_ext) * scaling
    far_scores = product("qhe,khe->hqk", queries, keys_glob) * scaling
    near_scores = jnp.where(allowed[None, :, :], near_scores, -jnp.inf)
    row_top = jnp.maximum(
        jnp.max(near_scores, axis=-1, keepdims=True), jnp.max(far_scores, axis=-1, keepdims=True)
    )
    near_exp = jnp.exp(near_scores - row_top)
    far_exp = jnp.exp(far_scores - row_top)
    row_total = jnp.sum(near_exp, axis=-1, keepdims=True) + jnp.sum(far_exp, axis=-1, keepdims=True)
    near_prob = (near_exp / row_total).astype(jnp.bfloat16)
    far_prob = (far_exp / row_total).astype(jnp.bfloat16)
    attended = (
        product("hqk,khe->qhe", near_prob, values_ext)
        + product("hqk,khe->qhe", far_prob, values_glob)
    ).astype(jnp.bfloat16)
    near_dot = product("qhe,khe->hqk", grad_rows, values_ext)
    far_dot = product("qhe,khe->hqk", grad_rows, values_glob)
    near_p32 = near_prob.astype(jnp.float32)
    far_p32 = far_prob.astype(jnp.float32)
    row_delta = jnp.sum(near_p32 * near_dot, axis=-1, keepdims=True) + jnp.sum(
        far_p32 * far_dot, axis=-1, keepdims=True
    )
    near_grad = (near_p32 * (near_dot - row_delta) * scaling).astype(jnp.bfloat16)
    far_grad = (far_p32 * (far_dot - row_delta) * scaling).astype(jnp.bfloat16)
    query_grad = (
        product("hqk,khe->qhe", near_grad, keys_ext) + product("hqk,khe->qhe", far_grad, keys_glob)
    ).astype(jnp.bfloat16)
    key_grad = product("hqk,qhe->khe", near_grad, queries)
    value_grad = product("hqk,qhe->khe", near_prob, grad_rows)
    glob_key_grad = product("hqk,qhe->khe", far_grad, queries)
    glob_value_grad = product("hqk,qhe->khe", far_prob, grad_rows)
    return (attended, query_grad, key_grad, value_grad, glob_key_grad, glob_value_grad)


def shards(frames, cotangent, weights, summary, owners):
    rows_here = frames.shape[0]
    width = frames.shape[1]
    local_width = weights.shape[2]
    heads_here = local_width // HEAD_DIM
    glob_count = summary.shape[0]
    shard_index = lax.axis_index("tm")
    shard_total = lax.axis_size("tm")
    mp_index = lax.axis_index("mp")
    mp_total = lax.axis_size("mp")
    frames32 = frames.astype(jnp.float32)
    unit_rows, inverse = normalize(frames32)
    normed = unit_rows.astype(jnp.bfloat16)
    block_mean = jnp.mean(frames32, axis=0, keepdims=True)
    pool_unit, pool_inv = normalize(block_mean)
    pooled = pool_unit.astype(jnp.bfloat16)
    pooled_rows = jnp.concatenate([pooled, frames[1:8]], 0)
    pooled_all = lax.all_gather(pooled_rows, "tm", axis=0, tiled=False)[:, 0, :]
    owned_mask = (owners == shard_index).astype(jnp.float32)[:, None]
    anchor = summary.astype(jnp.float32) + jnp.take(pooled_all, owners, axis=0).astype(jnp.float32)
    glob_unit, glob_inv = normalize(anchor)
    glob_normed = glob_unit.astype(jnp.bfloat16)
    kv_weights = weights[:, 1:3, :].reshape(width, 2 * local_width)
    glob_kv = jnp.dot(glob_normed, kv_weights, preferred_element_type=jnp.float32).astype(jnp.bfloat16)
    project = weights[:, :3, :].reshape(width, 3 * local_width)
    qkv = jnp.dot(normed, project, preferred_element_type=jnp.float32).astype(jnp.bfloat16)
    keys_local = qkv[:, local_width : 2 * local_width]
    values_local = qkv[:, 2 * local_width :]
    queries = qkv[:, :local_width].reshape(rows_here, heads_here, HEAD_DIM)
    grad_attended = jnp.dot(cotangent, weights[:, 3, :], preferred_element_type=jnp.float32).astype(
        jnp.bfloat16
    )
    grad_attended = grad_attended.reshape(rows_here, heads_here, HEAD_DIM)
    edge = from_behind(qkv[:, local_width:], "tm", 1)
    edge_keys, edge_values = edge[:, :local_width], edge[:, local_width:]
    keys_ext = jnp.concatenate([edge_keys, keys_local], 0).reshape(
        rows_here + WINDOW, heads_here, HEAD_DIM
    )
    values_ext = jnp.concatenate([edge_values, values_local], 0).reshape(
        rows_here + WINDOW, heads_here, HEAD_DIM
    )
    keys_glob = glob_kv[:, :local_width].reshape(glob_count, heads_here, HEAD_DIM)
    values_glob = glob_kv[:, local_width:].reshape(glob_count, heads_here, HEAD_DIM)
    allowed = window_mask(WINDOW, WINDOW, shard_index * rows_here + 0)
    results = block_pass(
        queries, keys_ext, values_ext, keys_glob, values_glob, grad_attended, allowed
    )
    attended = results[0].reshape(rows_here, local_width)
    grad_queries = results[1].reshape(rows_here, local_width)
    grad_kp = results[2].reshape(rows_here + WINDOW, local_width)
    grad_vp = results[3].reshape(rows_here + WINDOW, local_width)
    grad_kg = results[4].reshape(glob_count, local_width)
    grad_vg = results[5].reshape(glob_count, local_width)
    back = from_behind(
        jnp.concatenate([grad_kp[:WINDOW], grad_vp[:WINDOW]], 1).astype(jnp.bfloat16), "tm", -1
    )
    back_keys, back_values = back[:, :local_width], back[:, local_width:]
    grad_keys = grad_kp[WINDOW:].at[rows_here - WINDOW :].add(back_keys.astype(jnp.float32))
    grad_values = grad_vp[WINDOW:].at[rows_here - WINDOW :].add(back_values.astype(jnp.float32))
    grad_cat = jnp.concatenate(
        [grad_queries, grad_keys.astype(jnp.bfloat16), grad_values.astype(jnp.bfloat16)], 1
    )
    glob_grads = jnp.concatenate([grad_kg, grad_vg], 1)
    kv_weights32 = kv_weights.astype(jnp.float32)
    local_features = lax.dot_general(
        glob_grads, kv_weights32, (((1,), (1,)), ((), ())), precision=PRECISE
    )
    glob_cols = to_positions(glob_normed).astype(jnp.float32)
    inner = lax.dot_general(
        to_positions(normed), grad_cat, (((0,), (0,)), ((), ())), preferred_element_type=jnp.float32
    )
    glob_term = lax.dot_general(glob_cols, glob_grads, (((0,), (0,)), ((), ())), precision=PRECISE)
    inner = inner + jnp.concatenate([jnp.zeros((width, local_width), jnp.float32), glob_term], 1)
    last_term = lax.dot_general(
        to_positions(cotangent), attended, (((0,), (0,)), ((), ())), preferred_element_type=jnp.float32
    )
    weight_parts = jnp.concatenate(
        [inner.reshape(width, 3, local_width), last_term.reshape(width, 1, local_width)], 1
    )
    weight_rows, summary_features = butterfly(
        weight_parts.reshape(width, 4 * local_width), local_features, shard_index
    )
    grad_weights = weight_rows.reshape(width // shard_total, 4, local_width)
    grad_summary = norm_back(summary_features, glob_unit, glob_inv)
    pool_grads = lax.dot_general(
        owned_mask, grad_summary, (((0,), (0,)), ((), ())), precision=PRECISE
    )
    mean_grads = norm_back(pool_grads, pool_unit, pool_inv) / rows_here
    half_rows = rows_here // mp_total
    start_row = mp_index * half_rows
    other_row = (1 - mp_index) * half_rows
    feature_all = lax.dot_general(
        grad_cat, project, (((1,), (1,)), ((), ())), preferred_element_type=jnp.float32
    )
    mine = lax.dynamic_slice_in_dim(feature_all, start_row, half_rows, 0)
    theirs = lax.dynamic_slice_in_dim(feature_all, other_row, half_rows, 0).astype(jnp.bfloat16)
    received = lax.ppermute(theirs, "mp", [(0, 1), (1, 0)])
    feature_grads = mine + received.astype(jnp.float32)
    my_unit = lax.dynamic_slice_in_dim(unit_rows, start_row, half_rows, 0)
    my_inverse = lax.dynamic_slice_in_dim(inverse, start_row, half_rows, 0)
    my_cotangent = lax.dynamic_slice_in_dim(cotangent, start_row, half_rows, 0).astype(jnp.float32)
    grad_frames = (
        my_cotangent + norm_back(feature_grads, my_unit, my_inverse) + mean_grads
    ).astype(jnp.bfloat16)
    return (grad_frames, grad_weights, grad_summary)


def solution(mesh):
    in_specs = (P("tm", None), P("tm", None), P(None, None, "mp"), P(), P())
    out_specs = (P(("tm", "mp"), None), P("tm", None, "mp"), P())
    return jax.shard_map(shards, mesh=mesh, in_specs=in_specs, out_specs=out_specs, check_vma=False)
```

```python
import numpy as np
import jax
import jax.numpy as jnp
from jax import lax
from jax.sharding import PartitionSpec as P

HEAD_DIM = 64
WINDOW = 512


EPSILON = 1e-05
PRECISE = lax.Precision.HIGHEST


def from_behind(shard, axis, by):
    devices = lax.axis_size(axis)
    pairs = [(i, i + by) for i in range(devices) if 0 <= i + by < devices]
    return lax.ppermute(shard, axis, pairs)


def tm_coords(i):
    return (i >> 4) & 3, (i >> 3) & 1, (i >> 1) & 3, i & 1


def tm_index(x, y_half, z, core):
    return ((x * 2 + y_half) * 4 + z) * 2 + core


def butterfly_plan():
    pairs, bits = [], np.zeros((64, 6), np.int32)
    flips = [("z", 1), ("x", 1), ("z", 2), ("x", 2), ("y", 1)]
    round_pairs = [[(i, i ^ 1) for i in range(64)]]
    for i in range(64):
        bits[i, 0] = i & 1
    for r, (axis, mask) in enumerate(flips):
        these = []
        for i in range(64):
            x, y_half, z, core = tm_coords(i)
            zl, xl = (z + core) % 4, (x + core) % 4
            label = {"z": zl, "x": xl, "y": y_half}[axis]
            bits[i, r + 1] = 1 if label & mask else 0
            if axis == "z":
                z = ((zl ^ mask) - core) % 4
            elif axis == "x":
                x = ((xl ^ mask) - core) % 4
            else:
                y_half ^= 1
            these.append((i, tm_index(x, y_half, z, core)))
        round_pairs.append(these)
    pairs = round_pairs
    return pairs, bits


def to_positions(a):
    rows = a.shape[0]
    r = a.reshape(rows, 4, 2, 4, 2, 16)
    first = r[:, :, :, :, 0, :]
    second = jnp.roll(jnp.roll(r[:, :, :, :, 1, :], 1, axis=1), 1, axis=3)
    g = jnp.stack([first, second], axis=1).reshape(rows, 2, 2, 2, 2, 2, 2, 16)
    g = g.transpose(0, 1, 6, 3, 5, 2, 4, 7)
    return g.reshape(rows, 1024)


def labels(i):
    x, y_half, z, core = tm_coords(i)
    return core, (z + core) % 4, (x + core) % 4, y_half


def from_labels(core, zl, xl, y_half):
    return tm_index((xl - core) % 4, y_half, (zl - core) % 4, core)


def radix_plan():
    steps = []
    keep = np.array([i & 1 for i in range(64)], np.int32)
    steps.append((2, keep, [([(i, i ^ 1) for i in range(64)], keep ^ 1)]))
    for mask, shift in ((1, 0), (2, 1)):
        keep = np.zeros(64, np.int32)
        for i in range(64):
            core, zl, xl, y_half = labels(i)
            keep[i] = ((zl & mask) >> shift) * 2 + ((xl & mask) >> shift)
        partners = []
        for d in (1, 2, 3):
            pairs = []
            for i in range(64):
                core, zl, xl, y_half = labels(i)
                zl ^= mask if d & 2 else 0
                xl ^= mask if d & 1 else 0
                pairs.append((i, from_labels(core, zl, xl, y_half)))
            partners.append((pairs, keep ^ d))
        steps.append((4, keep, partners))
    keep = np.array([labels(i)[3] for i in range(64)], np.int32)
    steps.append((2, keep, [([(i, i ^ 8) for i in range(64)], keep ^ 1)]))
    return steps


def glob_rounds():
    rounds = []
    for flip in ((1, 0), (0, 1), (2, 0), (0, 2)):
        pairs = []
        for i in range(64):
            core, zl, xl, y_half = labels(i)
            pairs.append((i, from_labels(core, zl ^ flip[0], xl ^ flip[1], y_half)))
        rounds.append(pairs)
    rounds.append([(i, i ^ 8) for i in range(64)])
    rounds.append([(i, i ^ 1) for i in range(64)])
    return rounds


def butterfly(parts, glob, shard_index):
    for ways, keep_table, partners in radix_plan():
        size = parts.shape[0] // ways
        kept = jnp.asarray(keep_table)[shard_index]
        total = lax.dynamic_slice_in_dim(parts, kept * size, size, 0)
        for pairs, send_table in partners:
            sent = jnp.asarray(send_table)[shard_index]
            total = total + lax.ppermute(
                lax.dynamic_slice_in_dim(parts, sent * size, size, 0), "tm", pairs
            )
        parts = total
    for pairs in glob_rounds():
        glob = glob + lax.ppermute(glob, "tm", pairs)
    glob = glob + lax.ppermute(glob, "mp", [(0, 1), (1, 0)])
    return parts, glob


def normalize(rows_in):
    inverse = lax.rsqrt(jnp.mean(rows_in * rows_in, axis=-1, keepdims=True) + EPSILON)
    return (rows_in * inverse, inverse)


def norm_back(gradient, unit_rows, inverse):
    return (gradient - unit_rows * jnp.mean(gradient * unit_rows, axis=-1, keepdims=True)) * inverse


def product(form, left, right):
    return jnp.einsum(form, left, right, preferred_element_type=jnp.float32)


def window_mask(row_count, lead, root):
    query_pos = lax.broadcasted_iota(jnp.int32, (row_count, row_count + lead), 0)
    key_pos = lax.broadcasted_iota(jnp.int32, (row_count, row_count + lead), 1)
    inside = (key_pos > query_pos) & (key_pos <= query_pos + lead)
    return inside & (root - lead + key_pos >= 0)


def block_pass(queries, keys_ext, values_ext, keys_glob, values_glob, grad_rows, allowed):
    scaling = HEAD_DIM ** (-0.5)
    near_scores = product("qhe,khe->hqk", queries, keys_ext) * scaling
    far_scores = product("qhe,khe->hqk", queries, keys_glob) * scaling
    near_scores = jnp.where(allowed[None, :, :], near_scores, -jnp.inf)
    row_top = jnp.maximum(
        jnp.max(near_scores, axis=-1, keepdims=True), jnp.max(far_scores, axis=-1, keepdims=True)
    )
    near_exp = jnp.exp(near_scores - row_top)
    far_exp = jnp.exp(far_scores - row_top)
    row_total = jnp.sum(near_exp, axis=-1, keepdims=True) + jnp.sum(far_exp, axis=-1, keepdims=True)
    near_prob = (near_exp / row_total).astype(jnp.bfloat16)
    far_prob = (far_exp / row_total).astype(jnp.bfloat16)
    attended = (
        product("hqk,khe->qhe", near_prob, values_ext)
        + product("hqk,khe->qhe", far_prob, values_glob)
    ).astype(jnp.bfloat16)
    near_dot = product("qhe,khe->hqk", grad_rows, values_ext)
    far_dot = product("qhe,khe->hqk", grad_rows, values_glob)
    near_p32 = near_prob.astype(jnp.float32)
    far_p32 = far_prob.astype(jnp.float32)
    row_delta = jnp.sum(near_p32 * near_dot, axis=-1, keepdims=True) + jnp.sum(
        far_p32 * far_dot, axis=-1, keepdims=True
    )
    near_grad = (near_p32 * (near_dot - row_delta) * scaling).astype(jnp.bfloat16)
    far_grad = (far_p32 * (far_dot - row_delta) * scaling).astype(jnp.bfloat16)
    query_grad = (
        product("hqk,khe->qhe", near_grad, keys_ext) + product("hqk,khe->qhe", far_grad, keys_glob)
    ).astype(jnp.bfloat16)
    key_grad = product("hqk,qhe->khe", near_grad, queries)
    value_grad = product("hqk,qhe->khe", near_prob, grad_rows)
    glob_key_grad = product("hqk,qhe->khe", far_grad, queries)
    glob_value_grad = product("hqk,qhe->khe", far_prob, grad_rows)
    return (attended, query_grad, key_grad, value_grad, glob_key_grad, glob_value_grad)


def shards(frames, cotangent, weights, summary, owners):
    rows_here = frames.shape[0]
    width = frames.shape[1]
    local_width = weights.shape[2]
    heads_here = local_width // HEAD_DIM
    glob_count = summary.shape[0]
    shard_index = lax.axis_index("tm")
    shard_total = lax.axis_size("tm")
    mp_index = lax.axis_index("mp")
    mp_total = lax.axis_size("mp")
    frames32 = frames.astype(jnp.float32)
    unit_rows, inverse = normalize(frames32)
    normed = unit_rows.astype(jnp.bfloat16)
    block_mean = jnp.mean(frames32, axis=0, keepdims=True)
    pool_unit, pool_inv = normalize(block_mean)
    pooled = pool_unit.astype(jnp.bfloat16)
    pooled_rows = jnp.concatenate([pooled, frames[1:8]], 0)
    pooled_all = lax.all_gather(pooled_rows, "tm", axis=0, tiled=False)[:, 0, :]
    owned_mask = (owners == shard_index).astype(jnp.float32)[:, None]
    anchor = summary.astype(jnp.float32) + jnp.take(pooled_all, owners, axis=0).astype(jnp.float32)
    glob_unit, glob_inv = normalize(anchor)
    glob_normed = glob_unit.astype(jnp.bfloat16)
    kv_weights = weights[:, 1:3, :].reshape(width, 2 * local_width)
    glob_kv = jnp.dot(glob_normed, kv_weights, preferred_element_type=jnp.float32).astype(jnp.bfloat16)
    project = weights[:, :3, :].reshape(width, 3 * local_width)
    qkv = jnp.dot(normed, project, preferred_element_type=jnp.float32).astype(jnp.bfloat16)
    keys_local = qkv[:, local_width : 2 * local_width]
    values_local = qkv[:, 2 * local_width :]
    queries = qkv[:, :local_width].reshape(rows_here, heads_here, HEAD_DIM)
    grad_attended = jnp.dot(cotangent, weights[:, 3, :], preferred_element_type=jnp.float32).astype(
        jnp.bfloat16
    )
    grad_attended = grad_attended.reshape(rows_here, heads_here, HEAD_DIM)
    edge = from_behind(qkv[:, local_width:], "tm", 1)
    edge_keys, edge_values = edge[:, :local_width], edge[:, local_width:]
    keys_ext = jnp.concatenate([edge_keys, keys_local], 0).reshape(
        rows_here + WINDOW, heads_here, HEAD_DIM
    )
    values_ext = jnp.concatenate([edge_values, values_local], 0).reshape(
        rows_here + WINDOW, heads_here, HEAD_DIM
    )
    keys_glob = glob_kv[:, :local_width].reshape(glob_count, heads_here, HEAD_DIM)
    values_glob = glob_kv[:, local_width:].reshape(glob_count, heads_here, HEAD_DIM)
    allowed = window_mask(WINDOW, WINDOW, shard_index * rows_here + 0)
    results = block_pass(
        queries, keys_ext, values_ext, keys_glob, values_glob, grad_attended, allowed
    )
    attended = results[0].reshape(rows_here, local_width)
    grad_queries = results[1].reshape(rows_here, local_width)
    grad_kp = results[2].reshape(rows_here + WINDOW, local_width)
    grad_vp = results[3].reshape(rows_here + WINDOW, local_width)
    grad_kg = results[4].reshape(glob_count, local_width)
    grad_vg = results[5].reshape(glob_count, local_width)
    back = from_behind(
        jnp.concatenate([grad_kp[:WINDOW], grad_vp[:WINDOW]], 1).astype(jnp.bfloat16), "tm", -1
    )
    back_keys, back_values = back[:, :local_width], back[:, local_width:]
    grad_keys = grad_kp[WINDOW:].at[rows_here - WINDOW :].add(back_keys.astype(jnp.float32))
    grad_values = grad_vp[WINDOW:].at[rows_here - WINDOW :].add(back_values.astype(jnp.float32))
    grad_cat = jnp.concatenate(
        [grad_queries, grad_keys.astype(jnp.bfloat16), grad_values.astype(jnp.bfloat16)], 1
    )
    glob_grads = jnp.concatenate([grad_kg, grad_vg], 1)
    kv_weights32 = kv_weights.astype(jnp.float32)
    local_features = lax.dot_general(
        glob_grads, kv_weights32, (((1,), (1,)), ((), ())), precision=PRECISE
    )
    glob_cols = to_positions(glob_normed).astype(jnp.float32)
    inner = lax.dot_general(
        to_positions(normed), grad_cat, (((0,), (0,)), ((), ())), preferred_element_type=jnp.float32
    )
    glob_term = lax.dot_general(glob_cols, glob_grads, (((0,), (0,)), ((), ())), precision=PRECISE)
    inner = inner + jnp.concatenate([jnp.zeros((width, local_width), jnp.float32), glob_term], 1)
    last_term = lax.dot_general(
        to_positions(cotangent), attended, (((0,), (0,)), ((), ())), preferred_element_type=jnp.float32
    )
    weight_parts = jnp.concatenate(
        [inner.reshape(width, 3, local_width), last_term.reshape(width, 1, local_width)], 1
    )
    weight_rows, summary_features = butterfly(
        weight_parts.reshape(width, 4 * local_width), local_features, shard_index
    )
    grad_weights = weight_rows.reshape(width // shard_total, 4, local_width)
    grad_summary = norm_back(summary_features, glob_unit, glob_inv)
    pool_grads = lax.dot_general(
        owned_mask, grad_summary, (((0,), (0,)), ((), ())), precision=PRECISE
    )
    mean_grads = norm_back(pool_grads, pool_unit, pool_inv) / rows_here
    half_rows = rows_here // mp_total
    start_row = mp_index * half_rows
    other_row = (1 - mp_index) * half_rows
    feature_all = lax.dot_general(
        grad_cat, project, (((1,), (1,)), ((), ())), preferred_element_type=jnp.float32
    )
    mine = lax.dynamic_slice_in_dim(feature_all, start_row, half_rows, 0)
    theirs = lax.dynamic_slice_in_dim(feature_all, other_row, half_rows, 0).astype(jnp.bfloat16)
    received = lax.ppermute(theirs, "mp", [(0, 1), (1, 0)])
    feature_grads = mine + received.astype(jnp.float32)
    my_unit = lax.dynamic_slice_in_dim(unit_rows, start_row, half_rows, 0)
    my_inverse = lax.dynamic_slice_in_dim(inverse, start_row, half_rows, 0)
    my_cotangent = lax.dynamic_slice_in_dim(cotangent, start_row, half_rows, 0).astype(jnp.float32)
    grad_frames = (
        my_cotangent + norm_back(feature_grads, my_unit, my_inverse) + mean_grads
    ).astype(jnp.bfloat16)
    return (grad_frames, grad_weights, grad_summary)


def solution(mesh):
    in_specs = (P("tm", None), P("tm", None), P(None, None, "mp"), P(), P())
    out_specs = (P(("tm", "mp"), None), P("tm", None, "mp"), P())
    return jax.shard_map(shards, mesh=mesh, in_specs=in_specs, out_specs=out_specs, check_vma=False)
```

```python
import numpy as np
import jax
import jax.numpy as jnp
from jax import lax
from jax.sharding import PartitionSpec as P

HEAD_DIM = 64
WINDOW = 512


EPSILON = 1e-05
PRECISE = lax.Precision.HIGHEST


def from_behind(shard, axis, by):
    devices = lax.axis_size(axis)
    pairs = [(i, i + by) for i in range(devices) if 0 <= i + by < devices]
    return lax.ppermute(shard, axis, pairs)


def tm_coords(i):
    return (i >> 4) & 3, (i >> 3) & 1, (i >> 1) & 3, i & 1


def tm_index(x, y_half, z, core):
    return ((x * 2 + y_half) * 4 + z) * 2 + core


def butterfly_plan():
    pairs, bits = [], np.zeros((64, 6), np.int32)
    flips = [("z", 1), ("x", 1), ("z", 2), ("x", 2), ("y", 1)]
    round_pairs = [[(i, i ^ 1) for i in range(64)]]
    for i in range(64):
        bits[i, 0] = i & 1
    for r, (axis, mask) in enumerate(flips):
        these = []
        for i in range(64):
            x, y_half, z, core = tm_coords(i)
            zl, xl = (z + core) % 4, (x + core) % 4
            label = {"z": zl, "x": xl, "y": y_half}[axis]
            bits[i, r + 1] = 1 if label & mask else 0
            if axis == "z":
                z = ((zl ^ mask) - core) % 4
            elif axis == "x":
                x = ((xl ^ mask) - core) % 4
            else:
                y_half ^= 1
            these.append((i, tm_index(x, y_half, z, core)))
        round_pairs.append(these)
    pairs = round_pairs
    return pairs, bits


def to_positions(a):
    rows = a.shape[0]
    r = a.reshape(rows, 4, 2, 4, 2, 16)
    first = r[:, :, :, :, 0, :]
    second = jnp.roll(jnp.roll(r[:, :, :, :, 1, :], 1, axis=1), 1, axis=3)
    g = jnp.stack([first, second], axis=1).reshape(rows, 2, 2, 2, 2, 2, 2, 16)
    g = g.transpose(0, 1, 6, 3, 5, 2, 4, 7)
    return g.reshape(rows, 1024)


def labels(i):
    x, y_half, z, core = tm_coords(i)
    return core, (z + core) % 4, (x + core) % 4, y_half


def from_labels(core, zl, xl, y_half):
    return tm_index((xl - core) % 4, y_half, (zl - core) % 4, core)


def radix_plan():
    steps = []
    keep = np.array([i & 1 for i in range(64)], np.int32)
    steps.append((2, keep, [([(i, i ^ 1) for i in range(64)], keep ^ 1)]))
    for mask, shift in ((1, 0), (2, 1)):
        keep = np.zeros(64, np.int32)
        for i in range(64):
            core, zl, xl, y_half = labels(i)
            keep[i] = ((zl & mask) >> shift) * 2 + ((xl & mask) >> shift)
        partners = []
        for d in (1, 2, 3):
            pairs = []
            for i in range(64):
                core, zl, xl, y_half = labels(i)
                zl ^= mask if d & 2 else 0
                xl ^= mask if d & 1 else 0
                pairs.append((i, from_labels(core, zl, xl, y_half)))
            partners.append((pairs, keep ^ d))
        steps.append((4, keep, partners))
    keep = np.array([labels(i)[3] for i in range(64)], np.int32)
    steps.append((2, keep, [([(i, i ^ 8) for i in range(64)], keep ^ 1)]))
    return steps


def glob_steps():
    steps = []
    for mask, shift in ((1, 0), (2, 1)):
        slots = np.zeros(64, np.int32)
        for i in range(64):
            core, zl, xl, y_half = labels(i)
            slots[i] = ((zl & mask) >> shift) * 2 + ((xl & mask) >> shift)
        partners = []
        for d in (1, 2, 3):
            pairs = []
            for i in range(64):
                core, zl, xl, y_half = labels(i)
                zl ^= mask if d & 2 else 0
                xl ^= mask if d & 1 else 0
                pairs.append((i, from_labels(core, zl, xl, y_half)))
            partners.append(pairs)
        steps.append((slots, partners))
    slots = np.array([((i >> 3) & 1) * 2 + (i & 1) for i in range(64)], np.int32)
    steps.append((slots, [[(i, i ^ flip) for i in range(64)] for flip in (1, 8, 9)]))
    return steps


def butterfly(parts, glob, shard_index):
    for ways, keep_table, partners in radix_plan():
        size = parts.shape[0] // ways
        kept = jnp.asarray(keep_table)[shard_index]
        total = lax.dynamic_slice_in_dim(parts, kept * size, size, 0)
        for pairs, send_table in partners:
            sent = jnp.asarray(send_table)[shard_index]
            total = total + lax.ppermute(
                lax.dynamic_slice_in_dim(parts, sent * size, size, 0), "tm", pairs
            )
        parts = total
    for slot_table, partners in glob_steps():
        slot = jnp.asarray(slot_table)[shard_index]
        held = jnp.stack([glob] + [lax.ppermute(glob, "tm", pairs) for pairs in partners])
        ordered = [lax.dynamic_index_in_dim(held, slot ^ s, 0, keepdims=False) for s in range(4)]
        glob = (ordered[0] + ordered[1]) + (ordered[2] + ordered[3])
    glob = glob + lax.ppermute(glob, "mp", [(0, 1), (1, 0)])
    return parts, glob


def normalize(rows_in):
    inverse = lax.rsqrt(jnp.mean(rows_in * rows_in, axis=-1, keepdims=True) + EPSILON)
    return (rows_in * inverse, inverse)


def norm_back(gradient, unit_rows, inverse):
    return (gradient - unit_rows * jnp.mean(gradient * unit_rows, axis=-1, keepdims=True)) * inverse


def product(form, left, right):
    return jnp.einsum(form, left, right, preferred_element_type=jnp.float32)


def window_mask(row_count, lead, root):
    query_pos = lax.broadcasted_iota(jnp.int32, (row_count, row_count + lead), 0)
    key_pos = lax.broadcasted_iota(jnp.int32, (row_count, row_count + lead), 1)
    inside = (key_pos > query_pos) & (key_pos <= query_pos + lead)
    return inside & (root - lead + key_pos >= 0)


def block_pass(queries, keys_ext, values_ext, keys_glob, values_glob, grad_rows, allowed):
    scaling = HEAD_DIM ** (-0.5)
    near_scores = product("qhe,khe->hqk", queries, keys_ext) * scaling
    far_scores = product("qhe,khe->hqk", queries, keys_glob) * scaling
    near_scores = jnp.where(allowed[None, :, :], near_scores, -jnp.inf)
    row_top = jnp.maximum(
        jnp.max(near_scores, axis=-1, keepdims=True), jnp.max(far_scores, axis=-1, keepdims=True)
    )
    near_exp = jnp.exp(near_scores - row_top)
    far_exp = jnp.exp(far_scores - row_top)
    row_total = jnp.sum(near_exp, axis=-1, keepdims=True) + jnp.sum(far_exp, axis=-1, keepdims=True)
    near_prob = (near_exp / row_total).astype(jnp.bfloat16)
    far_prob = (far_exp / row_total).astype(jnp.bfloat16)
    attended = (
        product("hqk,khe->qhe", near_prob, values_ext)
        + product("hqk,khe->qhe", far_prob, values_glob)
    ).astype(jnp.bfloat16)
    near_dot = product("qhe,khe->hqk", grad_rows, values_ext)
    far_dot = product("qhe,khe->hqk", grad_rows, values_glob)
    near_p32 = near_prob.astype(jnp.float32)
    far_p32 = far_prob.astype(jnp.float32)
    row_delta = jnp.sum(near_p32 * near_dot, axis=-1, keepdims=True) + jnp.sum(
        far_p32 * far_dot, axis=-1, keepdims=True
    )
    near_grad = (near_p32 * (near_dot - row_delta) * scaling).astype(jnp.bfloat16)
    far_grad = (far_p32 * (far_dot - row_delta) * scaling).astype(jnp.bfloat16)
    query_grad = (
        product("hqk,khe->qhe", near_grad, keys_ext) + product("hqk,khe->qhe", far_grad, keys_glob)
    ).astype(jnp.bfloat16)
    key_grad = product("hqk,qhe->khe", near_grad, queries)
    value_grad = product("hqk,qhe->khe", near_prob, grad_rows)
    glob_key_grad = product("hqk,qhe->khe", far_grad, queries)
    glob_value_grad = product("hqk,qhe->khe", far_prob, grad_rows)
    return (attended, query_grad, key_grad, value_grad, glob_key_grad, glob_value_grad)


def shards(frames, cotangent, weights, summary, owners):
    rows_here = frames.shape[0]
    width = frames.shape[1]
    local_width = weights.shape[2]
    heads_here = local_width // HEAD_DIM
    glob_count = summary.shape[0]
    shard_index = lax.axis_index("tm")
    shard_total = lax.axis_size("tm")
    mp_index = lax.axis_index("mp")
    mp_total = lax.axis_size("mp")
    frames32 = frames.astype(jnp.float32)
    unit_rows, inverse = normalize(frames32)
    normed = unit_rows.astype(jnp.bfloat16)
    block_mean = jnp.mean(frames32, axis=0, keepdims=True)
    pool_unit, pool_inv = normalize(block_mean)
    pooled = pool_unit.astype(jnp.bfloat16)
    pooled_rows = jnp.concatenate([pooled, frames[1:8]], 0)
    pooled_all = lax.all_gather(pooled_rows, "tm", axis=0, tiled=False)[:, 0, :]
    owned_mask = (owners == shard_index).astype(jnp.float32)[:, None]
    anchor = summary.astype(jnp.float32) + jnp.take(pooled_all, owners, axis=0).astype(jnp.float32)
    glob_unit, glob_inv = normalize(anchor)
    glob_normed = glob_unit.astype(jnp.bfloat16)
    kv_weights = weights[:, 1:3, :].reshape(width, 2 * local_width)
    glob_kv = jnp.dot(glob_normed, kv_weights, preferred_element_type=jnp.float32).astype(jnp.bfloat16)
    project = weights[:, :3, :].reshape(width, 3 * local_width)
    qkv = jnp.dot(normed, project, preferred_element_type=jnp.float32).astype(jnp.bfloat16)
    keys_local = qkv[:, local_width : 2 * local_width]
    values_local = qkv[:, 2 * local_width :]
    queries = qkv[:, :local_width].reshape(rows_here, heads_here, HEAD_DIM)
    grad_attended = jnp.dot(cotangent, weights[:, 3, :], preferred_element_type=jnp.float32).astype(
        jnp.bfloat16
    )
    grad_attended = grad_attended.reshape(rows_here, heads_here, HEAD_DIM)
    edge = from_behind(qkv[:, local_width:], "tm", 1)
    edge_keys, edge_values = edge[:, :local_width], edge[:, local_width:]
    keys_ext = jnp.concatenate([edge_keys, keys_local], 0).reshape(
        rows_here + WINDOW, heads_here, HEAD_DIM
    )
    values_ext = jnp.concatenate([edge_values, values_local], 0).reshape(
        rows_here + WINDOW, heads_here, HEAD_DIM
    )
    keys_glob = glob_kv[:, :local_width].reshape(glob_count, heads_here, HEAD_DIM)
    values_glob = glob_kv[:, local_width:].reshape(glob_count, heads_here, HEAD_DIM)
    allowed = window_mask(WINDOW, WINDOW, shard_index * rows_here + 0)
    results = block_pass(
        queries, keys_ext, values_ext, keys_glob, values_glob, grad_attended, allowed
    )
    attended = results[0].reshape(rows_here, local_width)
    grad_queries = results[1].reshape(rows_here, local_width)
    grad_kp = results[2].reshape(rows_here + WINDOW, local_width)
    grad_vp = results[3].reshape(rows_here + WINDOW, local_width)
    grad_kg = results[4].reshape(glob_count, local_width)
    grad_vg = results[5].reshape(glob_count, local_width)
    back = from_behind(
        jnp.concatenate([grad_kp[:WINDOW], grad_vp[:WINDOW]], 1).astype(jnp.bfloat16), "tm", -1
    )
    back_keys, back_values = back[:, :local_width], back[:, local_width:]
    grad_keys = grad_kp[WINDOW:].at[rows_here - WINDOW :].add(back_keys.astype(jnp.float32))
    grad_values = grad_vp[WINDOW:].at[rows_here - WINDOW :].add(back_values.astype(jnp.float32))
    grad_cat = jnp.concatenate(
        [grad_queries, grad_keys.astype(jnp.bfloat16), grad_values.astype(jnp.bfloat16)], 1
    )
    glob_grads = jnp.concatenate([grad_kg, grad_vg], 1)
    kv_weights32 = kv_weights.astype(jnp.float32)
    local_features = lax.dot_general(
        glob_grads, kv_weights32, (((1,), (1,)), ((), ())), precision=PRECISE
    )
    glob_cols = to_positions(glob_normed).astype(jnp.float32)
    inner = lax.dot_general(
        to_positions(normed), grad_cat, (((0,), (0,)), ((), ())), preferred_element_type=jnp.float32
    )
    glob_term = lax.dot_general(glob_cols, glob_grads, (((0,), (0,)), ((), ())), precision=PRECISE)
    inner = inner + jnp.concatenate([jnp.zeros((width, local_width), jnp.float32), glob_term], 1)
    last_term = lax.dot_general(
        to_positions(cotangent), attended, (((0,), (0,)), ((), ())), preferred_element_type=jnp.float32
    )
    weight_parts = jnp.concatenate(
        [inner.reshape(width, 3, local_width), last_term.reshape(width, 1, local_width)], 1
    )
    weight_rows, summary_features = butterfly(
        weight_parts.reshape(width, 4 * local_width), local_features, shard_index
    )
    grad_weights = weight_rows.reshape(width // shard_total, 4, local_width)
    grad_summary = norm_back(summary_features, glob_unit, glob_inv)
    pool_grads = lax.dot_general(
        owned_mask, grad_summary, (((0,), (0,)), ((), ())), precision=PRECISE
    )
    mean_grads = norm_back(pool_grads, pool_unit, pool_inv) / rows_here
    half_rows = rows_here // mp_total
    start_row = mp_index * half_rows
    other_row = (1 - mp_index) * half_rows
    feature_all = lax.dot_general(
        grad_cat, project, (((1,), (1,)), ((), ())), preferred_element_type=jnp.float32
    )
    mine = lax.dynamic_slice_in_dim(feature_all, start_row, half_rows, 0)
    theirs = lax.dynamic_slice_in_dim(feature_all, other_row, half_rows, 0).astype(jnp.bfloat16)
    received = lax.ppermute(theirs, "mp", [(0, 1), (1, 0)])
    feature_grads = mine + received.astype(jnp.float32)
    my_unit = lax.dynamic_slice_in_dim(unit_rows, start_row, half_rows, 0)
    my_inverse = lax.dynamic_slice_in_dim(inverse, start_row, half_rows, 0)
    my_cotangent = lax.dynamic_slice_in_dim(cotangent, start_row, half_rows, 0).astype(jnp.float32)
    grad_frames = (
        my_cotangent + norm_back(feature_grads, my_unit, my_inverse) + mean_grads
    ).astype(jnp.bfloat16)
    return (grad_frames, grad_weights, grad_summary)


def solution(mesh):
    in_specs = (P("tm", None), P("tm", None), P(None, None, "mp"), P(), P())
    out_specs = (P(("tm", "mp"), None), P("tm", None, "mp"), P())
    return jax.shard_map(shards, mesh=mesh, in_specs=in_specs, out_specs=out_specs, check_vma=False)
```

```python
import numpy as np
import jax
import jax.numpy as jnp
from jax import lax
from jax.sharding import PartitionSpec as P

HEAD_DIM = 64
WINDOW = 512


EPSILON = 1e-05
PRECISE = lax.Precision.HIGHEST


def from_behind(shard, axis, by):
    devices = lax.axis_size(axis)
    pairs = [(i, i + by) for i in range(devices) if 0 <= i + by < devices]
    return lax.ppermute(shard, axis, pairs)


def tm_coords(i):
    return (i >> 4) & 3, (i >> 3) & 1, (i >> 1) & 3, i & 1


def tm_index(x, y_half, z, core):
    return ((x * 2 + y_half) * 4 + z) * 2 + core


def butterfly_plan():
    pairs, bits = [], np.zeros((64, 6), np.int32)
    flips = [("z", 1), ("x", 1), ("z", 2), ("x", 2), ("y", 1)]
    round_pairs = [[(i, i ^ 1) for i in range(64)]]
    for i in range(64):
        bits[i, 0] = i & 1
    for r, (axis, mask) in enumerate(flips):
        these = []
        for i in range(64):
            x, y_half, z, core = tm_coords(i)
            zl, xl = (z + core) % 4, (x + core) % 4
            label = {"z": zl, "x": xl, "y": y_half}[axis]
            bits[i, r + 1] = 1 if label & mask else 0
            if axis == "z":
                z = ((zl ^ mask) - core) % 4
            elif axis == "x":
                x = ((xl ^ mask) - core) % 4
            else:
                y_half ^= 1
            these.append((i, tm_index(x, y_half, z, core)))
        round_pairs.append(these)
    pairs = round_pairs
    return pairs, bits


def to_positions(a):
    rows = a.shape[0]
    r = a.reshape(rows, 4, 2, 4, 2, 16)
    first = r[:, :, :, :, 0, :]
    second = jnp.roll(jnp.roll(r[:, :, :, :, 1, :], 1, axis=1), 1, axis=3)
    g = jnp.stack([first, second], axis=1).reshape(rows, 2, 2, 2, 2, 2, 2, 16)
    g = g.transpose(0, 1, 6, 3, 5, 2, 4, 7)
    return g.reshape(rows, 1024)


def labels(i):
    x, y_half, z, core = tm_coords(i)
    return core, (z + core) % 4, (x + core) % 4, y_half


def from_labels(core, zl, xl, y_half):
    return tm_index((xl - core) % 4, y_half, (zl - core) % 4, core)


def radix_plan():
    steps = []
    keep = np.array([i & 1 for i in range(64)], np.int32)
    steps.append((2, keep, [([(i, i ^ 1) for i in range(64)], keep ^ 1)]))
    for mask, shift in ((1, 0), (2, 1)):
        keep = np.zeros(64, np.int32)
        for i in range(64):
            core, zl, xl, y_half = labels(i)
            keep[i] = ((zl & mask) >> shift) * 2 + ((xl & mask) >> shift)
        partners = []
        for d in (1, 2, 3):
            pairs = []
            for i in range(64):
                core, zl, xl, y_half = labels(i)
                zl ^= mask if d & 2 else 0
                xl ^= mask if d & 1 else 0
                pairs.append((i, from_labels(core, zl, xl, y_half)))
            partners.append((pairs, keep ^ d))
        steps.append((4, keep, partners))
    keep = np.array([labels(i)[3] for i in range(64)], np.int32)
    steps.append((2, keep, [([(i, i ^ 8) for i in range(64)], keep ^ 1)]))
    return steps


def glob_steps():
    steps = []
    for mask, shift in ((1, 0), (2, 1)):
        slots = np.zeros(64, np.int32)
        for i in range(64):
            core, zl, xl, y_half = labels(i)
            slots[i] = ((zl & mask) >> shift) * 2 + ((xl & mask) >> shift)
        partners = []
        for d in (1, 2, 3):
            pairs = []
            for i in range(64):
                core, zl, xl, y_half = labels(i)
                zl ^= mask if d & 2 else 0
                xl ^= mask if d & 1 else 0
                pairs.append((i, from_labels(core, zl, xl, y_half)))
            partners.append(pairs)
        steps.append((slots, partners))
    slots = np.array([((i >> 3) & 1) * 2 + (i & 1) for i in range(64)], np.int32)
    steps.append((slots, [[(i, i ^ flip) for i in range(64)] for flip in (1, 8, 9)]))
    return steps


def glob_sum(held, slot):
    ordered = [lax.dynamic_index_in_dim(held, slot ^ s, 0, keepdims=False) for s in range(4)]
    return (ordered[0] + ordered[1]) + (ordered[2] + ordered[3])


def butterfly(parts, glob, shard_index):
    for slot_table, partners in glob_steps():
        held = jnp.stack([glob] + [lax.ppermute(glob, "tm", pairs) for pairs in partners])
        glob = glob_sum(held, jnp.asarray(slot_table)[shard_index])
    glob = glob + lax.ppermute(glob, "mp", [(0, 1), (1, 0)])
    parts, glob = lax.optimization_barrier((parts, glob))
    for ways, keep_table, partners in radix_plan():
        size = parts.shape[0] // ways
        kept = jnp.asarray(keep_table)[shard_index]
        total = lax.dynamic_slice_in_dim(parts, kept * size, size, 0)
        for pairs, send_table in partners:
            sent = jnp.asarray(send_table)[shard_index]
            total = total + lax.ppermute(
                lax.dynamic_slice_in_dim(parts, sent * size, size, 0), "tm", pairs
            )
        parts = total
    return parts, glob


def normalize(rows_in):
    inverse = lax.rsqrt(jnp.mean(rows_in * rows_in, axis=-1, keepdims=True) + EPSILON)
    return (rows_in * inverse, inverse)


def norm_back(gradient, unit_rows, inverse):
    return (gradient - unit_rows * jnp.mean(gradient * unit_rows, axis=-1, keepdims=True)) * inverse


def product(form, left, right):
    return jnp.einsum(form, left, right, preferred_element_type=jnp.float32)


def window_mask(row_count, lead, root):
    query_pos = lax.broadcasted_iota(jnp.int32, (row_count, row_count + lead), 0)
    key_pos = lax.broadcasted_iota(jnp.int32, (row_count, row_count + lead), 1)
    inside = (key_pos > query_pos) & (key_pos <= query_pos + lead)
    return inside & (root - lead + key_pos >= 0)


def block_pass(queries, keys_ext, values_ext, keys_glob, values_glob, grad_rows, allowed):
    scaling = HEAD_DIM ** (-0.5)
    near_scores = product("qhe,khe->hqk", queries, keys_ext) * scaling
    far_scores = product("qhe,khe->hqk", queries, keys_glob) * scaling
    near_scores = jnp.where(allowed[None, :, :], near_scores, -jnp.inf)
    row_top = jnp.maximum(
        jnp.max(near_scores, axis=-1, keepdims=True), jnp.max(far_scores, axis=-1, keepdims=True)
    )
    near_exp = jnp.exp(near_scores - row_top)
    far_exp = jnp.exp(far_scores - row_top)
    row_total = jnp.sum(near_exp, axis=-1, keepdims=True) + jnp.sum(far_exp, axis=-1, keepdims=True)
    near_prob = (near_exp / row_total).astype(jnp.bfloat16)
    far_prob = (far_exp / row_total).astype(jnp.bfloat16)
    attended = (
        product("hqk,khe->qhe", near_prob, values_ext)
        + product("hqk,khe->qhe", far_prob, values_glob)
    ).astype(jnp.bfloat16)
    near_dot = product("qhe,khe->hqk", grad_rows, values_ext)
    far_dot = product("qhe,khe->hqk", grad_rows, values_glob)
    near_p32 = near_prob.astype(jnp.float32)
    far_p32 = far_prob.astype(jnp.float32)
    row_delta = jnp.sum(near_p32 * near_dot, axis=-1, keepdims=True) + jnp.sum(
        far_p32 * far_dot, axis=-1, keepdims=True
    )
    near_grad = (near_p32 * (near_dot - row_delta) * scaling).astype(jnp.bfloat16)
    far_grad = (far_p32 * (far_dot - row_delta) * scaling).astype(jnp.bfloat16)
    query_grad = (
        product("hqk,khe->qhe", near_grad, keys_ext) + product("hqk,khe->qhe", far_grad, keys_glob)
    ).astype(jnp.bfloat16)
    key_grad = product("hqk,qhe->khe", near_grad, queries)
    value_grad = product("hqk,qhe->khe", near_prob, grad_rows)
    glob_key_grad = product("hqk,qhe->khe", far_grad, queries)
    glob_value_grad = product("hqk,qhe->khe", far_prob, grad_rows)
    return (attended, query_grad, key_grad, value_grad, glob_key_grad, glob_value_grad)


def shards(frames, cotangent, weights, summary, owners):
    rows_here = frames.shape[0]
    width = frames.shape[1]
    local_width = weights.shape[2]
    heads_here = local_width // HEAD_DIM
    glob_count = summary.shape[0]
    shard_index = lax.axis_index("tm")
    shard_total = lax.axis_size("tm")
    mp_index = lax.axis_index("mp")
    mp_total = lax.axis_size("mp")
    frames32 = frames.astype(jnp.float32)
    unit_rows, inverse = normalize(frames32)
    normed = unit_rows.astype(jnp.bfloat16)
    block_mean = jnp.mean(frames32, axis=0, keepdims=True)
    pool_unit, pool_inv = normalize(block_mean)
    pooled = pool_unit.astype(jnp.bfloat16)
    pooled_rows = jnp.concatenate([pooled, frames[1:8]], 0)
    pooled_all = lax.all_gather(pooled_rows, "tm", axis=0, tiled=False)[:, 0, :]
    owned_mask = (owners == shard_index).astype(jnp.float32)[:, None]
    anchor = summary.astype(jnp.float32) + jnp.take(pooled_all, owners, axis=0).astype(jnp.float32)
    glob_unit, glob_inv = normalize(anchor)
    glob_normed = glob_unit.astype(jnp.bfloat16)
    kv_weights = weights[:, 1:3, :].reshape(width, 2 * local_width)
    glob_kv = jnp.dot(glob_normed, kv_weights, preferred_element_type=jnp.float32).astype(jnp.bfloat16)
    project = weights[:, :3, :].reshape(width, 3 * local_width)
    qkv = jnp.dot(normed, project, preferred_element_type=jnp.float32).astype(jnp.bfloat16)
    keys_local = qkv[:, local_width : 2 * local_width]
    values_local = qkv[:, 2 * local_width :]
    queries = qkv[:, :local_width].reshape(rows_here, heads_here, HEAD_DIM)
    grad_attended = jnp.dot(cotangent, weights[:, 3, :], preferred_element_type=jnp.float32).astype(
        jnp.bfloat16
    )
    grad_attended = grad_attended.reshape(rows_here, heads_here, HEAD_DIM)
    edge = from_behind(qkv[:, local_width:], "tm", 1)
    edge_keys, edge_values = edge[:, :local_width], edge[:, local_width:]
    keys_ext = jnp.concatenate([edge_keys, keys_local], 0).reshape(
        rows_here + WINDOW, heads_here, HEAD_DIM
    )
    values_ext = jnp.concatenate([edge_values, values_local], 0).reshape(
        rows_here + WINDOW, heads_here, HEAD_DIM
    )
    keys_glob = glob_kv[:, :local_width].reshape(glob_count, heads_here, HEAD_DIM)
    values_glob = glob_kv[:, local_width:].reshape(glob_count, heads_here, HEAD_DIM)
    allowed = window_mask(WINDOW, WINDOW, shard_index * rows_here + 0)
    results = block_pass(
        queries, keys_ext, values_ext, keys_glob, values_glob, grad_attended, allowed
    )
    attended = results[0].reshape(rows_here, local_width)
    grad_queries = results[1].reshape(rows_here, local_width)
    grad_kp = results[2].reshape(rows_here + WINDOW, local_width)
    grad_vp = results[3].reshape(rows_here + WINDOW, local_width)
    grad_kg = results[4].reshape(glob_count, local_width)
    grad_vg = results[5].reshape(glob_count, local_width)
    back = from_behind(
        jnp.concatenate([grad_kp[:WINDOW], grad_vp[:WINDOW]], 1).astype(jnp.bfloat16), "tm", -1
    )
    back_keys, back_values = back[:, :local_width], back[:, local_width:]
    grad_keys = grad_kp[WINDOW:].at[rows_here - WINDOW :].add(back_keys.astype(jnp.float32))
    grad_values = grad_vp[WINDOW:].at[rows_here - WINDOW :].add(back_values.astype(jnp.float32))
    grad_cat = jnp.concatenate(
        [grad_queries, grad_keys.astype(jnp.bfloat16), grad_values.astype(jnp.bfloat16)], 1
    )
    glob_grads = jnp.concatenate([grad_kg, grad_vg], 1)
    kv_weights32 = kv_weights.astype(jnp.float32)
    local_features = lax.dot_general(
        glob_grads, kv_weights32, (((1,), (1,)), ((), ())), precision=PRECISE
    )
    glob_cols = to_positions(glob_normed).astype(jnp.float32)
    inner = lax.dot_general(
        to_positions(normed), grad_cat, (((0,), (0,)), ((), ())), preferred_element_type=jnp.float32
    )
    glob_term = lax.dot_general(glob_cols, glob_grads, (((0,), (0,)), ((), ())), precision=PRECISE)
    inner = inner + jnp.concatenate([jnp.zeros((width, local_width), jnp.float32), glob_term], 1)
    last_term = lax.dot_general(
        to_positions(cotangent), attended, (((0,), (0,)), ((), ())), preferred_element_type=jnp.float32
    )
    weight_parts = jnp.concatenate(
        [inner.reshape(width, 3, local_width), last_term.reshape(width, 1, local_width)], 1
    )
    weight_rows, summary_features = butterfly(
        weight_parts.reshape(width, 4 * local_width), local_features, shard_index
    )
    grad_weights = weight_rows.reshape(width // shard_total, 4, local_width)
    grad_summary = norm_back(summary_features, glob_unit, glob_inv)
    pool_grads = lax.dot_general(
        owned_mask, grad_summary, (((0,), (0,)), ((), ())), precision=PRECISE
    )
    mean_grads = norm_back(pool_grads, pool_unit, pool_inv) / rows_here
    half_rows = rows_here // mp_total
    start_row = mp_index * half_rows
    other_row = (1 - mp_index) * half_rows
    feature_all = lax.dot_general(
        grad_cat, project, (((1,), (1,)), ((), ())), preferred_element_type=jnp.float32
    )
    mine = lax.dynamic_slice_in_dim(feature_all, start_row, half_rows, 0)
    theirs = lax.dynamic_slice_in_dim(feature_all, other_row, half_rows, 0).astype(jnp.bfloat16)
    received = lax.ppermute(theirs, "mp", [(0, 1), (1, 0)])
    feature_grads = mine + received.astype(jnp.float32)
    my_unit = lax.dynamic_slice_in_dim(unit_rows, start_row, half_rows, 0)
    my_inverse = lax.dynamic_slice_in_dim(inverse, start_row, half_rows, 0)
    my_cotangent = lax.dynamic_slice_in_dim(cotangent, start_row, half_rows, 0).astype(jnp.float32)
    grad_frames = (
        my_cotangent + norm_back(feature_grads, my_unit, my_inverse) + mean_grads
    ).astype(jnp.bfloat16)
    return (grad_frames, grad_weights, grad_summary)


def solution(mesh):
    in_specs = (P("tm", None), P("tm", None), P(None, None, "mp"), P(), P())
    out_specs = (P(("tm", "mp"), None), P("tm", None, "mp"), P())
    return jax.shard_map(shards, mesh=mesh, in_specs=in_specs, out_specs=out_specs, check_vma=False)
```

```python
import numpy as np
import jax
import jax.numpy as jnp
from jax import lax
from jax.sharding import PartitionSpec as P

HEAD_DIM = 64
WINDOW = 512


EPSILON = 1e-05
PRECISE = lax.Precision.HIGHEST


def from_behind(shard, axis, by):
    devices = lax.axis_size(axis)
    pairs = [(i, i + by) for i in range(devices) if 0 <= i + by < devices]
    return lax.ppermute(shard, axis, pairs)


def tm_coords(i):
    return (i >> 4) & 3, (i >> 3) & 1, (i >> 1) & 3, i & 1


def tm_index(x, y_half, z, core):
    return ((x * 2 + y_half) * 4 + z) * 2 + core


def butterfly_plan():
    pairs, bits = [], np.zeros((64, 6), np.int32)
    flips = [("z", 1), ("x", 1), ("z", 2), ("x", 2), ("y", 1)]
    round_pairs = [[(i, i ^ 1) for i in range(64)]]
    for i in range(64):
        bits[i, 0] = i & 1
    for r, (axis, mask) in enumerate(flips):
        these = []
        for i in range(64):
            x, y_half, z, core = tm_coords(i)
            zl, xl = (z + core) % 4, (x + core) % 4
            label = {"z": zl, "x": xl, "y": y_half}[axis]
            bits[i, r + 1] = 1 if label & mask else 0
            if axis == "z":
                z = ((zl ^ mask) - core) % 4
            elif axis == "x":
                x = ((xl ^ mask) - core) % 4
            else:
                y_half ^= 1
            these.append((i, tm_index(x, y_half, z, core)))
        round_pairs.append(these)
    pairs = round_pairs
    return pairs, bits


def to_positions(a):
    rows = a.shape[0]
    r = a.reshape(rows, 4, 2, 4, 2, 16)
    first = r[:, :, :, :, 0, :]
    second = jnp.roll(jnp.roll(r[:, :, :, :, 1, :], 1, axis=1), 1, axis=3)
    g = jnp.stack([first, second], axis=1).reshape(rows, 2, 2, 2, 2, 2, 2, 16)
    g = g.transpose(0, 1, 6, 3, 5, 2, 4, 7)
    return g.reshape(rows, 1024)


def labels(i):
    x, y_half, z, core = tm_coords(i)
    return core, (z + core) % 4, (x + core) % 4, y_half


def from_labels(core, zl, xl, y_half):
    return tm_index((xl - core) % 4, y_half, (zl - core) % 4, core)


def radix_plan():
    steps = []
    keep = np.array([i & 1 for i in range(64)], np.int32)
    steps.append((2, keep, [([(i, i ^ 1) for i in range(64)], keep ^ 1)]))
    for mask, shift in ((1, 0), (2, 1)):
        keep = np.zeros(64, np.int32)
        for i in range(64):
            core, zl, xl, y_half = labels(i)
            keep[i] = ((zl & mask) >> shift) * 2 + ((xl & mask) >> shift)
        partners = []
        for d in (1, 2, 3):
            pairs = []
            for i in range(64):
                core, zl, xl, y_half = labels(i)
                zl ^= mask if d & 2 else 0
                xl ^= mask if d & 1 else 0
                pairs.append((i, from_labels(core, zl, xl, y_half)))
            partners.append((pairs, keep ^ d))
        steps.append((4, keep, partners))
    keep = np.array([labels(i)[3] for i in range(64)], np.int32)
    steps.append((2, keep, [([(i, i ^ 8) for i in range(64)], keep ^ 1)]))
    return steps


def glob_steps():
    steps = []
    for mask, shift in ((1, 0), (2, 1)):
        slots = np.zeros(64, np.int32)
        for i in range(64):
            core, zl, xl, y_half = labels(i)
            slots[i] = ((zl & mask) >> shift) * 2 + ((xl & mask) >> shift)
        partners = []
        for d in (1, 2, 3):
            pairs = []
            for i in range(64):
                core, zl, xl, y_half = labels(i)
                zl ^= mask if d & 2 else 0
                xl ^= mask if d & 1 else 0
                pairs.append((i, from_labels(core, zl, xl, y_half)))
            partners.append(pairs)
        steps.append((slots, partners))
    slots = np.array([((i >> 3) & 1) * 2 + (i & 1) for i in range(64)], np.int32)
    steps.append((slots, [[(i, i ^ flip) for i in range(64)] for flip in (1, 8, 9)]))
    return steps


def glob_sum(held, slot):
    ordered = [lax.dynamic_index_in_dim(held, slot ^ s, 0, keepdims=False) for s in range(4)]
    return (ordered[0] + ordered[1]) + (ordered[2] + ordered[3])


def butterfly(parts, glob, shard_index):
    for step, (ways, keep_table, partners) in enumerate(radix_plan()):
        if step == 1:
            parts, glob = lax.optimization_barrier((parts, glob))
            for slot_table, glob_partners in glob_steps():
                held = jnp.stack(
                    [glob] + [lax.ppermute(glob, "tm", pairs) for pairs in glob_partners]
                )
                glob = glob_sum(held, jnp.asarray(slot_table)[shard_index])
            glob = glob + lax.ppermute(glob, "mp", [(0, 1), (1, 0)])
        size = parts.shape[0] // ways
        kept = jnp.asarray(keep_table)[shard_index]
        total = lax.dynamic_slice_in_dim(parts, kept * size, size, 0)
        for pairs, send_table in partners:
            sent = jnp.asarray(send_table)[shard_index]
            total = total + lax.ppermute(
                lax.dynamic_slice_in_dim(parts, sent * size, size, 0), "tm", pairs
            )
        parts = total
    return parts, glob


def normalize(rows_in):
    inverse = lax.rsqrt(jnp.mean(rows_in * rows_in, axis=-1, keepdims=True) + EPSILON)
    return (rows_in * inverse, inverse)


def norm_back(gradient, unit_rows, inverse):
    return (gradient - unit_rows * jnp.mean(gradient * unit_rows, axis=-1, keepdims=True)) * inverse


def product(form, left, right):
    return jnp.einsum(form, left, right, preferred_element_type=jnp.float32)


def window_mask(row_count, lead, root):
    query_pos = lax.broadcasted_iota(jnp.int32, (row_count, row_count + lead), 0)
    key_pos = lax.broadcasted_iota(jnp.int32, (row_count, row_count + lead), 1)
    inside = (key_pos > query_pos) & (key_pos <= query_pos + lead)
    return inside & (root - lead + key_pos >= 0)


def block_pass(queries, keys_ext, values_ext, keys_glob, values_glob, grad_rows, allowed):
    scaling = HEAD_DIM ** (-0.5)
    near_scores = product("qhe,khe->hqk", queries, keys_ext) * scaling
    far_scores = product("qhe,khe->hqk", queries, keys_glob) * scaling
    near_scores = jnp.where(allowed[None, :, :], near_scores, -jnp.inf)
    row_top = jnp.maximum(
        jnp.max(near_scores, axis=-1, keepdims=True), jnp.max(far_scores, axis=-1, keepdims=True)
    )
    near_exp = jnp.exp(near_scores - row_top)
    far_exp = jnp.exp(far_scores - row_top)
    row_total = jnp.sum(near_exp, axis=-1, keepdims=True) + jnp.sum(far_exp, axis=-1, keepdims=True)
    near_prob = (near_exp / row_total).astype(jnp.bfloat16)
    far_prob = (far_exp / row_total).astype(jnp.bfloat16)
    attended = (
        product("hqk,khe->qhe", near_prob, values_ext)
        + product("hqk,khe->qhe", far_prob, values_glob)
    ).astype(jnp.bfloat16)
    near_dot = product("qhe,khe->hqk", grad_rows, values_ext)
    far_dot = product("qhe,khe->hqk", grad_rows, values_glob)
    near_p32 = near_prob.astype(jnp.float32)
    far_p32 = far_prob.astype(jnp.float32)
    row_delta = jnp.sum(near_p32 * near_dot, axis=-1, keepdims=True) + jnp.sum(
        far_p32 * far_dot, axis=-1, keepdims=True
    )
    near_grad = (near_p32 * (near_dot - row_delta) * scaling).astype(jnp.bfloat16)
    far_grad = (far_p32 * (far_dot - row_delta) * scaling).astype(jnp.bfloat16)
    query_grad = (
        product("hqk,khe->qhe", near_grad, keys_ext) + product("hqk,khe->qhe", far_grad, keys_glob)
    ).astype(jnp.bfloat16)
    key_grad = product("hqk,qhe->khe", near_grad, queries)
    value_grad = product("hqk,qhe->khe", near_prob, grad_rows)
    glob_key_grad = product("hqk,qhe->khe", far_grad, queries)
    glob_value_grad = product("hqk,qhe->khe", far_prob, grad_rows)
    return (attended, query_grad, key_grad, value_grad, glob_key_grad, glob_value_grad)


def shards(frames, cotangent, weights, summary, owners):
    rows_here = frames.shape[0]
    width = frames.shape[1]
    local_width = weights.shape[2]
    heads_here = local_width // HEAD_DIM
    glob_count = summary.shape[0]
    shard_index = lax.axis_index("tm")
    shard_total = lax.axis_size("tm")
    mp_index = lax.axis_index("mp")
    mp_total = lax.axis_size("mp")
    frames32 = frames.astype(jnp.float32)
    unit_rows, inverse = normalize(frames32)
    normed = unit_rows.astype(jnp.bfloat16)
    block_mean = jnp.mean(frames32, axis=0, keepdims=True)
    pool_unit, pool_inv = normalize(block_mean)
    pooled = pool_unit.astype(jnp.bfloat16)
    pooled_rows = jnp.concatenate([pooled, frames[1:8]], 0)
    pooled_all = lax.all_gather(pooled_rows, "tm", axis=0, tiled=False)[:, 0, :]
    owned_mask = (owners == shard_index).astype(jnp.float32)[:, None]
    anchor = summary.astype(jnp.float32) + jnp.take(pooled_all, owners, axis=0).astype(jnp.float32)
    glob_unit, glob_inv = normalize(anchor)
    glob_normed = glob_unit.astype(jnp.bfloat16)
    kv_weights = weights[:, 1:3, :].reshape(width, 2 * local_width)
    glob_kv = jnp.dot(glob_normed, kv_weights, preferred_element_type=jnp.float32).astype(jnp.bfloat16)
    project = weights[:, :3, :].reshape(width, 3 * local_width)
    qkv = jnp.dot(normed, project, preferred_element_type=jnp.float32).astype(jnp.bfloat16)
    keys_local = qkv[:, local_width : 2 * local_width]
    values_local = qkv[:, 2 * local_width :]
    queries = qkv[:, :local_width].reshape(rows_here, heads_here, HEAD_DIM)
    grad_attended = jnp.dot(cotangent, weights[:, 3, :], preferred_element_type=jnp.float32).astype(
        jnp.bfloat16
    )
    grad_attended = grad_attended.reshape(rows_here, heads_here, HEAD_DIM)
    edge = from_behind(qkv[:, local_width:], "tm", 1)
    edge_keys, edge_values = edge[:, :local_width], edge[:, local_width:]
    keys_ext = jnp.concatenate([edge_keys, keys_local], 0).reshape(
        rows_here + WINDOW, heads_here, HEAD_DIM
    )
    values_ext = jnp.concatenate([edge_values, values_local], 0).reshape(
        rows_here + WINDOW, heads_here, HEAD_DIM
    )
    keys_glob = glob_kv[:, :local_width].reshape(glob_count, heads_here, HEAD_DIM)
    values_glob = glob_kv[:, local_width:].reshape(glob_count, heads_here, HEAD_DIM)
    allowed = window_mask(WINDOW, WINDOW, shard_index * rows_here + 0)
    results = block_pass(
        queries, keys_ext, values_ext, keys_glob, values_glob, grad_attended, allowed
    )
    attended = results[0].reshape(rows_here, local_width)
    grad_queries = results[1].reshape(rows_here, local_width)
    grad_kp = results[2].reshape(rows_here + WINDOW, local_width)
    grad_vp = results[3].reshape(rows_here + WINDOW, local_width)
    grad_kg = results[4].reshape(glob_count, local_width)
    grad_vg = results[5].reshape(glob_count, local_width)
    back = from_behind(
        jnp.concatenate([grad_kp[:WINDOW], grad_vp[:WINDOW]], 1).astype(jnp.bfloat16), "tm", -1
    )
    back_keys, back_values = back[:, :local_width], back[:, local_width:]
    grad_keys = grad_kp[WINDOW:].at[rows_here - WINDOW :].add(back_keys.astype(jnp.float32))
    grad_values = grad_vp[WINDOW:].at[rows_here - WINDOW :].add(back_values.astype(jnp.float32))
    grad_cat = jnp.concatenate(
        [grad_queries, grad_keys.astype(jnp.bfloat16), grad_values.astype(jnp.bfloat16)], 1
    )
    glob_grads = jnp.concatenate([grad_kg, grad_vg], 1)
    kv_weights32 = kv_weights.astype(jnp.float32)
    local_features = lax.dot_general(
        glob_grads, kv_weights32, (((1,), (1,)), ((), ())), precision=PRECISE
    )
    glob_cols = to_positions(glob_normed).astype(jnp.float32)
    inner = lax.dot_general(
        to_positions(normed), grad_cat, (((0,), (0,)), ((), ())), preferred_element_type=jnp.float32
    )
    glob_term = lax.dot_general(glob_cols, glob_grads, (((0,), (0,)), ((), ())), precision=PRECISE)
    inner = inner + jnp.concatenate([jnp.zeros((width, local_width), jnp.float32), glob_term], 1)
    last_term = lax.dot_general(
        to_positions(cotangent), attended, (((0,), (0,)), ((), ())), preferred_element_type=jnp.float32
    )
    weight_parts = jnp.concatenate(
        [inner.reshape(width, 3, local_width), last_term.reshape(width, 1, local_width)], 1
    )
    weight_rows, summary_features = butterfly(
        weight_parts.reshape(width, 4 * local_width), local_features, shard_index
    )
    grad_weights = weight_rows.reshape(width // shard_total, 4, local_width)
    grad_summary = norm_back(summary_features, glob_unit, glob_inv)
    pool_grads = lax.dot_general(
        owned_mask, grad_summary, (((0,), (0,)), ((), ())), precision=PRECISE
    )
    mean_grads = norm_back(pool_grads, pool_unit, pool_inv) / rows_here
    half_rows = rows_here // mp_total
    start_row = mp_index * half_rows
    other_row = (1 - mp_index) * half_rows
    feature_all = lax.dot_general(
        grad_cat, project, (((1,), (1,)), ((), ())), preferred_element_type=jnp.float32
    )
    mine = lax.dynamic_slice_in_dim(feature_all, start_row, half_rows, 0)
    theirs = lax.dynamic_slice_in_dim(feature_all, other_row, half_rows, 0).astype(jnp.bfloat16)
    received = lax.ppermute(theirs, "mp", [(0, 1), (1, 0)])
    feature_grads = mine + received.astype(jnp.float32)
    my_unit = lax.dynamic_slice_in_dim(unit_rows, start_row, half_rows, 0)
    my_inverse = lax.dynamic_slice_in_dim(inverse, start_row, half_rows, 0)
    my_cotangent = lax.dynamic_slice_in_dim(cotangent, start_row, half_rows, 0).astype(jnp.float32)
    grad_frames = (
        my_cotangent + norm_back(feature_grads, my_unit, my_inverse) + mean_grads
    ).astype(jnp.bfloat16)
    return (grad_frames, grad_weights, grad_summary)


def solution(mesh):
    in_specs = (P("tm", None), P("tm", None), P(None, None, "mp"), P(), P())
    out_specs = (P(("tm", "mp"), None), P("tm", None, "mp"), P())
    return jax.shard_map(shards, mesh=mesh, in_specs=in_specs, out_specs=out_specs, check_vma=False)
```

```python
import numpy as np
import jax
import jax.numpy as jnp
from jax import lax
from jax.sharding import PartitionSpec as P

HEAD_DIM = 64
WINDOW = 512


EPSILON = 1e-05
PRECISE = lax.Precision.HIGHEST


def from_behind(shard, axis, by):
    devices = lax.axis_size(axis)
    pairs = [(i, i + by) for i in range(devices) if 0 <= i + by < devices]
    return lax.ppermute(shard, axis, pairs)


def tm_coords(i):
    return (i >> 4) & 3, (i >> 3) & 1, (i >> 1) & 3, i & 1


def tm_index(x, y_half, z, core):
    return ((x * 2 + y_half) * 4 + z) * 2 + core


def butterfly_plan():
    pairs, bits = [], np.zeros((64, 6), np.int32)
    flips = [("z", 1), ("x", 1), ("z", 2), ("x", 2), ("y", 1)]
    round_pairs = [[(i, i ^ 1) for i in range(64)]]
    for i in range(64):
        bits[i, 0] = i & 1
    for r, (axis, mask) in enumerate(flips):
        these = []
        for i in range(64):
            x, y_half, z, core = tm_coords(i)
            zl, xl = (z + core) % 4, (x + core) % 4
            label = {"z": zl, "x": xl, "y": y_half}[axis]
            bits[i, r + 1] = 1 if label & mask else 0
            if axis == "z":
                z = ((zl ^ mask) - core) % 4
            elif axis == "x":
                x = ((xl ^ mask) - core) % 4
            else:
                y_half ^= 1
            these.append((i, tm_index(x, y_half, z, core)))
        round_pairs.append(these)
    pairs = round_pairs
    return pairs, bits


def to_positions(a):
    rows = a.shape[0]
    r = a.reshape(rows, 4, 2, 4, 2, 16)
    first = r[:, :, :, :, 0, :]
    second = jnp.roll(jnp.roll(r[:, :, :, :, 1, :], 1, axis=1), 1, axis=3)
    g = jnp.stack([first, second], axis=1).reshape(rows, 2, 2, 2, 2, 2, 2, 16)
    g = g.transpose(0, 1, 6, 3, 5, 2, 4, 7)
    return g.reshape(rows, 1024)


def butterfly(parts, glob, shard_index):
    pairs, bits = butterfly_plan()
    my_bits = jnp.asarray(bits)[shard_index]
    for r in range(6):
        half = parts.shape[0] // 2
        b = my_bits[r]
        keep = lax.dynamic_slice_in_dim(parts, b * half, half, 0)
        send = lax.dynamic_slice_in_dim(parts, (1 - b) * half, half, 0)
        got, got_glob = lax.ppermute((send, glob), "tm", pairs[r])
        parts = keep + got
        glob = glob + got_glob
    return parts, glob


def normalize(rows_in):
    inverse = lax.rsqrt(jnp.mean(rows_in * rows_in, axis=-1, keepdims=True) + EPSILON)
    return (rows_in * inverse, inverse)


def norm_back(gradient, unit_rows, inverse):
    return (gradient - unit_rows * jnp.mean(gradient * unit_rows, axis=-1, keepdims=True)) * inverse


def product(form, left, right):
    return jnp.einsum(form, left, right, preferred_element_type=jnp.float32)


def window_mask(row_count, lead, root):
    query_pos = lax.broadcasted_iota(jnp.int32, (row_count, row_count + lead), 0)
    key_pos = lax.broadcasted_iota(jnp.int32, (row_count, row_count + lead), 1)
    inside = (key_pos > query_pos) & (key_pos <= query_pos + lead)
    return inside & (root - lead + key_pos >= 0)


def block_pass(queries, keys_ext, values_ext, keys_glob, values_glob, grad_rows, allowed):
    scaling = HEAD_DIM ** (-0.5)
    near_scores = product("qhe,khe->hqk", queries, keys_ext) * scaling
    far_scores = product("qhe,khe->hqk", queries, keys_glob) * scaling
    near_scores = jnp.where(allowed[None, :, :], near_scores, -jnp.inf)
    row_top = jnp.maximum(
        jnp.max(near_scores, axis=-1, keepdims=True), jnp.max(far_scores, axis=-1, keepdims=True)
    )
    near_exp = jnp.exp(near_scores - row_top)
    far_exp = jnp.exp(far_scores - row_top)
    row_total = jnp.sum(near_exp, axis=-1, keepdims=True) + jnp.sum(far_exp, axis=-1, keepdims=True)
    near_prob = (near_exp / row_total).astype(jnp.bfloat16)
    far_prob = (far_exp / row_total).astype(jnp.bfloat16)
    attended = (
        product("hqk,khe->qhe", near_prob, values_ext)
        + product("hqk,khe->qhe", far_prob, values_glob)
    ).astype(jnp.bfloat16)
    near_dot = product("qhe,khe->hqk", grad_rows, values_ext)
    far_dot = product("qhe,khe->hqk", grad_rows, values_glob)
    near_p32 = near_prob.astype(jnp.float32)
    far_p32 = far_prob.astype(jnp.float32)
    row_delta = jnp.sum(near_p32 * near_dot, axis=-1, keepdims=True) + jnp.sum(
        far_p32 * far_dot, axis=-1, keepdims=True
    )
    near_grad = (near_p32 * (near_dot - row_delta) * scaling).astype(jnp.bfloat16)
    far_grad = (far_p32 * (far_dot - row_delta) * scaling).astype(jnp.bfloat16)
    query_grad = (
        product("hqk,khe->qhe", near_grad, keys_ext) + product("hqk,khe->qhe", far_grad, keys_glob)
    ).astype(jnp.bfloat16)
    key_grad = product("hqk,qhe->khe", near_grad, queries)
    value_grad = product("hqk,qhe->khe", near_prob, grad_rows)
    glob_key_grad = product("hqk,qhe->khe", far_grad, queries)
    glob_value_grad = product("hqk,qhe->khe", far_prob, grad_rows)
    return (attended, query_grad, key_grad, value_grad, glob_key_grad, glob_value_grad)


def shards(frames, cotangent, weights, summary, owners):
    rows_here = frames.shape[0]
    width = frames.shape[1]
    local_width = weights.shape[2]
    heads_here = local_width // HEAD_DIM
    glob_count = summary.shape[0]
    shard_index = lax.axis_index("tm")
    shard_total = lax.axis_size("tm")
    mp_index = lax.axis_index("mp")
    mp_total = lax.axis_size("mp")
    frames32 = frames.astype(jnp.float32)
    unit_rows, inverse = normalize(frames32)
    normed = unit_rows.astype(jnp.bfloat16)
    block_mean = jnp.mean(frames32, axis=0, keepdims=True)
    pool_unit, pool_inv = normalize(block_mean)
    pooled = pool_unit.astype(jnp.bfloat16)
    pooled_rows = jnp.concatenate([pooled, frames[1:8]], 0)
    pooled_all = lax.all_gather(pooled_rows, "tm", axis=0, tiled=False)[:, 0, :]
    owned_mask = (owners == shard_index).astype(jnp.float32)[:, None]
    anchor = summary.astype(jnp.float32) + jnp.take(pooled_all, owners, axis=0).astype(jnp.float32)
    glob_unit, glob_inv = normalize(anchor)
    glob_normed = glob_unit.astype(jnp.bfloat16)
    stacked = jnp.transpose(weights, (1, 0, 2))
    glob_kv = product("gf,kfc->gkc", glob_normed, stacked[1:3]).astype(jnp.bfloat16)
    glob_kv = glob_kv.reshape(glob_count, 2 * local_width)
    qkv = product("tf,kfc->tkc", normed, stacked[:3]).astype(jnp.bfloat16)
    qkv = qkv.reshape(rows_here, 3 * local_width)
    keys_local = qkv[:, local_width : 2 * local_width]
    values_local = qkv[:, 2 * local_width :]
    queries = qkv[:, :local_width].reshape(rows_here, heads_here, HEAD_DIM)
    grad_attended = jnp.dot(cotangent, stacked[3], preferred_element_type=jnp.float32).astype(
        jnp.bfloat16
    )
    grad_attended = grad_attended.reshape(rows_here, heads_here, HEAD_DIM)
    edge = from_behind(qkv[:, local_width:], "tm", 1)
    edge_keys, edge_values = edge[:, :local_width], edge[:, local_width:]
    keys_ext = jnp.concatenate([edge_keys, keys_local], 0).reshape(
        rows_here + WINDOW, heads_here, HEAD_DIM
    )
    values_ext = jnp.concatenate([edge_values, values_local], 0).reshape(
        rows_here + WINDOW, heads_here, HEAD_DIM
    )
    keys_glob = glob_kv[:, :local_width].reshape(glob_count, heads_here, HEAD_DIM)
    values_glob = glob_kv[:, local_width:].reshape(glob_count, heads_here, HEAD_DIM)
    allowed = window_mask(WINDOW, WINDOW, shard_index * rows_here + 0)
    results = block_pass(
        queries, keys_ext, values_ext, keys_glob, values_glob, grad_attended, allowed
    )
    attended = results[0].reshape(rows_here, local_width)
    grad_queries = results[1].reshape(rows_here, local_width)
    grad_kp = results[2].reshape(rows_here + WINDOW, local_width)
    grad_vp = results[3].reshape(rows_here + WINDOW, local_width)
    grad_kg = results[4].reshape(glob_count, local_width)
    grad_vg = results[5].reshape(glob_count, local_width)
    back = from_behind(
        jnp.concatenate([grad_kp[:WINDOW], grad_vp[:WINDOW]], 1).astype(jnp.bfloat16), "tm", -1
    )
    back_keys, back_values = back[:, :local_width], back[:, local_width:]
    grad_keys = grad_kp[WINDOW:].at[rows_here - WINDOW :].add(back_keys.astype(jnp.float32))
    grad_values = grad_vp[WINDOW:].at[rows_here - WINDOW :].add(back_values.astype(jnp.float32))
    grad_cat = jnp.concatenate(
        [grad_queries, grad_keys.astype(jnp.bfloat16), grad_values.astype(jnp.bfloat16)], 1
    )
    glob_grads = jnp.concatenate([grad_kg, grad_vg], 1)
    local_features = jnp.einsum(
        "gkc,kfc->gf",
        glob_grads.reshape(glob_count, 2, local_width),
        stacked[1:3].astype(jnp.float32),
        precision=PRECISE,
    )
    glob_cols = to_positions(glob_normed).astype(jnp.float32)
    inner = lax.dot_general(
        to_positions(normed), grad_cat, (((0,), (0,)), ((), ())), preferred_element_type=jnp.float32
    )
    glob_term = lax.dot_general(glob_cols, glob_grads, (((0,), (0,)), ((), ())), precision=PRECISE)
    inner = inner + jnp.concatenate([jnp.zeros((width, local_width), jnp.float32), glob_term], 1)
    last_term = lax.dot_general(
        to_positions(cotangent), attended, (((0,), (0,)), ((), ())), preferred_element_type=jnp.float32
    )
    weight_parts = jnp.concatenate(
        [inner.reshape(width, 3, local_width), last_term.reshape(width, 1, local_width)], 1
    )
    weight_rows, tm_features = butterfly(
        weight_parts.reshape(width, 4 * local_width), local_features, shard_index
    )
    grad_weights = weight_rows.reshape(width // shard_total, 4, local_width)
    summary_features = tm_features + lax.ppermute(tm_features, "mp", [(0, 1), (1, 0)])
    grad_summary = norm_back(summary_features, glob_unit, glob_inv)
    pool_grads = lax.dot_general(
        owned_mask, grad_summary, (((0,), (0,)), ((), ())), precision=PRECISE
    )
    mean_grads = norm_back(pool_grads, pool_unit, pool_inv) / rows_here
    half_rows = rows_here // mp_total
    start_row = mp_index * half_rows
    other_row = (1 - mp_index) * half_rows
    feature_all = product("tkc,kfc->tf", grad_cat.reshape(rows_here, 3, local_width), stacked[:3])
    mine = lax.dynamic_slice_in_dim(feature_all, start_row, half_rows, 0)
    theirs = lax.dynamic_slice_in_dim(feature_all, other_row, half_rows, 0).astype(jnp.bfloat16)
    received = lax.ppermute(theirs, "mp", [(0, 1), (1, 0)])
    feature_grads = mine + received.astype(jnp.float32)
    my_unit = lax.dynamic_slice_in_dim(unit_rows, start_row, half_rows, 0)
    my_inverse = lax.dynamic_slice_in_dim(inverse, start_row, half_rows, 0)
    my_cotangent = lax.dynamic_slice_in_dim(cotangent, start_row, half_rows, 0).astype(jnp.float32)
    grad_frames = (
        my_cotangent + norm_back(feature_grads, my_unit, my_inverse) + mean_grads
    ).astype(jnp.bfloat16)
    return (grad_frames, grad_weights, grad_summary)


def solution(mesh):
    in_specs = (P("tm", None), P("tm", None), P(None, None, "mp"), P(), P())
    out_specs = (P(("tm", "mp"), None), P("tm", None, "mp"), P())
    return jax.shard_map(shards, mesh=mesh, in_specs=in_specs, out_specs=out_specs, check_vma=False)
```

```python
import numpy as np
import jax
import jax.numpy as jnp
from jax import lax
from jax.sharding import PartitionSpec as P

HEAD_DIM = 64
WINDOW = 512


EPSILON = 1e-05
PRECISE = lax.Precision.HIGHEST


def from_behind(shard, axis, by):
    devices = lax.axis_size(axis)
    pairs = [(i, i + by) for i in range(devices) if 0 <= i + by < devices]
    return lax.ppermute(shard, axis, pairs)


def tm_coords(i):
    return (i >> 4) & 3, (i >> 3) & 1, (i >> 1) & 3, i & 1


def tm_index(x, y_half, z, core):
    return ((x * 2 + y_half) * 4 + z) * 2 + core


def butterfly_plan():
    pairs, bits = [], np.zeros((64, 6), np.int32)
    flips = [("z", 1), ("x", 1), ("z", 2), ("x", 2), ("y", 1)]
    round_pairs = [[(i, i ^ 1) for i in range(64)]]
    for i in range(64):
        bits[i, 0] = i & 1
    for r, (axis, mask) in enumerate(flips):
        these = []
        for i in range(64):
            x, y_half, z, core = tm_coords(i)
            zl, xl = (z + core) % 4, (x + core) % 4
            label = {"z": zl, "x": xl, "y": y_half}[axis]
            bits[i, r + 1] = 1 if label & mask else 0
            if axis == "z":
                z = ((zl ^ mask) - core) % 4
            elif axis == "x":
                x = ((xl ^ mask) - core) % 4
            else:
                y_half ^= 1
            these.append((i, tm_index(x, y_half, z, core)))
        round_pairs.append(these)
    pairs = round_pairs
    return pairs, bits


def to_positions(a):
    rows = a.shape[0]
    r = a.reshape(rows, 4, 2, 4, 2, 16)
    first = r[:, :, :, :, 0, :]
    second = jnp.roll(jnp.roll(r[:, :, :, :, 1, :], 1, axis=1), 1, axis=3)
    g = jnp.stack([first, second], axis=1).reshape(rows, 2, 2, 2, 2, 2, 2, 16)
    g = g.transpose(0, 1, 6, 3, 5, 2, 4, 7)
    return g.reshape(rows, 1024)


def butterfly(parts, glob, shard_index):
    pairs, bits = butterfly_plan()
    my_bits = jnp.asarray(bits)[shard_index]
    for r in range(6):
        half = parts.shape[0] // 2
        b = my_bits[r]
        keep = lax.dynamic_slice_in_dim(parts, b * half, half, 0)
        send = lax.dynamic_slice_in_dim(parts, (1 - b) * half, half, 0)
        got, got_glob = lax.ppermute((send, glob), "tm", pairs[r])
        parts = keep + got
        glob = glob + got_glob
    return parts, glob


def normalize(rows_in):
    inverse = lax.rsqrt(jnp.mean(rows_in * rows_in, axis=-1, keepdims=True) + EPSILON)
    return (rows_in * inverse, inverse)


def norm_back(gradient, unit_rows, inverse):
    return (gradient - unit_rows * jnp.mean(gradient * unit_rows, axis=-1, keepdims=True)) * inverse


def product(form, left, right):
    return jnp.einsum(form, left, right, preferred_element_type=jnp.float32)


def window_mask(row_count, lead, root):
    query_pos = lax.broadcasted_iota(jnp.int32, (row_count, row_count + lead), 0)
    key_pos = lax.broadcasted_iota(jnp.int32, (row_count, row_count + lead), 1)
    inside = (key_pos > query_pos) & (key_pos <= query_pos + lead)
    return inside & (root - lead + key_pos >= 0)


def block_pass(queries, keys_ext, values_ext, keys_glob, values_glob, grad_rows, allowed):
    scaling = HEAD_DIM ** (-0.5)
    near_scores = product("qhe,khe->hqk", queries, keys_ext) * scaling
    far_scores = product("qhe,khe->hqk", queries, keys_glob) * scaling
    near_scores = jnp.where(allowed[None, :, :], near_scores, -jnp.inf)
    row_top = jnp.maximum(
        jnp.max(near_scores, axis=-1, keepdims=True), jnp.max(far_scores, axis=-1, keepdims=True)
    )
    near_exp = jnp.exp(near_scores - row_top)
    far_exp = jnp.exp(far_scores - row_top)
    row_total = jnp.sum(near_exp, axis=-1, keepdims=True) + jnp.sum(far_exp, axis=-1, keepdims=True)
    near_prob = (near_exp / row_total).astype(jnp.bfloat16)
    far_prob = (far_exp / row_total).astype(jnp.bfloat16)
    attended = (
        product("hqk,khe->qhe", near_prob, values_ext)
        + product("hqk,khe->qhe", far_prob, values_glob)
    ).astype(jnp.bfloat16)
    near_dot = product("qhe,khe->hqk", grad_rows, values_ext)
    far_dot = product("qhe,khe->hqk", grad_rows, values_glob)
    near_p32 = near_prob.astype(jnp.float32)
    far_p32 = far_prob.astype(jnp.float32)
    row_delta = jnp.sum(near_p32 * near_dot, axis=-1, keepdims=True) + jnp.sum(
        far_p32 * far_dot, axis=-1, keepdims=True
    )
    near_grad = (near_p32 * (near_dot - row_delta) * scaling).astype(jnp.bfloat16)
    far_grad = (far_p32 * (far_dot - row_delta) * scaling).astype(jnp.bfloat16)
    query_grad = (
        product("hqk,khe->qhe", near_grad, keys_ext) + product("hqk,khe->qhe", far_grad, keys_glob)
    ).astype(jnp.bfloat16)
    key_grad = product("hqk,qhe->khe", near_grad, queries)
    value_grad = product("hqk,qhe->khe", near_prob, grad_rows)
    glob_key_grad = product("hqk,qhe->khe", far_grad, queries)
    glob_value_grad = product("hqk,qhe->khe", far_prob, grad_rows)
    return (attended, query_grad, key_grad, value_grad, glob_key_grad, glob_value_grad)


def shards(frames, cotangent, weights, summary, owners):
    rows_here = frames.shape[0]
    width = frames.shape[1]
    local_width = weights.shape[2]
    heads_here = local_width // HEAD_DIM
    glob_count = summary.shape[0]
    shard_index = lax.axis_index("tm")
    shard_total = lax.axis_size("tm")
    mp_index = lax.axis_index("mp")
    mp_total = lax.axis_size("mp")
    frames32 = frames.astype(jnp.float32)
    unit_rows, inverse = normalize(frames32)
    normed = unit_rows.astype(jnp.bfloat16)
    block_mean = jnp.mean(frames32, axis=0, keepdims=True)
    pool_unit, pool_inv = normalize(block_mean)
    pooled = pool_unit.astype(jnp.bfloat16)
    slots = lax.broadcasted_iota(jnp.int32, (shard_total, 1), 0)
    pooled_all = jnp.where(slots == shard_index, pooled, jnp.zeros_like(pooled))
    for step in range(3):
        shift = 2 * step
        pooled_all = pooled_all + sum(
            lax.ppermute(pooled_all, "tm", [(i, i ^ (d << shift)) for i in range(64)])
            for d in (1, 2, 3)
        )
    owned_mask = (owners == shard_index).astype(jnp.float32)[:, None]
    anchor = summary.astype(jnp.float32) + jnp.take(pooled_all, owners, axis=0).astype(jnp.float32)
    glob_unit, glob_inv = normalize(anchor)
    glob_normed = glob_unit.astype(jnp.bfloat16)
    stacked = jnp.transpose(weights, (1, 0, 2))
    glob_kv = product("gf,kfc->gkc", glob_normed, stacked[1:3]).astype(jnp.bfloat16)
    glob_kv = glob_kv.reshape(glob_count, 2 * local_width)
    qkv = product("tf,kfc->tkc", normed, stacked[:3]).astype(jnp.bfloat16)
    qkv = qkv.reshape(rows_here, 3 * local_width)
    keys_local = qkv[:, local_width : 2 * local_width]
    values_local = qkv[:, 2 * local_width :]
    queries = qkv[:, :local_width].reshape(rows_here, heads_here, HEAD_DIM)
    grad_attended = jnp.dot(cotangent, stacked[3], preferred_element_type=jnp.float32).astype(
        jnp.bfloat16
    )
    grad_attended = grad_attended.reshape(rows_here, heads_here, HEAD_DIM)
    edge = from_behind(qkv[:, local_width:], "tm", 1)
    edge_keys, edge_values = edge[:, :local_width], edge[:, local_width:]
    keys_ext = jnp.concatenate([edge_keys, keys_local], 0).reshape(
        rows_here + WINDOW, heads_here, HEAD_DIM
    )
    values_ext = jnp.concatenate([edge_values, values_local], 0).reshape(
        rows_here + WINDOW, heads_here, HEAD_DIM
    )
    keys_glob = glob_kv[:, :local_width].reshape(glob_count, heads_here, HEAD_DIM)
    values_glob = glob_kv[:, local_width:].reshape(glob_count, heads_here, HEAD_DIM)
    allowed = window_mask(WINDOW, WINDOW, shard_index * rows_here + 0)
    results = block_pass(
        queries, keys_ext, values_ext, keys_glob, values_glob, grad_attended, allowed
    )
    attended = results[0].reshape(rows_here, local_width)
    grad_queries = results[1].reshape(rows_here, local_width)
    grad_kp = results[2].reshape(rows_here + WINDOW, local_width)
    grad_vp = results[3].reshape(rows_here + WINDOW, local_width)
    grad_kg = results[4].reshape(glob_count, local_width)
    grad_vg = results[5].reshape(glob_count, local_width)
    back = from_behind(
        jnp.concatenate([grad_kp[:WINDOW], grad_vp[:WINDOW]], 1).astype(jnp.bfloat16), "tm", -1
    )
    back_keys, back_values = back[:, :local_width], back[:, local_width:]
    grad_keys = grad_kp[WINDOW:].at[rows_here - WINDOW :].add(back_keys.astype(jnp.float32))
    grad_values = grad_vp[WINDOW:].at[rows_here - WINDOW :].add(back_values.astype(jnp.float32))
    grad_cat = jnp.concatenate(
        [grad_queries, grad_keys.astype(jnp.bfloat16), grad_values.astype(jnp.bfloat16)], 1
    )
    glob_grads = jnp.concatenate([grad_kg, grad_vg], 1)
    local_features = jnp.einsum(
        "gkc,kfc->gf",
        glob_grads.reshape(glob_count, 2, local_width),
        stacked[1:3].astype(jnp.float32),
        precision=PRECISE,
    )
    glob_cols = to_positions(glob_normed).astype(jnp.float32)
    inner = lax.dot_general(
        to_positions(normed), grad_cat, (((0,), (0,)), ((), ())), preferred_element_type=jnp.float32
    )
    glob_term = lax.dot_general(glob_cols, glob_grads, (((0,), (0,)), ((), ())), precision=PRECISE)
    inner = inner + jnp.concatenate([jnp.zeros((width, local_width), jnp.float32), glob_term], 1)
    last_term = lax.dot_general(
        to_positions(cotangent), attended, (((0,), (0,)), ((), ())), preferred_element_type=jnp.float32
    )
    weight_parts = jnp.concatenate(
        [inner.reshape(width, 3, local_width), last_term.reshape(width, 1, local_width)], 1
    )
    weight_rows, tm_features = butterfly(
        weight_parts.reshape(width, 4 * local_width), local_features, shard_index
    )
    grad_weights = weight_rows.reshape(width // shard_total, 4, local_width)
    summary_features = tm_features + lax.ppermute(tm_features, "mp", [(0, 1), (1, 0)])
    grad_summary = norm_back(summary_features, glob_unit, glob_inv)
    pool_grads = lax.dot_general(
        owned_mask, grad_summary, (((0,), (0,)), ((), ())), precision=PRECISE
    )
    mean_grads = norm_back(pool_grads, pool_unit, pool_inv) / rows_here
    half_rows = rows_here // mp_total
    start_row = mp_index * half_rows
    other_row = (1 - mp_index) * half_rows
    feature_all = product("tkc,kfc->tf", grad_cat.reshape(rows_here, 3, local_width), stacked[:3])
    mine = lax.dynamic_slice_in_dim(feature_all, start_row, half_rows, 0)
    theirs = lax.dynamic_slice_in_dim(feature_all, other_row, half_rows, 0).astype(jnp.bfloat16)
    received = lax.ppermute(theirs, "mp", [(0, 1), (1, 0)])
    feature_grads = mine + received.astype(jnp.float32)
    my_unit = lax.dynamic_slice_in_dim(unit_rows, start_row, half_rows, 0)
    my_inverse = lax.dynamic_slice_in_dim(inverse, start_row, half_rows, 0)
    my_cotangent = lax.dynamic_slice_in_dim(cotangent, start_row, half_rows, 0).astype(jnp.float32)
    grad_frames = (
        my_cotangent + norm_back(feature_grads, my_unit, my_inverse) + mean_grads
    ).astype(jnp.bfloat16)
    return (grad_frames, grad_weights, grad_summary)


def solution(mesh):
    in_specs = (P("tm", None), P("tm", None), P(None, None, "mp"), P(), P())
    out_specs = (P(("tm", "mp"), None), P("tm", None, "mp"), P())
    return jax.shard_map(shards, mesh=mesh, in_specs=in_specs, out_specs=out_specs, check_vma=False)
```

```python
import numpy as np
import jax
import jax.numpy as jnp
from jax import lax
from jax.sharding import PartitionSpec as P

HEAD_DIM = 64
WINDOW = 512


EPSILON = 1e-05
PRECISE = lax.Precision.HIGHEST


def from_behind(shard, axis, by):
    devices = lax.axis_size(axis)
    pairs = [(i, i + by) for i in range(devices) if 0 <= i + by < devices]
    return lax.ppermute(shard, axis, pairs)


def tm_coords(i):
    return (i >> 4) & 3, (i >> 3) & 1, (i >> 1) & 3, i & 1


def tm_index(x, y_half, z, core):
    return ((x * 2 + y_half) * 4 + z) * 2 + core


def butterfly_plan():
    pairs, bits = [], np.zeros((64, 6), np.int32)
    flips = [("z", 1), ("x", 1), ("z", 2), ("x", 2), ("y", 1)]
    round_pairs = [[(i, i ^ 1) for i in range(64)]]
    for i in range(64):
        bits[i, 0] = i & 1
    for r, (axis, mask) in enumerate(flips):
        these = []
        for i in range(64):
            x, y_half, z, core = tm_coords(i)
            zl, xl = (z + core) % 4, (x + core) % 4
            label = {"z": zl, "x": xl, "y": y_half}[axis]
            bits[i, r + 1] = 1 if label & mask else 0
            if axis == "z":
                z = ((zl ^ mask) - core) % 4
            elif axis == "x":
                x = ((xl ^ mask) - core) % 4
            else:
                y_half ^= 1
            these.append((i, tm_index(x, y_half, z, core)))
        round_pairs.append(these)
    pairs = round_pairs
    return pairs, bits


def to_positions(a):
    rows = a.shape[0]
    r = a.reshape(rows, 4, 2, 4, 2, 16)
    first = r[:, :, :, :, 0, :]
    second = jnp.roll(jnp.roll(r[:, :, :, :, 1, :], 1, axis=1), 1, axis=3)
    g = jnp.stack([first, second], axis=1).reshape(rows, 2, 2, 2, 2, 2, 2, 16)
    g = g.transpose(0, 1, 6, 3, 5, 2, 4, 7)
    return g.reshape(rows, 1024)


def labels(i):
    x, y_half, z, core = tm_coords(i)
    return core, (z + core) % 4, (x + core) % 4, y_half


def from_labels(core, zl, xl, y_half):
    return tm_index((xl - core) % 4, y_half, (zl - core) % 4, core)


def radix_plan():
    steps = []
    keep = np.array([i & 1 for i in range(64)], np.int32)
    steps.append((2, keep, [([(i, i ^ 1) for i in range(64)], keep ^ 1)]))
    for mask, shift in ((1, 0), (2, 1)):
        keep = np.zeros(64, np.int32)
        for i in range(64):
            core, zl, xl, y_half = labels(i)
            keep[i] = ((zl & mask) >> shift) * 2 + ((xl & mask) >> shift)
        partners = []
        for d in (1, 2, 3):
            pairs = []
            for i in range(64):
                core, zl, xl, y_half = labels(i)
                zl ^= mask if d & 2 else 0
                xl ^= mask if d & 1 else 0
                pairs.append((i, from_labels(core, zl, xl, y_half)))
            partners.append((pairs, keep ^ d))
        steps.append((4, keep, partners))
    keep = np.array([labels(i)[3] for i in range(64)], np.int32)
    steps.append((2, keep, [([(i, i ^ 8) for i in range(64)], keep ^ 1)]))
    return steps


def glob_steps():
    steps = []
    for mask, shift in ((1, 0), (2, 1)):
        slots = np.zeros(64, np.int32)
        for i in range(64):
            core, zl, xl, y_half = labels(i)
            slots[i] = ((zl & mask) >> shift) * 2 + ((xl & mask) >> shift)
        partners = []
        for d in (1, 2, 3):
            pairs = []
            for i in range(64):
                core, zl, xl, y_half = labels(i)
                zl ^= mask if d & 2 else 0
                xl ^= mask if d & 1 else 0
                pairs.append((i, from_labels(core, zl, xl, y_half)))
            partners.append(pairs)
        steps.append((slots, partners))
    slots = np.array([((i >> 3) & 1) * 2 + (i & 1) for i in range(64)], np.int32)
    steps.append((slots, [[(i, i ^ flip) for i in range(64)] for flip in (1, 8, 9)]))
    return steps


def glob_sum(held, slot):
    ordered = [lax.dynamic_index_in_dim(held, slot ^ s, 0, keepdims=False) for s in range(4)]
    return (ordered[0] + ordered[1]) + (ordered[2] + ordered[3])


def butterfly(parts, glob, shard_index):
    plan = radix_plan()
    glob_plan = glob_steps()
    glob_shape = glob.shape
    carried = glob.reshape(glob.size // parts.shape[1], parts.shape[1])
    for step, (ways, keep_table, partners) in enumerate(plan):
        size = parts.shape[0] // ways
        kept = jnp.asarray(keep_table)[shard_index]
        total = lax.dynamic_slice_in_dim(parts, kept * size, size, 0)
        pieces = [
            (pairs, lax.dynamic_slice_in_dim(parts, jnp.asarray(sent)[shard_index] * size, size, 0))
            for pairs, sent in partners
        ]
        if ways == 4:
            held = [carried]
            for pairs, piece in pieces:
                got = lax.ppermute(jnp.concatenate([piece, carried], 0), "tm", pairs)
                total = total + got[:size]
                held.append(got[size:])
            carried = glob_sum(jnp.stack(held), jnp.asarray(glob_plan[step - 1][0])[shard_index])
        elif step == 0:
            pairs, piece = pieces[0]
            total = total + lax.ppermute(piece, "tm", pairs)
        else:
            slot_table, last_partners = glob_plan[2]
            pairs, piece = pieces[0]
            got = lax.ppermute(jnp.concatenate([piece, carried], 0), "tm", pairs)
            total = total + got[:size]
            held = [
                carried,
                lax.ppermute(carried, "tm", last_partners[0]),
                got[size:],
                lax.ppermute(carried, "tm", last_partners[2]),
            ]
            carried = glob_sum(jnp.stack(held), jnp.asarray(slot_table)[shard_index])
        parts = total
    return parts, carried.reshape(glob_shape)


def normalize(rows_in):
    inverse = lax.rsqrt(jnp.mean(rows_in * rows_in, axis=-1, keepdims=True) + EPSILON)
    return (rows_in * inverse, inverse)


def norm_back(gradient, unit_rows, inverse):
    return (gradient - unit_rows * jnp.mean(gradient * unit_rows, axis=-1, keepdims=True)) * inverse


def product(form, left, right):
    return jnp.einsum(form, left, right, preferred_element_type=jnp.float32)


def window_mask(row_count, lead, root):
    query_pos = lax.broadcasted_iota(jnp.int32, (row_count, row_count + lead), 0)
    key_pos = lax.broadcasted_iota(jnp.int32, (row_count, row_count + lead), 1)
    inside = (key_pos > query_pos) & (key_pos <= query_pos + lead)
    return inside & (root - lead + key_pos >= 0)


def block_pass(queries, keys_ext, values_ext, keys_glob, values_glob, grad_rows, allowed):
    scaling = HEAD_DIM ** (-0.5)
    near_scores = product("qhe,khe->hqk", queries, keys_ext) * scaling
    far_scores = product("qhe,khe->hqk", queries, keys_glob) * scaling
    near_scores = jnp.where(allowed[None, :, :], near_scores, -jnp.inf)
    row_top = jnp.maximum(
        jnp.max(near_scores, axis=-1, keepdims=True), jnp.max(far_scores, axis=-1, keepdims=True)
    )
    near_exp = jnp.exp(near_scores - row_top)
    far_exp = jnp.exp(far_scores - row_top)
    row_total = jnp.sum(near_exp, axis=-1, keepdims=True) + jnp.sum(far_exp, axis=-1, keepdims=True)
    near_prob = (near_exp / row_total).astype(jnp.bfloat16)
    far_prob = (far_exp / row_total).astype(jnp.bfloat16)
    attended = (
        product("hqk,khe->qhe", near_prob, values_ext)
        + product("hqk,khe->qhe", far_prob, values_glob)
    ).astype(jnp.bfloat16)
    near_dot = product("qhe,khe->hqk", grad_rows, values_ext)
    far_dot = product("qhe,khe->hqk", grad_rows, values_glob)
    near_p32 = near_prob.astype(jnp.float32)
    far_p32 = far_prob.astype(jnp.float32)
    row_delta = jnp.sum(near_p32 * near_dot, axis=-1, keepdims=True) + jnp.sum(
        far_p32 * far_dot, axis=-1, keepdims=True
    )
    near_grad = (near_p32 * (near_dot - row_delta) * scaling).astype(jnp.bfloat16)
    far_grad = (far_p32 * (far_dot - row_delta) * scaling).astype(jnp.bfloat16)
    query_grad = (
        product("hqk,khe->qhe", near_grad, keys_ext) + product("hqk,khe->qhe", far_grad, keys_glob)
    ).astype(jnp.bfloat16)
    key_grad = product("hqk,qhe->khe", near_grad, queries)
    value_grad = product("hqk,qhe->khe", near_prob, grad_rows)
    glob_key_grad = product("hqk,qhe->khe", far_grad, queries)
    glob_value_grad = product("hqk,qhe->khe", far_prob, grad_rows)
    return (attended, query_grad, key_grad, value_grad, glob_key_grad, glob_value_grad)


def shards(frames, cotangent, weights, summary, owners):
    rows_here = frames.shape[0]
    width = frames.shape[1]
    local_width = weights.shape[2]
    heads_here = local_width // HEAD_DIM
    glob_count = summary.shape[0]
    shard_index = lax.axis_index("tm")
    shard_total = lax.axis_size("tm")
    mp_index = lax.axis_index("mp")
    mp_total = lax.axis_size("mp")
    frames32 = frames.astype(jnp.float32)
    unit_rows, inverse = normalize(frames32)
    normed = unit_rows.astype(jnp.bfloat16)
    block_mean = jnp.mean(frames32, axis=0, keepdims=True)
    pool_unit, pool_inv = normalize(block_mean)
    pooled = pool_unit.astype(jnp.bfloat16)
    slots = lax.broadcasted_iota(jnp.int32, (shard_total, 1), 0)
    pooled_all = jnp.where(slots == shard_index, pooled, jnp.zeros_like(pooled))
    for step in range(3):
        shift = 2 * step
        pooled_all = pooled_all + sum(
            lax.ppermute(pooled_all, "tm", [(i, i ^ (d << shift)) for i in range(64)])
            for d in (1, 2, 3)
        )
    owned_mask = (owners == shard_index).astype(jnp.float32)[:, None]
    anchor = summary.astype(jnp.float32) + jnp.take(pooled_all, owners, axis=0).astype(jnp.float32)
    glob_unit, glob_inv = normalize(anchor)
    glob_normed = glob_unit.astype(jnp.bfloat16)
    stacked = jnp.transpose(weights, (1, 0, 2))
    glob_kv = product("gf,kfc->gkc", glob_normed, stacked[1:3]).astype(jnp.bfloat16)
    glob_kv = glob_kv.reshape(glob_count, 2 * local_width)
    qkv = product("tf,kfc->tkc", normed, stacked[:3]).astype(jnp.bfloat16)
    qkv = qkv.reshape(rows_here, 3 * local_width)
    keys_local = qkv[:, local_width : 2 * local_width]
    values_local = qkv[:, 2 * local_width :]
    queries = qkv[:, :local_width].reshape(rows_here, heads_here, HEAD_DIM)
    grad_attended = jnp.dot(cotangent, stacked[3], preferred_element_type=jnp.float32).astype(
        jnp.bfloat16
    )
    grad_attended = grad_attended.reshape(rows_here, heads_here, HEAD_DIM)
    edge = from_behind(qkv[:, local_width:], "tm", 1)
    edge_keys, edge_values = edge[:, :local_width], edge[:, local_width:]
    keys_ext = jnp.concatenate([edge_keys, keys_local], 0).reshape(
        rows_here + WINDOW, heads_here, HEAD_DIM
    )
    values_ext = jnp.concatenate([edge_values, values_local], 0).reshape(
        rows_here + WINDOW, heads_here, HEAD_DIM
    )
    keys_glob = glob_kv[:, :local_width].reshape(glob_count, heads_here, HEAD_DIM)
    values_glob = glob_kv[:, local_width:].reshape(glob_count, heads_here, HEAD_DIM)
    allowed = window_mask(WINDOW, WINDOW, shard_index * rows_here + 0)
    results = block_pass(
        queries, keys_ext, values_ext, keys_glob, values_glob, grad_attended, allowed
    )
    attended = results[0].reshape(rows_here, local_width)
    grad_queries = results[1].reshape(rows_here, local_width)
    grad_kp = results[2].reshape(rows_here + WINDOW, local_width)
    grad_vp = results[3].reshape(rows_here + WINDOW, local_width)
    grad_kg = results[4].reshape(glob_count, local_width)
    grad_vg = results[5].reshape(glob_count, local_width)
    back = from_behind(
        jnp.concatenate([grad_kp[:WINDOW], grad_vp[:WINDOW]], 1).astype(jnp.bfloat16), "tm", -1
    )
    back_keys, back_values = back[:, :local_width], back[:, local_width:]
    grad_keys = grad_kp[WINDOW:].at[rows_here - WINDOW :].add(back_keys.astype(jnp.float32))
    grad_values = grad_vp[WINDOW:].at[rows_here - WINDOW :].add(back_values.astype(jnp.float32))
    grad_cat = jnp.concatenate(
        [grad_queries, grad_keys.astype(jnp.bfloat16), grad_values.astype(jnp.bfloat16)], 1
    )
    glob_grads = jnp.concatenate([grad_kg, grad_vg], 1)
    local_features = jnp.einsum(
        "gkc,kfc->gf",
        glob_grads.reshape(glob_count, 2, local_width),
        stacked[1:3].astype(jnp.float32),
        precision=PRECISE,
    )
    glob_cols = to_positions(glob_normed).astype(jnp.float32)
    inner = lax.dot_general(
        to_positions(normed), grad_cat, (((0,), (0,)), ((), ())), preferred_element_type=jnp.float32
    )
    glob_term = lax.dot_general(glob_cols, glob_grads, (((0,), (0,)), ((), ())), precision=PRECISE)
    inner = inner + jnp.concatenate([jnp.zeros((width, local_width), jnp.float32), glob_term], 1)
    last_term = lax.dot_general(
        to_positions(cotangent), attended, (((0,), (0,)), ((), ())), preferred_element_type=jnp.float32
    )
    weight_parts = jnp.concatenate(
        [inner.reshape(width, 3, local_width), last_term.reshape(width, 1, local_width)], 1
    )
    weight_rows, tm_features = butterfly(
        weight_parts.reshape(width, 4 * local_width), local_features, shard_index
    )
    grad_weights = weight_rows.reshape(width // shard_total, 4, local_width)
    summary_features = tm_features + lax.ppermute(tm_features, "mp", [(0, 1), (1, 0)])
    grad_summary = norm_back(summary_features, glob_unit, glob_inv)
    pool_grads = lax.dot_general(
        owned_mask, grad_summary, (((0,), (0,)), ((), ())), precision=PRECISE
    )
    mean_grads = norm_back(pool_grads, pool_unit, pool_inv) / rows_here
    half_rows = rows_here // mp_total
    start_row = mp_index * half_rows
    other_row = (1 - mp_index) * half_rows
    feature_all = product("tkc,kfc->tf", grad_cat.reshape(rows_here, 3, local_width), stacked[:3])
    mine = lax.dynamic_slice_in_dim(feature_all, start_row, half_rows, 0)
    theirs = lax.dynamic_slice_in_dim(feature_all, other_row, half_rows, 0).astype(jnp.bfloat16)
    received = lax.ppermute(theirs, "mp", [(0, 1), (1, 0)])
    feature_grads = mine + received.astype(jnp.float32)
    my_unit = lax.dynamic_slice_in_dim(unit_rows, start_row, half_rows, 0)
    my_inverse = lax.dynamic_slice_in_dim(inverse, start_row, half_rows, 0)
    my_cotangent = lax.dynamic_slice_in_dim(cotangent, start_row, half_rows, 0).astype(jnp.float32)
    grad_frames = (
        my_cotangent + norm_back(feature_grads, my_unit, my_inverse) + mean_grads
    ).astype(jnp.bfloat16)
    return (grad_frames, grad_weights, grad_summary)


def solution(mesh):
    in_specs = (P("tm", None), P("tm", None), P(None, None, "mp"), P(), P())
    out_specs = (P(("tm", "mp"), None), P("tm", None, "mp"), P())
    return jax.shard_map(shards, mesh=mesh, in_specs=in_specs, out_specs=out_specs, check_vma=False)
```

```python
import numpy as np
import jax
import jax.numpy as jnp
from jax import lax
from jax.sharding import PartitionSpec as P

HEAD_DIM = 64
WINDOW = 512


EPSILON = 1e-05
PRECISE = lax.Precision.HIGHEST


def from_behind(shard, axis, by):
    devices = lax.axis_size(axis)
    pairs = [(i, i + by) for i in range(devices) if 0 <= i + by < devices]
    return lax.ppermute(shard, axis, pairs)


def tm_coords(i):
    return (i >> 4) & 3, (i >> 3) & 1, (i >> 1) & 3, i & 1


def tm_index(x, y_half, z, core):
    return ((x * 2 + y_half) * 4 + z) * 2 + core


def butterfly_plan():
    pairs, bits = [], np.zeros((64, 6), np.int32)
    flips = [("z", 1), ("x", 1), ("z", 2), ("x", 2), ("y", 1)]
    round_pairs = [[(i, i ^ 1) for i in range(64)]]
    for i in range(64):
        bits[i, 0] = i & 1
    for r, (axis, mask) in enumerate(flips):
        these = []
        for i in range(64):
            x, y_half, z, core = tm_coords(i)
            zl, xl = (z + core) % 4, (x + core) % 4
            label = {"z": zl, "x": xl, "y": y_half}[axis]
            bits[i, r + 1] = 1 if label & mask else 0
            if axis == "z":
                z = ((zl ^ mask) - core) % 4
            elif axis == "x":
                x = ((xl ^ mask) - core) % 4
            else:
                y_half ^= 1
            these.append((i, tm_index(x, y_half, z, core)))
        round_pairs.append(these)
    pairs = round_pairs
    return pairs, bits


def to_positions(a):
    rows = a.shape[0]
    r = a.reshape(rows, 4, 2, 4, 2, 16)
    first = r[:, :, :, :, 0, :]
    second = jnp.roll(jnp.roll(r[:, :, :, :, 1, :], 1, axis=1), 1, axis=3)
    g = jnp.stack([first, second], axis=1).reshape(rows, 2, 2, 2, 2, 2, 2, 16)
    g = g.transpose(0, 1, 6, 3, 5, 2, 4, 7)
    return g.reshape(rows, 1024)


def butterfly(parts, glob, shard_index):
    pairs, bits = butterfly_plan()
    my_bits = jnp.asarray(bits)[shard_index]
    for r in range(6):
        half = parts.shape[0] // 2
        b = my_bits[r]
        keep = lax.dynamic_slice_in_dim(parts, b * half, half, 0)
        send = lax.dynamic_slice_in_dim(parts, (1 - b) * half, half, 0)
        if r == 0:
            parts = keep + lax.ppermute(send, "tm", pairs[r])
            continue
        got, got_glob = lax.ppermute((send, glob), "tm", pairs[r])
        parts = keep + got
        glob = glob + got_glob
    glob = glob + lax.ppermute(glob, "tm", pairs[0])
    return parts, glob


def normalize(rows_in):
    inverse = lax.rsqrt(jnp.mean(rows_in * rows_in, axis=-1, keepdims=True) + EPSILON)
    return (rows_in * inverse, inverse)


def norm_back(gradient, unit_rows, inverse):
    return (gradient - unit_rows * jnp.mean(gradient * unit_rows, axis=-1, keepdims=True)) * inverse


def product(form, left, right):
    return jnp.einsum(form, left, right, preferred_element_type=jnp.float32)


def window_mask(row_count, lead, root):
    query_pos = lax.broadcasted_iota(jnp.int32, (row_count, row_count + lead), 0)
    key_pos = lax.broadcasted_iota(jnp.int32, (row_count, row_count + lead), 1)
    inside = (key_pos > query_pos) & (key_pos <= query_pos + lead)
    return inside & (root - lead + key_pos >= 0)


def block_pass(queries, keys_ext, values_ext, keys_glob, values_glob, grad_rows, allowed):
    scaling = HEAD_DIM ** (-0.5)
    near_scores = product("qhe,khe->hqk", queries, keys_ext) * scaling
    far_scores = product("qhe,khe->hqk", queries, keys_glob) * scaling
    near_scores = jnp.where(allowed[None, :, :], near_scores, -jnp.inf)
    row_top = jnp.maximum(
        jnp.max(near_scores, axis=-1, keepdims=True), jnp.max(far_scores, axis=-1, keepdims=True)
    )
    near_exp = jnp.exp(near_scores - row_top)
    far_exp = jnp.exp(far_scores - row_top)
    row_total = jnp.sum(near_exp, axis=-1, keepdims=True) + jnp.sum(far_exp, axis=-1, keepdims=True)
    near_prob = (near_exp / row_total).astype(jnp.bfloat16)
    far_prob = (far_exp / row_total).astype(jnp.bfloat16)
    attended = (
        product("hqk,khe->qhe", near_prob, values_ext)
        + product("hqk,khe->qhe", far_prob, values_glob)
    ).astype(jnp.bfloat16)
    near_dot = product("qhe,khe->hqk", grad_rows, values_ext)
    far_dot = product("qhe,khe->hqk", grad_rows, values_glob)
    near_p32 = near_prob.astype(jnp.float32)
    far_p32 = far_prob.astype(jnp.float32)
    row_delta = jnp.sum(near_p32 * near_dot, axis=-1, keepdims=True) + jnp.sum(
        far_p32 * far_dot, axis=-1, keepdims=True
    )
    near_grad = (near_p32 * (near_dot - row_delta) * scaling).astype(jnp.bfloat16)
    far_grad = (far_p32 * (far_dot - row_delta) * scaling).astype(jnp.bfloat16)
    query_grad = (
        product("hqk,khe->qhe", near_grad, keys_ext) + product("hqk,khe->qhe", far_grad, keys_glob)
    ).astype(jnp.bfloat16)
    key_grad = product("hqk,qhe->khe", near_grad, queries)
    value_grad = product("hqk,qhe->khe", near_prob, grad_rows)
    glob_key_grad = product("hqk,qhe->khe", far_grad, queries)
    glob_value_grad = product("hqk,qhe->khe", far_prob, grad_rows)
    return (attended, query_grad, key_grad, value_grad, glob_key_grad, glob_value_grad)


def shards(frames, cotangent, weights, summary, owners):
    rows_here = frames.shape[0]
    width = frames.shape[1]
    local_width = weights.shape[2]
    heads_here = local_width // HEAD_DIM
    glob_count = summary.shape[0]
    shard_index = lax.axis_index("tm")
    shard_total = lax.axis_size("tm")
    mp_index = lax.axis_index("mp")
    mp_total = lax.axis_size("mp")
    frames32 = frames.astype(jnp.float32)
    unit_rows, inverse = normalize(frames32)
    normed = unit_rows.astype(jnp.bfloat16)
    block_mean = jnp.mean(frames32, axis=0, keepdims=True)
    pool_unit, pool_inv = normalize(block_mean)
    pooled = pool_unit.astype(jnp.bfloat16)
    slots = lax.broadcasted_iota(jnp.int32, (shard_total, 1), 0)
    pooled_all = jnp.where(slots == shard_index, pooled, jnp.zeros_like(pooled))
    for step in range(3):
        shift = 2 * step
        pooled_all = pooled_all + sum(
            lax.ppermute(pooled_all, "tm", [(i, i ^ (d << shift)) for i in range(64)])
            for d in (1, 2, 3)
        )
    owned_mask = (owners == shard_index).astype(jnp.float32)[:, None]
    anchor = summary.astype(jnp.float32) + jnp.take(pooled_all, owners, axis=0).astype(jnp.float32)
    glob_unit, glob_inv = normalize(anchor)
    glob_normed = glob_unit.astype(jnp.bfloat16)
    stacked = jnp.transpose(weights, (1, 0, 2))
    glob_kv = product("gf,kfc->gkc", glob_normed, stacked[1:3]).astype(jnp.bfloat16)
    glob_kv = glob_kv.reshape(glob_count, 2 * local_width)
    qkv = product("tf,kfc->tkc", normed, stacked[:3]).astype(jnp.bfloat16)
    qkv = qkv.reshape(rows_here, 3 * local_width)
    keys_local = qkv[:, local_width : 2 * local_width]
    values_local = qkv[:, 2 * local_width :]
    queries = qkv[:, :local_width].reshape(rows_here, heads_here, HEAD_DIM)
    grad_attended = jnp.dot(cotangent, stacked[3], preferred_element_type=jnp.float32).astype(
        jnp.bfloat16
    )
    grad_attended = grad_attended.reshape(rows_here, heads_here, HEAD_DIM)
    edge = from_behind(qkv[:, local_width:], "tm", 1)
    edge_keys, edge_values = edge[:, :local_width], edge[:, local_width:]
    keys_ext = jnp.concatenate([edge_keys, keys_local], 0).reshape(
        rows_here + WINDOW, heads_here, HEAD_DIM
    )
    values_ext = jnp.concatenate([edge_values, values_local], 0).reshape(
        rows_here + WINDOW, heads_here, HEAD_DIM
    )
    keys_glob = glob_kv[:, :local_width].reshape(glob_count, heads_here, HEAD_DIM)
    values_glob = glob_kv[:, local_width:].reshape(glob_count, heads_here, HEAD_DIM)
    allowed = window_mask(WINDOW, WINDOW, shard_index * rows_here + 0)
    results = block_pass(
        queries, keys_ext, values_ext, keys_glob, values_glob, grad_attended, allowed
    )
    attended = results[0].reshape(rows_here, local_width)
    grad_queries = results[1].reshape(rows_here, local_width)
    grad_kp = results[2].reshape(rows_here + WINDOW, local_width)
    grad_vp = results[3].reshape(rows_here + WINDOW, local_width)
    grad_kg = results[4].reshape(glob_count, local_width)
    grad_vg = results[5].reshape(glob_count, local_width)
    back = from_behind(
        jnp.concatenate([grad_kp[:WINDOW], grad_vp[:WINDOW]], 1).astype(jnp.bfloat16), "tm", -1
    )
    back_keys, back_values = back[:, :local_width], back[:, local_width:]
    grad_keys = grad_kp[WINDOW:].at[rows_here - WINDOW :].add(back_keys.astype(jnp.float32))
    grad_values = grad_vp[WINDOW:].at[rows_here - WINDOW :].add(back_values.astype(jnp.float32))
    grad_cat = jnp.concatenate(
        [grad_queries, grad_keys.astype(jnp.bfloat16), grad_values.astype(jnp.bfloat16)], 1
    )
    glob_grads = jnp.concatenate([grad_kg, grad_vg], 1)
    local_features = jnp.einsum(
        "gkc,kfc->gf",
        glob_grads.reshape(glob_count, 2, local_width),
        stacked[1:3].astype(jnp.float32),
        precision=PRECISE,
    )
    glob_cols = to_positions(glob_normed).astype(jnp.float32)
    inner = lax.dot_general(
        to_positions(normed), grad_cat, (((0,), (0,)), ((), ())), preferred_element_type=jnp.float32
    )
    glob_term = lax.dot_general(glob_cols, glob_grads, (((0,), (0,)), ((), ())), precision=PRECISE)
    inner = inner + jnp.concatenate([jnp.zeros((width, local_width), jnp.float32), glob_term], 1)
    last_term = lax.dot_general(
        to_positions(cotangent), attended, (((0,), (0,)), ((), ())), preferred_element_type=jnp.float32
    )
    weight_parts = jnp.concatenate(
        [inner.reshape(width, 3, local_width), last_term.reshape(width, 1, local_width)], 1
    )
    weight_rows, tm_features = butterfly(
        weight_parts.reshape(width, 4 * local_width), local_features, shard_index
    )
    grad_weights = weight_rows.reshape(width // shard_total, 4, local_width)
    summary_features = tm_features + lax.ppermute(tm_features, "mp", [(0, 1), (1, 0)])
    grad_summary = norm_back(summary_features, glob_unit, glob_inv)
    pool_grads = lax.dot_general(
        owned_mask, grad_summary, (((0,), (0,)), ((), ())), precision=PRECISE
    )
    mean_grads = norm_back(pool_grads, pool_unit, pool_inv) / rows_here
    half_rows = rows_here // mp_total
    start_row = mp_index * half_rows
    other_row = (1 - mp_index) * half_rows
    feature_all = product("tkc,kfc->tf", grad_cat.reshape(rows_here, 3, local_width), stacked[:3])
    mine = lax.dynamic_slice_in_dim(feature_all, start_row, half_rows, 0)
    theirs = lax.dynamic_slice_in_dim(feature_all, other_row, half_rows, 0).astype(jnp.bfloat16)
    received = lax.ppermute(theirs, "mp", [(0, 1), (1, 0)])
    feature_grads = mine + received.astype(jnp.float32)
    my_unit = lax.dynamic_slice_in_dim(unit_rows, start_row, half_rows, 0)
    my_inverse = lax.dynamic_slice_in_dim(inverse, start_row, half_rows, 0)
    my_cotangent = lax.dynamic_slice_in_dim(cotangent, start_row, half_rows, 0).astype(jnp.float32)
    grad_frames = (
        my_cotangent + norm_back(feature_grads, my_unit, my_inverse) + mean_grads
    ).astype(jnp.bfloat16)
    return (grad_frames, grad_weights, grad_summary)


def solution(mesh):
    in_specs = (P("tm", None), P("tm", None), P(None, None, "mp"), P(), P())
    out_specs = (P(("tm", "mp"), None), P("tm", None, "mp"), P())
    return jax.shard_map(shards, mesh=mesh, in_specs=in_specs, out_specs=out_specs, check_vma=False)
```

```python
import numpy as np
import jax
import jax.numpy as jnp
from jax import lax
from jax.sharding import PartitionSpec as P

HEAD_DIM = 64
WINDOW = 512


EPSILON = 1e-05
PRECISE = lax.Precision.HIGHEST


def from_behind(shard, axis, by):
    devices = lax.axis_size(axis)
    pairs = [(i, i + by) for i in range(devices) if 0 <= i + by < devices]
    return lax.ppermute(shard, axis, pairs)


def tm_coords(i):
    return (i >> 4) & 3, (i >> 3) & 1, (i >> 1) & 3, i & 1


def tm_index(x, y_half, z, core):
    return ((x * 2 + y_half) * 4 + z) * 2 + core


def butterfly_plan():
    pairs, bits = [], np.zeros((64, 6), np.int32)
    flips = [("z", 1), ("x", 1), ("z", 2), ("x", 2), ("y", 1)]
    round_pairs = [[(i, i ^ 1) for i in range(64)]]
    for i in range(64):
        bits[i, 0] = i & 1
    for r, (axis, mask) in enumerate(flips):
        these = []
        for i in range(64):
            x, y_half, z, core = tm_coords(i)
            zl, xl = (z + core) % 4, (x + core) % 4
            label = {"z": zl, "x": xl, "y": y_half}[axis]
            bits[i, r + 1] = 1 if label & mask else 0
            if axis == "z":
                z = ((zl ^ mask) - core) % 4
            elif axis == "x":
                x = ((xl ^ mask) - core) % 4
            else:
                y_half ^= 1
            these.append((i, tm_index(x, y_half, z, core)))
        round_pairs.append(these)
    pairs = round_pairs
    return pairs, bits


def to_positions(a):
    rows = a.shape[0]
    r = a.reshape(rows, 4, 2, 4, 2, 16)
    first = r[:, :, :, :, 0, :]
    second = jnp.roll(jnp.roll(r[:, :, :, :, 1, :], 1, axis=1), 1, axis=3)
    g = jnp.stack([first, second], axis=1).reshape(rows, 2, 2, 2, 2, 2, 2, 16)
    g = g.transpose(0, 1, 6, 3, 5, 2, 4, 7)
    return g.reshape(rows, 1024)


GLOB_FLIPS = (1, 2, 16, 4, 32, 8)


def butterfly(parts, glob, shard_index):
    pairs, bits = butterfly_plan()
    my_bits = jnp.asarray(bits)[shard_index]
    for r in range(6):
        half = parts.shape[0] // 2
        b = my_bits[r]
        keep = lax.dynamic_slice_in_dim(parts, b * half, half, 0)
        send = lax.dynamic_slice_in_dim(parts, (1 - b) * half, half, 0)
        parts = keep + lax.ppermute(send, "tm", pairs[r])
        glob = glob + lax.ppermute(glob, "tm", [(i, i ^ GLOB_FLIPS[r]) for i in range(64)])
    return parts, glob


def normalize(rows_in):
    inverse = lax.rsqrt(jnp.mean(rows_in * rows_in, axis=-1, keepdims=True) + EPSILON)
    return (rows_in * inverse, inverse)


def norm_back(gradient, unit_rows, inverse):
    return (gradient - unit_rows * jnp.mean(gradient * unit_rows, axis=-1, keepdims=True)) * inverse


def product(form, left, right):
    return jnp.einsum(form, left, right, preferred_element_type=jnp.float32)


def window_mask(row_count, lead, root):
    query_pos = lax.broadcasted_iota(jnp.int32, (row_count, row_count + lead), 0)
    key_pos = lax.broadcasted_iota(jnp.int32, (row_count, row_count + lead), 1)
    inside = (key_pos > query_pos) & (key_pos <= query_pos + lead)
    return inside & (root - lead + key_pos >= 0)


def block_pass(queries, keys_ext, values_ext, keys_glob, values_glob, grad_rows, allowed):
    scaling = HEAD_DIM ** (-0.5)
    near_scores = product("qhe,khe->hqk", queries, keys_ext) * scaling
    far_scores = product("qhe,khe->hqk", queries, keys_glob) * scaling
    near_scores = jnp.where(allowed[None, :, :], near_scores, -jnp.inf)
    row_top = jnp.maximum(
        jnp.max(near_scores, axis=-1, keepdims=True), jnp.max(far_scores, axis=-1, keepdims=True)
    )
    near_exp = jnp.exp(near_scores - row_top)
    far_exp = jnp.exp(far_scores - row_top)
    row_total = jnp.sum(near_exp, axis=-1, keepdims=True) + jnp.sum(far_exp, axis=-1, keepdims=True)
    near_prob = (near_exp / row_total).astype(jnp.bfloat16)
    far_prob = (far_exp / row_total).astype(jnp.bfloat16)
    attended = (
        product("hqk,khe->qhe", near_prob, values_ext)
        + product("hqk,khe->qhe", far_prob, values_glob)
    ).astype(jnp.bfloat16)
    near_dot = product("qhe,khe->hqk", grad_rows, values_ext)
    far_dot = product("qhe,khe->hqk", grad_rows, values_glob)
    near_p32 = near_prob.astype(jnp.float32)
    far_p32 = far_prob.astype(jnp.float32)
    row_delta = jnp.sum(near_p32 * near_dot, axis=-1, keepdims=True) + jnp.sum(
        far_p32 * far_dot, axis=-1, keepdims=True
    )
    near_grad = (near_p32 * (near_dot - row_delta) * scaling).astype(jnp.bfloat16)
    far_grad = (far_p32 * (far_dot - row_delta) * scaling).astype(jnp.bfloat16)
    query_grad = (
        product("hqk,khe->qhe", near_grad, keys_ext) + product("hqk,khe->qhe", far_grad, keys_glob)
    ).astype(jnp.bfloat16)
    key_grad = product("hqk,qhe->khe", near_grad, queries)
    value_grad = product("hqk,qhe->khe", near_prob, grad_rows)
    glob_key_grad = product("hqk,qhe->khe", far_grad, queries)
    glob_value_grad = product("hqk,qhe->khe", far_prob, grad_rows)
    return (attended, query_grad, key_grad, value_grad, glob_key_grad, glob_value_grad)


def shards(frames, cotangent, weights, summary, owners):
    rows_here = frames.shape[0]
    width = frames.shape[1]
    local_width = weights.shape[2]
    heads_here = local_width // HEAD_DIM
    glob_count = summary.shape[0]
    shard_index = lax.axis_index("tm")
    shard_total = lax.axis_size("tm")
    mp_index = lax.axis_index("mp")
    mp_total = lax.axis_size("mp")
    frames32 = frames.astype(jnp.float32)
    unit_rows, inverse = normalize(frames32)
    normed = unit_rows.astype(jnp.bfloat16)
    block_mean = jnp.mean(frames32, axis=0, keepdims=True)
    pool_unit, pool_inv = normalize(block_mean)
    pooled = pool_unit.astype(jnp.bfloat16)
    slots = lax.broadcasted_iota(jnp.int32, (shard_total, 1), 0)
    pooled_all = jnp.where(slots == shard_index, pooled, jnp.zeros_like(pooled))
    for step in range(3):
        shift = 2 * step
        pooled_all = pooled_all + sum(
            lax.ppermute(pooled_all, "tm", [(i, i ^ (d << shift)) for i in range(64)])
            for d in (1, 2, 3)
        )
    owned_mask = (owners == shard_index).astype(jnp.float32)[:, None]
    anchor = summary.astype(jnp.float32) + jnp.take(pooled_all, owners, axis=0).astype(jnp.float32)
    glob_unit, glob_inv = normalize(anchor)
    glob_normed = glob_unit.astype(jnp.bfloat16)
    stacked = jnp.transpose(weights, (1, 0, 2))
    glob_kv = product("gf,kfc->gkc", glob_normed, stacked[1:3]).astype(jnp.bfloat16)
    glob_kv = glob_kv.reshape(glob_count, 2 * local_width)
    qkv = product("tf,kfc->tkc", normed, stacked[:3]).astype(jnp.bfloat16)
    qkv = qkv.reshape(rows_here, 3 * local_width)
    keys_local = qkv[:, local_width : 2 * local_width]
    values_local = qkv[:, 2 * local_width :]
    queries = qkv[:, :local_width].reshape(rows_here, heads_here, HEAD_DIM)
    grad_attended = jnp.dot(cotangent, stacked[3], preferred_element_type=jnp.float32).astype(
        jnp.bfloat16
    )
    grad_attended = grad_attended.reshape(rows_here, heads_here, HEAD_DIM)
    edge = from_behind(qkv[:, local_width:], "tm", 1)
    edge_keys, edge_values = edge[:, :local_width], edge[:, local_width:]
    keys_ext = jnp.concatenate([edge_keys, keys_local], 0).reshape(
        rows_here + WINDOW, heads_here, HEAD_DIM
    )
    values_ext = jnp.concatenate([edge_values, values_local], 0).reshape(
        rows_here + WINDOW, heads_here, HEAD_DIM
    )
    keys_glob = glob_kv[:, :local_width].reshape(glob_count, heads_here, HEAD_DIM)
    values_glob = glob_kv[:, local_width:].reshape(glob_count, heads_here, HEAD_DIM)
    allowed = window_mask(WINDOW, WINDOW, shard_index * rows_here + 0)
    results = block_pass(
        queries, keys_ext, values_ext, keys_glob, values_glob, grad_attended, allowed
    )
    attended = results[0].reshape(rows_here, local_width)
    grad_queries = results[1].reshape(rows_here, local_width)
    grad_kp = results[2].reshape(rows_here + WINDOW, local_width)
    grad_vp = results[3].reshape(rows_here + WINDOW, local_width)
    grad_kg = results[4].reshape(glob_count, local_width)
    grad_vg = results[5].reshape(glob_count, local_width)
    back = from_behind(
        jnp.concatenate([grad_kp[:WINDOW], grad_vp[:WINDOW]], 1).astype(jnp.bfloat16), "tm", -1
    )
    back_keys, back_values = back[:, :local_width], back[:, local_width:]
    grad_keys = grad_kp[WINDOW:].at[rows_here - WINDOW :].add(back_keys.astype(jnp.float32))
    grad_values = grad_vp[WINDOW:].at[rows_here - WINDOW :].add(back_values.astype(jnp.float32))
    grad_cat = jnp.concatenate(
        [grad_queries, grad_keys.astype(jnp.bfloat16), grad_values.astype(jnp.bfloat16)], 1
    )
    glob_grads = jnp.concatenate([grad_kg, grad_vg], 1)
    local_features = jnp.einsum(
        "gkc,kfc->gf",
        glob_grads.reshape(glob_count, 2, local_width),
        stacked[1:3].astype(jnp.float32),
        precision=PRECISE,
    )
    glob_cols = to_positions(glob_normed).astype(jnp.float32)
    inner = lax.dot_general(
        to_positions(normed), grad_cat, (((0,), (0,)), ((), ())), preferred_element_type=jnp.float32
    )
    glob_term = lax.dot_general(glob_cols, glob_grads, (((0,), (0,)), ((), ())), precision=PRECISE)
    inner = inner + jnp.concatenate([jnp.zeros((width, local_width), jnp.float32), glob_term], 1)
    last_term = lax.dot_general(
        to_positions(cotangent), attended, (((0,), (0,)), ((), ())), preferred_element_type=jnp.float32
    )
    weight_parts = jnp.concatenate(
        [inner.reshape(width, 3, local_width), last_term.reshape(width, 1, local_width)], 1
    )
    weight_rows, tm_features = butterfly(
        weight_parts.reshape(width, 4 * local_width), local_features, shard_index
    )
    grad_weights = weight_rows.reshape(width // shard_total, 4, local_width)
    summary_features = tm_features + lax.ppermute(tm_features, "mp", [(0, 1), (1, 0)])
    grad_summary = norm_back(summary_features, glob_unit, glob_inv)
    pool_grads = lax.dot_general(
        owned_mask, grad_summary, (((0,), (0,)), ((), ())), precision=PRECISE
    )
    mean_grads = norm_back(pool_grads, pool_unit, pool_inv) / rows_here
    half_rows = rows_here // mp_total
    start_row = mp_index * half_rows
    other_row = (1 - mp_index) * half_rows
    feature_all = product("tkc,kfc->tf", grad_cat.reshape(rows_here, 3, local_width), stacked[:3])
    mine = lax.dynamic_slice_in_dim(feature_all, start_row, half_rows, 0)
    theirs = lax.dynamic_slice_in_dim(feature_all, other_row, half_rows, 0).astype(jnp.bfloat16)
    received = lax.ppermute(theirs, "mp", [(0, 1), (1, 0)])
    feature_grads = mine + received.astype(jnp.float32)
    my_unit = lax.dynamic_slice_in_dim(unit_rows, start_row, half_rows, 0)
    my_inverse = lax.dynamic_slice_in_dim(inverse, start_row, half_rows, 0)
    my_cotangent = lax.dynamic_slice_in_dim(cotangent, start_row, half_rows, 0).astype(jnp.float32)
    grad_frames = (
        my_cotangent + norm_back(feature_grads, my_unit, my_inverse) + mean_grads
    ).astype(jnp.bfloat16)
    return (grad_frames, grad_weights, grad_summary)


def solution(mesh):
    in_specs = (P("tm", None), P("tm", None), P(None, None, "mp"), P(), P())
    out_specs = (P(("tm", "mp"), None), P("tm", None, "mp"), P())
    return jax.shard_map(shards, mesh=mesh, in_specs=in_specs, out_specs=out_specs, check_vma=False)
```

```python
import numpy as np
import jax
import jax.numpy as jnp
from jax import lax
from jax.sharding import PartitionSpec as P

HEAD_DIM = 64
WINDOW = 512


EPSILON = 1e-05
PRECISE = lax.Precision.HIGHEST


def from_behind(shard, axis, by):
    devices = lax.axis_size(axis)
    pairs = [(i, i + by) for i in range(devices) if 0 <= i + by < devices]
    return lax.ppermute(shard, axis, pairs)


def tm_coords(i):
    return (i >> 4) & 3, (i >> 3) & 1, (i >> 1) & 3, i & 1


def tm_index(x, y_half, z, core):
    return ((x * 2 + y_half) * 4 + z) * 2 + core


def butterfly_plan():
    pairs, bits = [], np.zeros((64, 6), np.int32)
    flips = [("z", 1), ("x", 1), ("z", 2), ("x", 2), ("y", 1)]
    round_pairs = [[(i, i ^ 1) for i in range(64)]]
    for i in range(64):
        bits[i, 0] = i & 1
    for r, (axis, mask) in enumerate(flips):
        these = []
        for i in range(64):
            x, y_half, z, core = tm_coords(i)
            zl, xl = (z + core) % 4, (x + core) % 4
            label = {"z": zl, "x": xl, "y": y_half}[axis]
            bits[i, r + 1] = 1 if label & mask else 0
            if axis == "z":
                z = ((zl ^ mask) - core) % 4
            elif axis == "x":
                x = ((xl ^ mask) - core) % 4
            else:
                y_half ^= 1
            these.append((i, tm_index(x, y_half, z, core)))
        round_pairs.append(these)
    pairs = round_pairs
    return pairs, bits


def to_positions(a):
    rows = a.shape[0]
    r = a.reshape(rows, 4, 2, 4, 2, 16)
    first = r[:, :, :, :, 0, :]
    second = jnp.roll(jnp.roll(r[:, :, :, :, 1, :], 1, axis=1), 1, axis=3)
    g = jnp.stack([first, second], axis=1).reshape(rows, 2, 2, 2, 2, 2, 2, 16)
    g = g.transpose(0, 1, 6, 3, 5, 2, 4, 7)
    return g.reshape(rows, 1024)


GLOB_FLIPS = (1, 2, 16, 4, 32, 8)


def butterfly(parts, glob, shard_index):
    pairs, bits = butterfly_plan()
    my_bits = jnp.asarray(bits)[shard_index]
    for r in range(6):
        half = parts.shape[0] // 2
        b = my_bits[r]
        keep = lax.dynamic_slice_in_dim(parts, b * half, half, 0)
        send = lax.dynamic_slice_in_dim(parts, (1 - b) * half, half, 0)
        if r in (1, 2):
            got = lax.ppermute(send.astype(jnp.bfloat16), "tm", pairs[r]).astype(jnp.float32)
        else:
            got = lax.ppermute(send, "tm", pairs[r])
        parts = keep + got
        glob = glob + lax.ppermute(glob, "tm", [(i, i ^ GLOB_FLIPS[r]) for i in range(64)])
    return parts, glob


def normalize(rows_in):
    inverse = lax.rsqrt(jnp.mean(rows_in * rows_in, axis=-1, keepdims=True) + EPSILON)
    return (rows_in * inverse, inverse)


def norm_back(gradient, unit_rows, inverse):
    return (gradient - unit_rows * jnp.mean(gradient * unit_rows, axis=-1, keepdims=True)) * inverse


def product(form, left, right):
    return jnp.einsum(form, left, right, preferred_element_type=jnp.float32)


def window_mask(row_count, lead, root):
    query_pos = lax.broadcasted_iota(jnp.int32, (row_count, row_count + lead), 0)
    key_pos = lax.broadcasted_iota(jnp.int32, (row_count, row_count + lead), 1)
    inside = (key_pos > query_pos) & (key_pos <= query_pos + lead)
    return inside & (root - lead + key_pos >= 0)


def block_pass(queries, keys_ext, values_ext, keys_glob, values_glob, grad_rows, allowed):
    scaling = HEAD_DIM ** (-0.5)
    near_scores = product("qhe,khe->hqk", queries, keys_ext) * scaling
    far_scores = product("qhe,khe->hqk", queries, keys_glob) * scaling
    near_scores = jnp.where(allowed[None, :, :], near_scores, -jnp.inf)
    row_top = jnp.maximum(
        jnp.max(near_scores, axis=-1, keepdims=True), jnp.max(far_scores, axis=-1, keepdims=True)
    )
    near_exp = jnp.exp(near_scores - row_top)
    far_exp = jnp.exp(far_scores - row_top)
    row_total = jnp.sum(near_exp, axis=-1, keepdims=True) + jnp.sum(far_exp, axis=-1, keepdims=True)
    near_prob = (near_exp / row_total).astype(jnp.bfloat16)
    far_prob = (far_exp / row_total).astype(jnp.bfloat16)
    attended = (
        product("hqk,khe->qhe", near_prob, values_ext)
        + product("hqk,khe->qhe", far_prob, values_glob)
    ).astype(jnp.bfloat16)
    near_dot = product("qhe,khe->hqk", grad_rows, values_ext)
    far_dot = product("qhe,khe->hqk", grad_rows, values_glob)
    near_p32 = near_prob.astype(jnp.float32)
    far_p32 = far_prob.astype(jnp.float32)
    row_delta = jnp.sum(near_p32 * near_dot, axis=-1, keepdims=True) + jnp.sum(
        far_p32 * far_dot, axis=-1, keepdims=True
    )
    near_grad = (near_p32 * (near_dot - row_delta) * scaling).astype(jnp.bfloat16)
    far_grad = (far_p32 * (far_dot - row_delta) * scaling).astype(jnp.bfloat16)
    query_grad = (
        product("hqk,khe->qhe", near_grad, keys_ext) + product("hqk,khe->qhe", far_grad, keys_glob)
    ).astype(jnp.bfloat16)
    key_grad = product("hqk,qhe->khe", near_grad, queries)
    value_grad = product("hqk,qhe->khe", near_prob, grad_rows)
    glob_key_grad = product("hqk,qhe->khe", far_grad, queries)
    glob_value_grad = product("hqk,qhe->khe", far_prob, grad_rows)
    return (attended, query_grad, key_grad, value_grad, glob_key_grad, glob_value_grad)


def shards(frames, cotangent, weights, summary, owners):
    rows_here = frames.shape[0]
    width = frames.shape[1]
    local_width = weights.shape[2]
    heads_here = local_width // HEAD_DIM
    glob_count = summary.shape[0]
    shard_index = lax.axis_index("tm")
    shard_total = lax.axis_size("tm")
    mp_index = lax.axis_index("mp")
    mp_total = lax.axis_size("mp")
    frames32 = frames.astype(jnp.float32)
    unit_rows, inverse = normalize(frames32)
    normed = unit_rows.astype(jnp.bfloat16)
    block_mean = jnp.mean(frames32, axis=0, keepdims=True)
    pool_unit, pool_inv = normalize(block_mean)
    pooled = pool_unit.astype(jnp.bfloat16)
    slots = lax.broadcasted_iota(jnp.int32, (shard_total, 1), 0)
    pooled_all = jnp.where(slots == shard_index, pooled, jnp.zeros_like(pooled))
    for step in range(3):
        shift = 2 * step
        pooled_all = pooled_all + sum(
            lax.ppermute(pooled_all, "tm", [(i, i ^ (d << shift)) for i in range(64)])
            for d in (1, 2, 3)
        )
    owned_mask = (owners == shard_index).astype(jnp.float32)[:, None]
    anchor = summary.astype(jnp.float32) + jnp.take(pooled_all, owners, axis=0).astype(jnp.float32)
    glob_unit, glob_inv = normalize(anchor)
    glob_normed = glob_unit.astype(jnp.bfloat16)
    stacked = jnp.transpose(weights, (1, 0, 2))
    glob_kv = product("gf,kfc->gkc", glob_normed, stacked[1:3]).astype(jnp.bfloat16)
    glob_kv = glob_kv.reshape(glob_count, 2 * local_width)
    qkv = product("tf,kfc->tkc", normed, stacked[:3]).astype(jnp.bfloat16)
    qkv = qkv.reshape(rows_here, 3 * local_width)
    keys_local = qkv[:, local_width : 2 * local_width]
    values_local = qkv[:, 2 * local_width :]
    queries = qkv[:, :local_width].reshape(rows_here, heads_here, HEAD_DIM)
    grad_attended = jnp.dot(cotangent, stacked[3], preferred_element_type=jnp.float32).astype(
        jnp.bfloat16
    )
    grad_attended = grad_attended.reshape(rows_here, heads_here, HEAD_DIM)
    edge = from_behind(qkv[:, local_width:], "tm", 1)
    edge_keys, edge_values = edge[:, :local_width], edge[:, local_width:]
    keys_ext = jnp.concatenate([edge_keys, keys_local], 0).reshape(
        rows_here + WINDOW, heads_here, HEAD_DIM
    )
    values_ext = jnp.concatenate([edge_values, values_local], 0).reshape(
        rows_here + WINDOW, heads_here, HEAD_DIM
    )
    keys_glob = glob_kv[:, :local_width].reshape(glob_count, heads_here, HEAD_DIM)
    values_glob = glob_kv[:, local_width:].reshape(glob_count, heads_here, HEAD_DIM)
    allowed = window_mask(WINDOW, WINDOW, shard_index * rows_here + 0)
    results = block_pass(
        queries, keys_ext, values_ext, keys_glob, values_glob, grad_attended, allowed
    )
    attended = results[0].reshape(rows_here, local_width)
    grad_queries = results[1].reshape(rows_here, local_width)
    grad_kp = results[2].reshape(rows_here + WINDOW, local_width)
    grad_vp = results[3].reshape(rows_here + WINDOW, local_width)
    grad_kg = results[4].reshape(glob_count, local_width)
    grad_vg = results[5].reshape(glob_count, local_width)
    back = from_behind(
        jnp.concatenate([grad_kp[:WINDOW], grad_vp[:WINDOW]], 1).astype(jnp.bfloat16), "tm", -1
    )
    back_keys, back_values = back[:, :local_width], back[:, local_width:]
    grad_keys = grad_kp[WINDOW:].at[rows_here - WINDOW :].add(back_keys.astype(jnp.float32))
    grad_values = grad_vp[WINDOW:].at[rows_here - WINDOW :].add(back_values.astype(jnp.float32))
    grad_cat = jnp.concatenate(
        [grad_queries, grad_keys.astype(jnp.bfloat16), grad_values.astype(jnp.bfloat16)], 1
    )
    glob_grads = jnp.concatenate([grad_kg, grad_vg], 1)
    local_features = jnp.einsum(
        "gkc,kfc->gf",
        glob_grads.reshape(glob_count, 2, local_width),
        stacked[1:3].astype(jnp.float32),
        precision=PRECISE,
    )
    glob_cols = to_positions(glob_normed).astype(jnp.float32)
    inner = lax.dot_general(
        to_positions(normed), grad_cat, (((0,), (0,)), ((), ())), preferred_element_type=jnp.float32
    )
    glob_term = lax.dot_general(glob_cols, glob_grads, (((0,), (0,)), ((), ())), precision=PRECISE)
    inner = inner + jnp.concatenate([jnp.zeros((width, local_width), jnp.float32), glob_term], 1)
    last_term = lax.dot_general(
        to_positions(cotangent), attended, (((0,), (0,)), ((), ())), preferred_element_type=jnp.float32
    )
    weight_parts = jnp.concatenate(
        [inner.reshape(width, 3, local_width), last_term.reshape(width, 1, local_width)], 1
    )
    weight_rows, tm_features = butterfly(
        weight_parts.reshape(width, 4 * local_width), local_features, shard_index
    )
    grad_weights = weight_rows.reshape(width // shard_total, 4, local_width)
    summary_features = tm_features + lax.ppermute(tm_features, "mp", [(0, 1), (1, 0)])
    grad_summary = norm_back(summary_features, glob_unit, glob_inv)
    pool_grads = lax.dot_general(
        owned_mask, grad_summary, (((0,), (0,)), ((), ())), precision=PRECISE
    )
    mean_grads = norm_back(pool_grads, pool_unit, pool_inv) / rows_here
    half_rows = rows_here // mp_total
    start_row = mp_index * half_rows
    other_row = (1 - mp_index) * half_rows
    feature_all = product("tkc,kfc->tf", grad_cat.reshape(rows_here, 3, local_width), stacked[:3])
    mine = lax.dynamic_slice_in_dim(feature_all, start_row, half_rows, 0)
    theirs = lax.dynamic_slice_in_dim(feature_all, other_row, half_rows, 0).astype(jnp.bfloat16)
    received = lax.ppermute(theirs, "mp", [(0, 1), (1, 0)])
    feature_grads = mine + received.astype(jnp.float32)
    my_unit = lax.dynamic_slice_in_dim(unit_rows, start_row, half_rows, 0)
    my_inverse = lax.dynamic_slice_in_dim(inverse, start_row, half_rows, 0)
    my_cotangent = lax.dynamic_slice_in_dim(cotangent, start_row, half_rows, 0).astype(jnp.float32)
    grad_frames = (
        my_cotangent + norm_back(feature_grads, my_unit, my_inverse) + mean_grads
    ).astype(jnp.bfloat16)
    return (grad_frames, grad_weights, grad_summary)


def solution(mesh):
    in_specs = (P("tm", None), P("tm", None), P(None, None, "mp"), P(), P())
    out_specs = (P(("tm", "mp"), None), P("tm", None, "mp"), P())
    return jax.shard_map(shards, mesh=mesh, in_specs=in_specs, out_specs=out_specs, check_vma=False)
```

```python
import numpy as np
import jax
import jax.numpy as jnp
from jax import lax
from jax.sharding import PartitionSpec as P

HEAD_DIM = 64
WINDOW = 512


EPSILON = 1e-05
PRECISE = lax.Precision.HIGHEST


def from_behind(shard, axis, by):
    devices = lax.axis_size(axis)
    pairs = [(i, i + by) for i in range(devices) if 0 <= i + by < devices]
    return lax.ppermute(shard, axis, pairs)


def tm_coords(i):
    return (i >> 4) & 3, (i >> 3) & 1, (i >> 1) & 3, i & 1


def tm_index(x, y_half, z, core):
    return ((x * 2 + y_half) * 4 + z) * 2 + core


def butterfly_plan():
    pairs, bits = [], np.zeros((64, 6), np.int32)
    flips = [("z", 1), ("x", 1), ("z", 2), ("x", 2), ("y", 1)]
    round_pairs = [[(i, i ^ 1) for i in range(64)]]
    for i in range(64):
        bits[i, 0] = i & 1
    for r, (axis, mask) in enumerate(flips):
        these = []
        for i in range(64):
            x, y_half, z, core = tm_coords(i)
            zl, xl = (z + core) % 4, (x + core) % 4
            label = {"z": zl, "x": xl, "y": y_half}[axis]
            bits[i, r + 1] = 1 if label & mask else 0
            if axis == "z":
                z = ((zl ^ mask) - core) % 4
            elif axis == "x":
                x = ((xl ^ mask) - core) % 4
            else:
                y_half ^= 1
            these.append((i, tm_index(x, y_half, z, core)))
        round_pairs.append(these)
    pairs = round_pairs
    return pairs, bits


def to_positions(a):
    rows = a.shape[0]
    r = a.reshape(rows, 4, 2, 4, 2, 16)
    first = r[:, :, :, :, 0, :]
    second = jnp.roll(jnp.roll(r[:, :, :, :, 1, :], 1, axis=1), 1, axis=3)
    g = jnp.stack([first, second], axis=1).reshape(rows, 2, 2, 2, 2, 2, 2, 16)
    g = g.transpose(0, 1, 6, 3, 5, 2, 4, 7)
    return g.reshape(rows, 1024)


GLOB_FLIPS = (1, 2, 16, 4, 32, 8)


def butterfly(parts, glob, shard_index):
    pairs, bits = butterfly_plan()
    my_bits = jnp.asarray(bits)[shard_index]
    for r in range(6):
        half = parts.shape[0] // 2
        b = my_bits[r]
        keep = lax.dynamic_slice_in_dim(parts, b * half, half, 0)
        send = lax.dynamic_slice_in_dim(parts, (1 - b) * half, half, 0)
        if r < 5:
            got = lax.ppermute(send.astype(jnp.bfloat16), "tm", pairs[r]).astype(jnp.float32)
        else:
            got = lax.ppermute(send, "tm", pairs[r])
        parts = keep + got
        glob = glob + lax.ppermute(glob, "tm", [(i, i ^ GLOB_FLIPS[r]) for i in range(64)])
    return parts, glob


def normalize(rows_in):
    inverse = lax.rsqrt(jnp.mean(rows_in * rows_in, axis=-1, keepdims=True) + EPSILON)
    return (rows_in * inverse, inverse)


def norm_back(gradient, unit_rows, inverse):
    return (gradient - unit_rows * jnp.mean(gradient * unit_rows, axis=-1, keepdims=True)) * inverse


def product(form, left, right):
    return jnp.einsum(form, left, right, preferred_element_type=jnp.float32)


def window_mask(row_count, lead, root):
    query_pos = lax.broadcasted_iota(jnp.int32, (row_count, row_count + lead), 0)
    key_pos = lax.broadcasted_iota(jnp.int32, (row_count, row_count + lead), 1)
    inside = (key_pos > query_pos) & (key_pos <= query_pos + lead)
    return inside & (root - lead + key_pos >= 0)


def block_pass(queries, keys_ext, values_ext, keys_glob, values_glob, grad_rows, allowed):
    scaling = HEAD_DIM ** (-0.5)
    near_scores = product("qhe,khe->hqk", queries, keys_ext) * scaling
    far_scores = product("qhe,khe->hqk", queries, keys_glob) * scaling
    near_scores = jnp.where(allowed[None, :, :], near_scores, -jnp.inf)
    row_top = jnp.maximum(
        jnp.max(near_scores, axis=-1, keepdims=True), jnp.max(far_scores, axis=-1, keepdims=True)
    )
    near_exp = jnp.exp(near_scores - row_top)
    far_exp = jnp.exp(far_scores - row_top)
    row_total = jnp.sum(near_exp, axis=-1, keepdims=True) + jnp.sum(far_exp, axis=-1, keepdims=True)
    near_prob = (near_exp / row_total).astype(jnp.bfloat16)
    far_prob = (far_exp / row_total).astype(jnp.bfloat16)
    attended = (
        product("hqk,khe->qhe", near_prob, values_ext)
        + product("hqk,khe->qhe", far_prob, values_glob)
    ).astype(jnp.bfloat16)
    near_dot = product("qhe,khe->hqk", grad_rows, values_ext)
    far_dot = product("qhe,khe->hqk", grad_rows, values_glob)
    near_p32 = near_prob.astype(jnp.float32)
    far_p32 = far_prob.astype(jnp.float32)
    row_delta = jnp.sum(near_p32 * near_dot, axis=-1, keepdims=True) + jnp.sum(
        far_p32 * far_dot, axis=-1, keepdims=True
    )
    near_grad = (near_p32 * (near_dot - row_delta) * scaling).astype(jnp.bfloat16)
    far_grad = (far_p32 * (far_dot - row_delta) * scaling).astype(jnp.bfloat16)
    query_grad = (
        product("hqk,khe->qhe", near_grad, keys_ext) + product("hqk,khe->qhe", far_grad, keys_glob)
    ).astype(jnp.bfloat16)
    key_grad = product("hqk,qhe->khe", near_grad, queries)
    value_grad = product("hqk,qhe->khe", near_prob, grad_rows)
    glob_key_grad = product("hqk,qhe->khe", far_grad, queries)
    glob_value_grad = product("hqk,qhe->khe", far_prob, grad_rows)
    return (attended, query_grad, key_grad, value_grad, glob_key_grad, glob_value_grad)


def shards(frames, cotangent, weights, summary, owners):
    rows_here = frames.shape[0]
    width = frames.shape[1]
    local_width = weights.shape[2]
    heads_here = local_width // HEAD_DIM
    glob_count = summary.shape[0]
    shard_index = lax.axis_index("tm")
    shard_total = lax.axis_size("tm")
    mp_index = lax.axis_index("mp")
    mp_total = lax.axis_size("mp")
    frames32 = frames.astype(jnp.float32)
    unit_rows, inverse = normalize(frames32)
    normed = unit_rows.astype(jnp.bfloat16)
    block_mean = jnp.mean(frames32, axis=0, keepdims=True)
    pool_unit, pool_inv = normalize(block_mean)
    pooled = pool_unit.astype(jnp.bfloat16)
    slots = lax.broadcasted_iota(jnp.int32, (shard_total, 1), 0)
    pooled_all = jnp.where(slots == shard_index, pooled, jnp.zeros_like(pooled))
    for step in range(3):
        shift = 2 * step
        pooled_all = pooled_all + sum(
            lax.ppermute(pooled_all, "tm", [(i, i ^ (d << shift)) for i in range(64)])
            for d in (1, 2, 3)
        )
    owned_mask = (owners == shard_index).astype(jnp.float32)[:, None]
    anchor = summary.astype(jnp.float32) + jnp.take(pooled_all, owners, axis=0).astype(jnp.float32)
    glob_unit, glob_inv = normalize(anchor)
    glob_normed = glob_unit.astype(jnp.bfloat16)
    stacked = jnp.transpose(weights, (1, 0, 2))
    glob_kv = product("gf,kfc->gkc", glob_normed, stacked[1:3]).astype(jnp.bfloat16)
    glob_kv = glob_kv.reshape(glob_count, 2 * local_width)
    qkv = product("tf,kfc->tkc", normed, stacked[:3]).astype(jnp.bfloat16)
    qkv = qkv.reshape(rows_here, 3 * local_width)
    keys_local = qkv[:, local_width : 2 * local_width]
    values_local = qkv[:, 2 * local_width :]
    queries = qkv[:, :local_width].reshape(rows_here, heads_here, HEAD_DIM)
    grad_attended = jnp.dot(cotangent, stacked[3], preferred_element_type=jnp.float32).astype(
        jnp.bfloat16
    )
    grad_attended = grad_attended.reshape(rows_here, heads_here, HEAD_DIM)
    edge = from_behind(qkv[:, local_width:], "tm", 1)
    edge_keys, edge_values = edge[:, :local_width], edge[:, local_width:]
    keys_ext = jnp.concatenate([edge_keys, keys_local], 0).reshape(
        rows_here + WINDOW, heads_here, HEAD_DIM
    )
    values_ext = jnp.concatenate([edge_values, values_local], 0).reshape(
        rows_here + WINDOW, heads_here, HEAD_DIM
    )
    keys_glob = glob_kv[:, :local_width].reshape(glob_count, heads_here, HEAD_DIM)
    values_glob = glob_kv[:, local_width:].reshape(glob_count, heads_here, HEAD_DIM)
    allowed = window_mask(WINDOW, WINDOW, shard_index * rows_here + 0)
    results = block_pass(
        queries, keys_ext, values_ext, keys_glob, values_glob, grad_attended, allowed
    )
    attended = results[0].reshape(rows_here, local_width)
    grad_queries = results[1].reshape(rows_here, local_width)
    grad_kp = results[2].reshape(rows_here + WINDOW, local_width)
    grad_vp = results[3].reshape(rows_here + WINDOW, local_width)
    grad_kg = results[4].reshape(glob_count, local_width)
    grad_vg = results[5].reshape(glob_count, local_width)
    back = from_behind(
        jnp.concatenate([grad_kp[:WINDOW], grad_vp[:WINDOW]], 1).astype(jnp.bfloat16), "tm", -1
    )
    back_keys, back_values = back[:, :local_width], back[:, local_width:]
    grad_keys = grad_kp[WINDOW:].at[rows_here - WINDOW :].add(back_keys.astype(jnp.float32))
    grad_values = grad_vp[WINDOW:].at[rows_here - WINDOW :].add(back_values.astype(jnp.float32))
    grad_cat = jnp.concatenate(
        [grad_queries, grad_keys.astype(jnp.bfloat16), grad_values.astype(jnp.bfloat16)], 1
    )
    glob_grads = jnp.concatenate([grad_kg, grad_vg], 1)
    local_features = jnp.einsum(
        "gkc,kfc->gf",
        glob_grads.reshape(glob_count, 2, local_width),
        stacked[1:3].astype(jnp.float32),
        precision=PRECISE,
    )
    glob_cols = to_positions(glob_normed).astype(jnp.float32)
    inner = lax.dot_general(
        to_positions(normed), grad_cat, (((0,), (0,)), ((), ())), preferred_element_type=jnp.float32
    )
    glob_term = lax.dot_general(glob_cols, glob_grads, (((0,), (0,)), ((), ())), precision=PRECISE)
    inner = inner + jnp.concatenate([jnp.zeros((width, local_width), jnp.float32), glob_term], 1)
    last_term = lax.dot_general(
        to_positions(cotangent), attended, (((0,), (0,)), ((), ())), preferred_element_type=jnp.float32
    )
    weight_parts = jnp.concatenate(
        [inner.reshape(width, 3, local_width), last_term.reshape(width, 1, local_width)], 1
    )
    weight_rows, tm_features = butterfly(
        weight_parts.reshape(width, 4 * local_width), local_features, shard_index
    )
    grad_weights = weight_rows.reshape(width // shard_total, 4, local_width)
    summary_features = tm_features + lax.ppermute(tm_features, "mp", [(0, 1), (1, 0)])
    grad_summary = norm_back(summary_features, glob_unit, glob_inv)
    pool_grads = lax.dot_general(
        owned_mask, grad_summary, (((0,), (0,)), ((), ())), precision=PRECISE
    )
    mean_grads = norm_back(pool_grads, pool_unit, pool_inv) / rows_here
    half_rows = rows_here // mp_total
    start_row = mp_index * half_rows
    other_row = (1 - mp_index) * half_rows
    feature_all = product("tkc,kfc->tf", grad_cat.reshape(rows_here, 3, local_width), stacked[:3])
    mine = lax.dynamic_slice_in_dim(feature_all, start_row, half_rows, 0)
    theirs = lax.dynamic_slice_in_dim(feature_all, other_row, half_rows, 0).astype(jnp.bfloat16)
    received = lax.ppermute(theirs, "mp", [(0, 1), (1, 0)])
    feature_grads = mine + received.astype(jnp.float32)
    my_unit = lax.dynamic_slice_in_dim(unit_rows, start_row, half_rows, 0)
    my_inverse = lax.dynamic_slice_in_dim(inverse, start_row, half_rows, 0)
    my_cotangent = lax.dynamic_slice_in_dim(cotangent, start_row, half_rows, 0).astype(jnp.float32)
    grad_frames = (
        my_cotangent + norm_back(feature_grads, my_unit, my_inverse) + mean_grads
    ).astype(jnp.bfloat16)
    return (grad_frames, grad_weights, grad_summary)


def solution(mesh):
    in_specs = (P("tm", None), P("tm", None), P(None, None, "mp"), P(), P())
    out_specs = (P(("tm", "mp"), None), P("tm", None, "mp"), P())
    return jax.shard_map(shards, mesh=mesh, in_specs=in_specs, out_specs=out_specs, check_vma=False)
```

```python
import numpy as np
import jax
import jax.numpy as jnp
from jax import lax
from jax.sharding import PartitionSpec as P

HEAD_DIM = 64
WINDOW = 512


EPSILON = 1e-05
PRECISE = lax.Precision.HIGHEST


def from_behind(shard, axis, by):
    devices = lax.axis_size(axis)
    pairs = [(i, i + by) for i in range(devices) if 0 <= i + by < devices]
    return lax.ppermute(shard, axis, pairs)


def tm_coords(i):
    return (i >> 4) & 3, (i >> 3) & 1, (i >> 1) & 3, i & 1


def tm_index(x, y_half, z, core):
    return ((x * 2 + y_half) * 4 + z) * 2 + core


def butterfly_plan():
    pairs, bits = [], np.zeros((64, 6), np.int32)
    flips = [("z", 1), ("x", 1), ("z", 2), ("x", 2), ("y", 1)]
    round_pairs = [[(i, i ^ 1) for i in range(64)]]
    for i in range(64):
        bits[i, 0] = i & 1
    for r, (axis, mask) in enumerate(flips):
        these = []
        for i in range(64):
            x, y_half, z, core = tm_coords(i)
            zl, xl = (z + core) % 4, (x + core) % 4
            label = {"z": zl, "x": xl, "y": y_half}[axis]
            bits[i, r + 1] = 1 if label & mask else 0
            if axis == "z":
                z = ((zl ^ mask) - core) % 4
            elif axis == "x":
                x = ((xl ^ mask) - core) % 4
            else:
                y_half ^= 1
            these.append((i, tm_index(x, y_half, z, core)))
        round_pairs.append(these)
    pairs = round_pairs
    return pairs, bits


def to_positions(a):
    rows = a.shape[0]
    r = a.reshape(rows, 4, 2, 4, 2, 16)
    first = r[:, :, :, :, 0, :]
    second = jnp.roll(jnp.roll(r[:, :, :, :, 1, :], 1, axis=1), 1, axis=3)
    g = jnp.stack([first, second], axis=1).reshape(rows, 2, 2, 2, 2, 2, 2, 16)
    g = g.transpose(0, 1, 6, 3, 5, 2, 4, 7)
    return g.reshape(rows, 1024)


GLOB_FLIPS = (1, 2, 16, 4, 32, 8)


def butterfly(parts, glob, shard_index):
    pairs, bits = butterfly_plan()
    my_bits = jnp.asarray(bits)[shard_index]
    for r in range(6):
        half = parts.shape[0] // 2
        b = my_bits[r]
        keep = lax.dynamic_slice_in_dim(parts, b * half, half, 0)
        send = lax.dynamic_slice_in_dim(parts, (1 - b) * half, half, 0)
        if r < 3:
            got = lax.ppermute(send.astype(jnp.bfloat16), "tm", pairs[r]).astype(jnp.float32)
        else:
            got = lax.ppermute(send, "tm", pairs[r])
        parts = keep + got
        glob = glob + lax.ppermute(glob, "tm", [(i, i ^ GLOB_FLIPS[r]) for i in range(64)])
    return parts, glob


def normalize(rows_in):
    inverse = lax.rsqrt(jnp.mean(rows_in * rows_in, axis=-1, keepdims=True) + EPSILON)
    return (rows_in * inverse, inverse)


def norm_back(gradient, unit_rows, inverse):
    return (gradient - unit_rows * jnp.mean(gradient * unit_rows, axis=-1, keepdims=True)) * inverse


def product(form, left, right):
    return jnp.einsum(form, left, right, preferred_element_type=jnp.float32)


def window_mask(row_count, lead, root):
    query_pos = lax.broadcasted_iota(jnp.int32, (row_count, row_count + lead), 0)
    key_pos = lax.broadcasted_iota(jnp.int32, (row_count, row_count + lead), 1)
    inside = (key_pos > query_pos) & (key_pos <= query_pos + lead)
    return inside & (root - lead + key_pos >= 0)


def block_pass(queries, keys_ext, values_ext, keys_glob, values_glob, grad_rows, allowed):
    scaling = HEAD_DIM ** (-0.5)
    near_scores = product("qhe,khe->hqk", queries, keys_ext) * scaling
    far_scores = product("qhe,khe->hqk", queries, keys_glob) * scaling
    near_scores = jnp.where(allowed[None, :, :], near_scores, -jnp.inf)
    row_top = jnp.maximum(
        jnp.max(near_scores, axis=-1, keepdims=True), jnp.max(far_scores, axis=-1, keepdims=True)
    )
    near_exp = jnp.exp(near_scores - row_top)
    far_exp = jnp.exp(far_scores - row_top)
    row_total = jnp.sum(near_exp, axis=-1, keepdims=True) + jnp.sum(far_exp, axis=-1, keepdims=True)
    near_prob = (near_exp / row_total).astype(jnp.bfloat16)
    far_prob = (far_exp / row_total).astype(jnp.bfloat16)
    attended = (
        product("hqk,khe->qhe", near_prob, values_ext)
        + product("hqk,khe->qhe", far_prob, values_glob)
    ).astype(jnp.bfloat16)
    near_dot = product("qhe,khe->hqk", grad_rows, values_ext)
    far_dot = product("qhe,khe->hqk", grad_rows, values_glob)
    near_p32 = near_prob.astype(jnp.float32)
    far_p32 = far_prob.astype(jnp.float32)
    row_delta = jnp.sum(near_p32 * near_dot, axis=-1, keepdims=True) + jnp.sum(
        far_p32 * far_dot, axis=-1, keepdims=True
    )
    near_grad = (near_p32 * (near_dot - row_delta) * scaling).astype(jnp.bfloat16)
    far_grad = (far_p32 * (far_dot - row_delta) * scaling).astype(jnp.bfloat16)
    query_grad = (
        product("hqk,khe->qhe", near_grad, keys_ext) + product("hqk,khe->qhe", far_grad, keys_glob)
    ).astype(jnp.bfloat16)
    key_grad = product("hqk,qhe->khe", near_grad, queries)
    value_grad = product("hqk,qhe->khe", near_prob, grad_rows)
    glob_key_grad = product("hqk,qhe->khe", far_grad, queries)
    glob_value_grad = product("hqk,qhe->khe", far_prob, grad_rows)
    return (attended, query_grad, key_grad, value_grad, glob_key_grad, glob_value_grad)


def shards(frames, cotangent, weights, summary, owners):
    rows_here = frames.shape[0]
    width = frames.shape[1]
    local_width = weights.shape[2]
    heads_here = local_width // HEAD_DIM
    glob_count = summary.shape[0]
    shard_index = lax.axis_index("tm")
    shard_total = lax.axis_size("tm")
    mp_index = lax.axis_index("mp")
    mp_total = lax.axis_size("mp")
    frames32 = frames.astype(jnp.float32)
    unit_rows, inverse = normalize(frames32)
    normed = unit_rows.astype(jnp.bfloat16)
    block_mean = jnp.mean(frames32, axis=0, keepdims=True)
    pool_unit, pool_inv = normalize(block_mean)
    pooled = pool_unit.astype(jnp.bfloat16)
    slots = lax.broadcasted_iota(jnp.int32, (shard_total, 1), 0)
    pooled_all = jnp.where(slots == shard_index, pooled, jnp.zeros_like(pooled))
    for step in range(3):
        shift = 2 * step
        pooled_all = pooled_all + sum(
            lax.ppermute(pooled_all, "tm", [(i, i ^ (d << shift)) for i in range(64)])
            for d in (1, 2, 3)
        )
    owned_mask = (owners == shard_index).astype(jnp.float32)[:, None]
    anchor = summary.astype(jnp.float32) + jnp.take(pooled_all, owners, axis=0).astype(jnp.float32)
    glob_unit, glob_inv = normalize(anchor)
    glob_normed = glob_unit.astype(jnp.bfloat16)
    stacked = jnp.transpose(weights, (1, 0, 2))
    glob_kv = product("gf,kfc->gkc", glob_normed, stacked[1:3]).astype(jnp.bfloat16)
    glob_kv = glob_kv.reshape(glob_count, 2 * local_width)
    qkv = product("tf,kfc->tkc", normed, stacked[:3]).astype(jnp.bfloat16)
    qkv = qkv.reshape(rows_here, 3 * local_width)
    keys_local = qkv[:, local_width : 2 * local_width]
    values_local = qkv[:, 2 * local_width :]
    queries = qkv[:, :local_width].reshape(rows_here, heads_here, HEAD_DIM)
    grad_attended = jnp.dot(cotangent, stacked[3], preferred_element_type=jnp.float32).astype(
        jnp.bfloat16
    )
    grad_attended = grad_attended.reshape(rows_here, heads_here, HEAD_DIM)
    edge = from_behind(qkv[:, local_width:], "tm", 1)
    edge_keys, edge_values = edge[:, :local_width], edge[:, local_width:]
    keys_ext = jnp.concatenate([edge_keys, keys_local], 0).reshape(
        rows_here + WINDOW, heads_here, HEAD_DIM
    )
    values_ext = jnp.concatenate([edge_values, values_local], 0).reshape(
        rows_here + WINDOW, heads_here, HEAD_DIM
    )
    keys_glob = glob_kv[:, :local_width].reshape(glob_count, heads_here, HEAD_DIM)
    values_glob = glob_kv[:, local_width:].reshape(glob_count, heads_here, HEAD_DIM)
    allowed = window_mask(WINDOW, WINDOW, shard_index * rows_here + 0)
    results = block_pass(
        queries, keys_ext, values_ext, keys_glob, values_glob, grad_attended, allowed
    )
    attended = results[0].reshape(rows_here, local_width)
    grad_queries = results[1].reshape(rows_here, local_width)
    grad_kp = results[2].reshape(rows_here + WINDOW, local_width)
    grad_vp = results[3].reshape(rows_here + WINDOW, local_width)
    grad_kg = results[4].reshape(glob_count, local_width)
    grad_vg = results[5].reshape(glob_count, local_width)
    back = from_behind(
        jnp.concatenate([grad_kp[:WINDOW], grad_vp[:WINDOW]], 1).astype(jnp.bfloat16), "tm", -1
    )
    back_keys, back_values = back[:, :local_width], back[:, local_width:]
    grad_keys = grad_kp[WINDOW:].at[rows_here - WINDOW :].add(back_keys.astype(jnp.float32))
    grad_values = grad_vp[WINDOW:].at[rows_here - WINDOW :].add(back_values.astype(jnp.float32))
    grad_cat = jnp.concatenate(
        [grad_queries, grad_keys.astype(jnp.bfloat16), grad_values.astype(jnp.bfloat16)], 1
    )
    glob_grads = jnp.concatenate([grad_kg, grad_vg], 1)
    local_features = jnp.einsum(
        "gkc,kfc->gf",
        glob_grads.reshape(glob_count, 2, local_width),
        stacked[1:3].astype(jnp.float32),
        precision=PRECISE,
    )
    glob_cols = to_positions(glob_normed).astype(jnp.float32)
    inner = lax.dot_general(
        to_positions(normed), grad_cat, (((0,), (0,)), ((), ())), preferred_element_type=jnp.float32
    )
    glob_term = lax.dot_general(glob_cols, glob_grads, (((0,), (0,)), ((), ())), precision=PRECISE)
    inner = inner + jnp.concatenate([jnp.zeros((width, local_width), jnp.float32), glob_term], 1)
    last_term = lax.dot_general(
        to_positions(cotangent), attended, (((0,), (0,)), ((), ())), preferred_element_type=jnp.float32
    )
    weight_parts = jnp.concatenate(
        [inner.reshape(width, 3, local_width), last_term.reshape(width, 1, local_width)], 1
    )
    weight_rows, tm_features = butterfly(
        weight_parts.reshape(width, 4 * local_width), local_features, shard_index
    )
    grad_weights = weight_rows.reshape(width // shard_total, 4, local_width)
    summary_features = tm_features + lax.ppermute(tm_features, "mp", [(0, 1), (1, 0)])
    grad_summary = norm_back(summary_features, glob_unit, glob_inv)
    pool_grads = lax.dot_general(
        owned_mask, grad_summary, (((0,), (0,)), ((), ())), precision=PRECISE
    )
    mean_grads = norm_back(pool_grads, pool_unit, pool_inv) / rows_here
    half_rows = rows_here // mp_total
    start_row = mp_index * half_rows
    other_row = (1 - mp_index) * half_rows
    feature_all = product("tkc,kfc->tf", grad_cat.reshape(rows_here, 3, local_width), stacked[:3])
    mine = lax.dynamic_slice_in_dim(feature_all, start_row, half_rows, 0)
    theirs = lax.dynamic_slice_in_dim(feature_all, other_row, half_rows, 0).astype(jnp.bfloat16)
    received = lax.ppermute(theirs, "mp", [(0, 1), (1, 0)])
    feature_grads = mine + received.astype(jnp.float32)
    my_unit = lax.dynamic_slice_in_dim(unit_rows, start_row, half_rows, 0)
    my_inverse = lax.dynamic_slice_in_dim(inverse, start_row, half_rows, 0)
    my_cotangent = lax.dynamic_slice_in_dim(cotangent, start_row, half_rows, 0).astype(jnp.float32)
    grad_frames = (
        my_cotangent + norm_back(feature_grads, my_unit, my_inverse) + mean_grads
    ).astype(jnp.bfloat16)
    return (grad_frames, grad_weights, grad_summary)


def solution(mesh):
    in_specs = (P("tm", None), P("tm", None), P(None, None, "mp"), P(), P())
    out_specs = (P(("tm", "mp"), None), P("tm", None, "mp"), P())
    return jax.shard_map(shards, mesh=mesh, in_specs=in_specs, out_specs=out_specs, check_vma=False)
```

```python
import numpy as np
import jax
import jax.numpy as jnp
from jax import lax
from jax.sharding import PartitionSpec as P

HEAD_DIM = 64
WINDOW = 512


EPSILON = 1e-05
PRECISE = lax.Precision.HIGHEST


def from_behind(shard, axis, by):
    devices = lax.axis_size(axis)
    pairs = [(i, i + by) for i in range(devices) if 0 <= i + by < devices]
    return lax.ppermute(shard, axis, pairs)


def tm_coords(i):
    return (i >> 4) & 3, (i >> 3) & 1, (i >> 1) & 3, i & 1


def tm_index(x, y_half, z, core):
    return ((x * 2 + y_half) * 4 + z) * 2 + core


def butterfly_plan():
    pairs, bits = [], np.zeros((64, 6), np.int32)
    flips = [("z", 1), ("x", 1), ("z", 2), ("x", 2), ("y", 1)]
    round_pairs = [[(i, i ^ 1) for i in range(64)]]
    for i in range(64):
        bits[i, 0] = i & 1
    for r, (axis, mask) in enumerate(flips):
        these = []
        for i in range(64):
            x, y_half, z, core = tm_coords(i)
            zl, xl = (z + core) % 4, (x + core) % 4
            label = {"z": zl, "x": xl, "y": y_half}[axis]
            bits[i, r + 1] = 1 if label & mask else 0
            if axis == "z":
                z = ((zl ^ mask) - core) % 4
            elif axis == "x":
                x = ((xl ^ mask) - core) % 4
            else:
                y_half ^= 1
            these.append((i, tm_index(x, y_half, z, core)))
        round_pairs.append(these)
    pairs = round_pairs
    return pairs, bits


def to_positions(a):
    rows = a.shape[0]
    r = a.reshape(rows, 4, 2, 4, 2, 16)
    first = r[:, :, :, :, 0, :]
    second = jnp.roll(jnp.roll(r[:, :, :, :, 1, :], 1, axis=1), 1, axis=3)
    g = jnp.stack([first, second], axis=1).reshape(rows, 2, 2, 2, 2, 2, 2, 16)
    g = g.transpose(0, 1, 6, 3, 5, 2, 4, 7)
    return g.reshape(rows, 1024)


GLOB_FLIPS = (1, 2, 16, 4, 32, 8)


def butterfly(parts, glob, shard_index):
    pairs, bits = butterfly_plan()
    my_bits = jnp.asarray(bits)[shard_index]
    for r in range(6):
        half = parts.shape[0] // 2
        b = my_bits[r]
        keep = lax.dynamic_slice_in_dim(parts, b * half, half, 0)
        send = lax.dynamic_slice_in_dim(parts, (1 - b) * half, half, 0)
        if r in (1, 2):
            got = lax.ppermute(send.astype(jnp.bfloat16), "tm", pairs[r]).astype(jnp.float32)
        else:
            got = lax.ppermute(send, "tm", pairs[r])
        parts = keep + got
        sent_glob = lax.ppermute(
            glob.astype(jnp.bfloat16), "tm", [(i, i ^ GLOB_FLIPS[r]) for i in range(64)]
        )
        glob = glob.astype(jnp.bfloat16).astype(jnp.float32) + sent_glob.astype(jnp.float32)
    return parts, glob


def normalize(rows_in):
    inverse = lax.rsqrt(jnp.mean(rows_in * rows_in, axis=-1, keepdims=True) + EPSILON)
    return (rows_in * inverse, inverse)


def norm_back(gradient, unit_rows, inverse):
    return (gradient - unit_rows * jnp.mean(gradient * unit_rows, axis=-1, keepdims=True)) * inverse


def product(form, left, right):
    return jnp.einsum(form, left, right, preferred_element_type=jnp.float32)


def window_mask(row_count, lead, root):
    query_pos = lax.broadcasted_iota(jnp.int32, (row_count, row_count + lead), 0)
    key_pos = lax.broadcasted_iota(jnp.int32, (row_count, row_count + lead), 1)
    inside = (key_pos > query_pos) & (key_pos <= query_pos + lead)
    return inside & (root - lead + key_pos >= 0)


def block_pass(queries, keys_ext, values_ext, keys_glob, values_glob, grad_rows, allowed):
    scaling = HEAD_DIM ** (-0.5)
    near_scores = product("qhe,khe->hqk", queries, keys_ext) * scaling
    far_scores = product("qhe,khe->hqk", queries, keys_glob) * scaling
    near_scores = jnp.where(allowed[None, :, :], near_scores, -jnp.inf)
    row_top = jnp.maximum(
        jnp.max(near_scores, axis=-1, keepdims=True), jnp.max(far_scores, axis=-1, keepdims=True)
    )
    near_exp = jnp.exp(near_scores - row_top)
    far_exp = jnp.exp(far_scores - row_top)
    row_total = jnp.sum(near_exp, axis=-1, keepdims=True) + jnp.sum(far_exp, axis=-1, keepdims=True)
    near_prob = (near_exp / row_total).astype(jnp.bfloat16)
    far_prob = (far_exp / row_total).astype(jnp.bfloat16)
    attended = (
        product("hqk,khe->qhe", near_prob, values_ext)
        + product("hqk,khe->qhe", far_prob, values_glob)
    ).astype(jnp.bfloat16)
    near_dot = product("qhe,khe->hqk", grad_rows, values_ext)
    far_dot = product("qhe,khe->hqk", grad_rows, values_glob)
    near_p32 = near_prob.astype(jnp.float32)
    far_p32 = far_prob.astype(jnp.float32)
    row_delta = jnp.sum(near_p32 * near_dot, axis=-1, keepdims=True) + jnp.sum(
        far_p32 * far_dot, axis=-1, keepdims=True
    )
    near_grad = (near_p32 * (near_dot - row_delta) * scaling).astype(jnp.bfloat16)
    far_grad = (far_p32 * (far_dot - row_delta) * scaling).astype(jnp.bfloat16)
    query_grad = (
        product("hqk,khe->qhe", near_grad, keys_ext) + product("hqk,khe->qhe", far_grad, keys_glob)
    ).astype(jnp.bfloat16)
    key_grad = product("hqk,qhe->khe", near_grad, queries)
    value_grad = product("hqk,qhe->khe", near_prob, grad_rows)
    glob_key_grad = product("hqk,qhe->khe", far_grad, queries)
    glob_value_grad = product("hqk,qhe->khe", far_prob, grad_rows)
    return (attended, query_grad, key_grad, value_grad, glob_key_grad, glob_value_grad)


def shards(frames, cotangent, weights, summary, owners):
    rows_here = frames.shape[0]
    width = frames.shape[1]
    local_width = weights.shape[2]
    heads_here = local_width // HEAD_DIM
    glob_count = summary.shape[0]
    shard_index = lax.axis_index("tm")
    shard_total = lax.axis_size("tm")
    mp_index = lax.axis_index("mp")
    mp_total = lax.axis_size("mp")
    frames32 = frames.astype(jnp.float32)
    unit_rows, inverse = normalize(frames32)
    normed = unit_rows.astype(jnp.bfloat16)
    block_mean = jnp.mean(frames32, axis=0, keepdims=True)
    pool_unit, pool_inv = normalize(block_mean)
    pooled = pool_unit.astype(jnp.bfloat16)
    slots = lax.broadcasted_iota(jnp.int32, (shard_total, 1), 0)
    pooled_all = jnp.where(slots == shard_index, pooled, jnp.zeros_like(pooled))
    for step in range(3):
        shift = 2 * step
        pooled_all = pooled_all + sum(
            lax.ppermute(pooled_all, "tm", [(i, i ^ (d << shift)) for i in range(64)])
            for d in (1, 2, 3)
        )
    owned_mask = (owners == shard_index).astype(jnp.float32)[:, None]
    anchor = summary.astype(jnp.float32) + jnp.take(pooled_all, owners, axis=0).astype(jnp.float32)
    glob_unit, glob_inv = normalize(anchor)
    glob_normed = glob_unit.astype(jnp.bfloat16)
    stacked = jnp.transpose(weights, (1, 0, 2))
    glob_kv = product("gf,kfc->gkc", glob_normed, stacked[1:3]).astype(jnp.bfloat16)
    glob_kv = glob_kv.reshape(glob_count, 2 * local_width)
    qkv = product("tf,kfc->tkc", normed, stacked[:3]).astype(jnp.bfloat16)
    qkv = qkv.reshape(rows_here, 3 * local_width)
    keys_local = qkv[:, local_width : 2 * local_width]
    values_local = qkv[:, 2 * local_width :]
    queries = qkv[:, :local_width].reshape(rows_here, heads_here, HEAD_DIM)
    grad_attended = jnp.dot(cotangent, stacked[3], preferred_element_type=jnp.float32).astype(
        jnp.bfloat16
    )
    grad_attended = grad_attended.reshape(rows_here, heads_here, HEAD_DIM)
    edge = from_behind(qkv[:, local_width:], "tm", 1)
    edge_keys, edge_values = edge[:, :local_width], edge[:, local_width:]
    keys_ext = jnp.concatenate([edge_keys, keys_local], 0).reshape(
        rows_here + WINDOW, heads_here, HEAD_DIM
    )
    values_ext = jnp.concatenate([edge_values, values_local], 0).reshape(
        rows_here + WINDOW, heads_here, HEAD_DIM
    )
    keys_glob = glob_kv[:, :local_width].reshape(glob_count, heads_here, HEAD_DIM)
    values_glob = glob_kv[:, local_width:].reshape(glob_count, heads_here, HEAD_DIM)
    allowed = window_mask(WINDOW, WINDOW, shard_index * rows_here + 0)
    results = block_pass(
        queries, keys_ext, values_ext, keys_glob, values_glob, grad_attended, allowed
    )
    attended = results[0].reshape(rows_here, local_width)
    grad_queries = results[1].reshape(rows_here, local_width)
    grad_kp = results[2].reshape(rows_here + WINDOW, local_width)
    grad_vp = results[3].reshape(rows_here + WINDOW, local_width)
    grad_kg = results[4].reshape(glob_count, local_width)
    grad_vg = results[5].reshape(glob_count, local_width)
    back = from_behind(
        jnp.concatenate([grad_kp[:WINDOW], grad_vp[:WINDOW]], 1).astype(jnp.bfloat16), "tm", -1
    )
    back_keys, back_values = back[:, :local_width], back[:, local_width:]
    grad_keys = grad_kp[WINDOW:].at[rows_here - WINDOW :].add(back_keys.astype(jnp.float32))
    grad_values = grad_vp[WINDOW:].at[rows_here - WINDOW :].add(back_values.astype(jnp.float32))
    grad_cat = jnp.concatenate(
        [grad_queries, grad_keys.astype(jnp.bfloat16), grad_values.astype(jnp.bfloat16)], 1
    )
    glob_grads = jnp.concatenate([grad_kg, grad_vg], 1)
    local_features = jnp.einsum(
        "gkc,kfc->gf",
        glob_grads.reshape(glob_count, 2, local_width),
        stacked[1:3].astype(jnp.float32),
        precision=PRECISE,
    )
    glob_cols = to_positions(glob_normed).astype(jnp.float32)
    inner = lax.dot_general(
        to_positions(normed), grad_cat, (((0,), (0,)), ((), ())), preferred_element_type=jnp.float32
    )
    glob_term = lax.dot_general(glob_cols, glob_grads, (((0,), (0,)), ((), ())), precision=PRECISE)
    inner = inner + jnp.concatenate([jnp.zeros((width, local_width), jnp.float32), glob_term], 1)
    last_term = lax.dot_general(
        to_positions(cotangent), attended, (((0,), (0,)), ((), ())), preferred_element_type=jnp.float32
    )
    weight_parts = jnp.concatenate(
        [inner.reshape(width, 3, local_width), last_term.reshape(width, 1, local_width)], 1
    )
    weight_rows, tm_features = butterfly(
        weight_parts.reshape(width, 4 * local_width), local_features, shard_index
    )
    grad_weights = weight_rows.reshape(width // shard_total, 4, local_width)
    summary_features = tm_features + lax.ppermute(tm_features, "mp", [(0, 1), (1, 0)])
    grad_summary = norm_back(summary_features, glob_unit, glob_inv)
    pool_grads = lax.dot_general(
        owned_mask, grad_summary, (((0,), (0,)), ((), ())), precision=PRECISE
    )
    mean_grads = norm_back(pool_grads, pool_unit, pool_inv) / rows_here
    half_rows = rows_here // mp_total
    start_row = mp_index * half_rows
    other_row = (1 - mp_index) * half_rows
    feature_all = product("tkc,kfc->tf", grad_cat.reshape(rows_here, 3, local_width), stacked[:3])
    mine = lax.dynamic_slice_in_dim(feature_all, start_row, half_rows, 0)
    theirs = lax.dynamic_slice_in_dim(feature_all, other_row, half_rows, 0).astype(jnp.bfloat16)
    received = lax.ppermute(theirs, "mp", [(0, 1), (1, 0)])
    feature_grads = mine + received.astype(jnp.float32)
    my_unit = lax.dynamic_slice_in_dim(unit_rows, start_row, half_rows, 0)
    my_inverse = lax.dynamic_slice_in_dim(inverse, start_row, half_rows, 0)
    my_cotangent = lax.dynamic_slice_in_dim(cotangent, start_row, half_rows, 0).astype(jnp.float32)
    grad_frames = (
        my_cotangent + norm_back(feature_grads, my_unit, my_inverse) + mean_grads
    ).astype(jnp.bfloat16)
    return (grad_frames, grad_weights, grad_summary)


def solution(mesh):
    in_specs = (P("tm", None), P("tm", None), P(None, None, "mp"), P(), P())
    out_specs = (P(("tm", "mp"), None), P("tm", None, "mp"), P())
    return jax.shard_map(shards, mesh=mesh, in_specs=in_specs, out_specs=out_specs, check_vma=False)
```

```python
import numpy as np
import jax
import jax.numpy as jnp
from jax import lax
from jax.sharding import PartitionSpec as P

HEAD_DIM = 64
WINDOW = 512


EPSILON = 1e-05
PRECISE = lax.Precision.HIGHEST


def from_behind(shard, axis, by):
    devices = lax.axis_size(axis)
    pairs = [(i, i + by) for i in range(devices) if 0 <= i + by < devices]
    return lax.ppermute(shard, axis, pairs)


def tm_coords(i):
    return (i >> 4) & 3, (i >> 3) & 1, (i >> 1) & 3, i & 1


def tm_index(x, y_half, z, core):
    return ((x * 2 + y_half) * 4 + z) * 2 + core


def butterfly_plan():
    pairs, bits = [], np.zeros((64, 6), np.int32)
    flips = [("z", 1), ("x", 1), ("z", 2), ("x", 2), ("y", 1)]
    round_pairs = [[(i, i ^ 1) for i in range(64)]]
    for i in range(64):
        bits[i, 0] = i & 1
    for r, (axis, mask) in enumerate(flips):
        these = []
        for i in range(64):
            x, y_half, z, core = tm_coords(i)
            zl, xl = (z + core) % 4, (x + core) % 4
            label = {"z": zl, "x": xl, "y": y_half}[axis]
            bits[i, r + 1] = 1 if label & mask else 0
            if axis == "z":
                z = ((zl ^ mask) - core) % 4
            elif axis == "x":
                x = ((xl ^ mask) - core) % 4
            else:
                y_half ^= 1
            these.append((i, tm_index(x, y_half, z, core)))
        round_pairs.append(these)
    pairs = round_pairs
    return pairs, bits


def to_positions(a):
    rows = a.shape[0]
    r = a.reshape(rows, 4, 2, 4, 2, 16)
    first = r[:, :, :, :, 0, :]
    second = jnp.roll(jnp.roll(r[:, :, :, :, 1, :], 1, axis=1), 1, axis=3)
    g = jnp.stack([first, second], axis=1).reshape(rows, 2, 2, 2, 2, 2, 2, 16)
    g = g.transpose(0, 1, 6, 3, 5, 2, 4, 7)
    return g.reshape(rows, 1024)


GLOB_FLIPS = (1, 2, 16, 4, 32, 8)


def butterfly(parts, glob, shard_index):
    pairs, bits = butterfly_plan()
    my_bits = jnp.asarray(bits)[shard_index]
    for r in range(6):
        half = parts.shape[0] // 2
        b = my_bits[r]
        keep = lax.dynamic_slice_in_dim(parts, b * half, half, 0)
        send = lax.dynamic_slice_in_dim(parts, (1 - b) * half, half, 0)
        if r in (1, 2):
            got = lax.ppermute(send.astype(jnp.bfloat16), "tm", pairs[r]).astype(jnp.float32)
        else:
            got = lax.ppermute(send, "tm", pairs[r])
        parts = keep + got
        sent_glob = lax.ppermute(
            glob.astype(jnp.bfloat16), "tm", [(i, i ^ GLOB_FLIPS[r]) for i in range(64)]
        )
        glob = glob.astype(jnp.bfloat16).astype(jnp.float32) + sent_glob.astype(jnp.float32)
    return parts, glob


def normalize(rows_in):
    inverse = lax.rsqrt(jnp.mean(rows_in * rows_in, axis=-1, keepdims=True) + EPSILON)
    return (rows_in * inverse, inverse)


def norm_back(gradient, unit_rows, inverse):
    return (gradient - unit_rows * jnp.mean(gradient * unit_rows, axis=-1, keepdims=True)) * inverse


def product(form, left, right):
    return jnp.einsum(form, left, right, preferred_element_type=jnp.float32)


def window_mask(row_count, lead, root):
    query_pos = lax.broadcasted_iota(jnp.int32, (row_count, row_count + lead), 0)
    key_pos = lax.broadcasted_iota(jnp.int32, (row_count, row_count + lead), 1)
    inside = (key_pos > query_pos) & (key_pos <= query_pos + lead)
    return inside & (root - lead + key_pos >= 0)


def block_pass(queries, keys_ext, values_ext, keys_glob, values_glob, grad_rows, allowed):
    scaling = HEAD_DIM ** (-0.5)
    near_scores = product("qhe,khe->hqk", queries, keys_ext) * scaling
    far_scores = product("qhe,khe->hqk", queries, keys_glob) * scaling
    near_scores = jnp.where(allowed[None, :, :], near_scores, -jnp.inf)
    row_top = jnp.maximum(
        jnp.max(near_scores, axis=-1, keepdims=True), jnp.max(far_scores, axis=-1, keepdims=True)
    )
    near_exp = jnp.exp(near_scores - row_top)
    far_exp = jnp.exp(far_scores - row_top)
    row_total = jnp.sum(near_exp, axis=-1, keepdims=True) + jnp.sum(far_exp, axis=-1, keepdims=True)
    near_prob = (near_exp / row_total).astype(jnp.bfloat16)
    far_prob = (far_exp / row_total).astype(jnp.bfloat16)
    attended = (
        product("hqk,khe->qhe", near_prob, values_ext)
        + product("hqk,khe->qhe", far_prob, values_glob)
    ).astype(jnp.bfloat16)
    near_dot = product("qhe,khe->hqk", grad_rows, values_ext)
    far_dot = product("qhe,khe->hqk", grad_rows, values_glob)
    near_p32 = near_prob.astype(jnp.float32)
    far_p32 = far_prob.astype(jnp.float32)
    row_delta = jnp.sum(near_p32 * near_dot, axis=-1, keepdims=True) + jnp.sum(
        far_p32 * far_dot, axis=-1, keepdims=True
    )
    near_grad = (near_p32 * (near_dot - row_delta) * scaling).astype(jnp.bfloat16)
    far_grad = (far_p32 * (far_dot - row_delta) * scaling).astype(jnp.bfloat16)
    query_grad = (
        product("hqk,khe->qhe", near_grad, keys_ext) + product("hqk,khe->qhe", far_grad, keys_glob)
    ).astype(jnp.bfloat16)
    key_grad = product("hqk,qhe->khe", near_grad, queries)
    value_grad = product("hqk,qhe->khe", near_prob, grad_rows)
    glob_key_grad = product("hqk,qhe->khe", far_grad, queries)
    glob_value_grad = product("hqk,qhe->khe", far_prob, grad_rows)
    return (attended, query_grad, key_grad, value_grad, glob_key_grad, glob_value_grad)


def shards(frames, cotangent, weights, summary, owners):
    rows_here = frames.shape[0]
    width = frames.shape[1]
    local_width = weights.shape[2]
    heads_here = local_width // HEAD_DIM
    glob_count = summary.shape[0]
    shard_index = lax.axis_index("tm")
    shard_total = lax.axis_size("tm")
    mp_index = lax.axis_index("mp")
    mp_total = lax.axis_size("mp")
    frames32 = frames.astype(jnp.float32)
    unit_rows, inverse = normalize(frames32)
    normed = unit_rows.astype(jnp.bfloat16)
    block_mean = jnp.mean(frames32, axis=0, keepdims=True)
    pool_unit, pool_inv = normalize(block_mean)
    pooled = pool_unit.astype(jnp.bfloat16)
    slots = lax.broadcasted_iota(jnp.int32, (shard_total, 1), 0)
    pooled_all = jnp.where(slots == shard_index, pooled, jnp.zeros_like(pooled))
    for step in range(3):
        shift = 2 * step
        pooled_all = pooled_all + sum(
            lax.ppermute(pooled_all, "tm", [(i, i ^ (d << shift)) for i in range(64)])
            for d in (1, 2, 3)
        )
    owned_mask = (owners == shard_index).astype(jnp.float32)[:, None]
    anchor = summary.astype(jnp.float32) + jnp.take(pooled_all, owners, axis=0).astype(jnp.float32)
    glob_unit, glob_inv = normalize(anchor)
    glob_normed = glob_unit.astype(jnp.bfloat16)
    stacked = jnp.transpose(weights, (1, 0, 2))
    glob_kv = product("gf,kfc->gkc", glob_normed, stacked[1:3]).astype(jnp.bfloat16)
    glob_kv = glob_kv.reshape(glob_count, 2 * local_width)
    qkv = product("tf,kfc->tkc", normed, stacked[:3]).astype(jnp.bfloat16)
    qkv = qkv.reshape(rows_here, 3 * local_width)
    keys_local = qkv[:, local_width : 2 * local_width]
    values_local = qkv[:, 2 * local_width :]
    queries = qkv[:, :local_width].reshape(rows_here, heads_here, HEAD_DIM)
    grad_attended = jnp.dot(cotangent, stacked[3], preferred_element_type=jnp.float32).astype(
        jnp.bfloat16
    )
    grad_attended = grad_attended.reshape(rows_here, heads_here, HEAD_DIM)
    edge = from_behind(qkv[:, local_width:], "tm", 1)
    edge_keys, edge_values = edge[:, :local_width], edge[:, local_width:]
    keys_ext = jnp.concatenate([edge_keys, keys_local], 0).reshape(
        rows_here + WINDOW, heads_here, HEAD_DIM
    )
    values_ext = jnp.concatenate([edge_values, values_local], 0).reshape(
        rows_here + WINDOW, heads_here, HEAD_DIM
    )
    keys_glob = glob_kv[:, :local_width].reshape(glob_count, heads_here, HEAD_DIM)
    values_glob = glob_kv[:, local_width:].reshape(glob_count, heads_here, HEAD_DIM)
    allowed = window_mask(WINDOW, WINDOW, shard_index * rows_here + 0)
    results = block_pass(
        queries, keys_ext, values_ext, keys_glob, values_glob, grad_attended, allowed
    )
    attended = results[0].reshape(rows_here, local_width)
    grad_queries = results[1].reshape(rows_here, local_width)
    grad_kp = results[2].reshape(rows_here + WINDOW, local_width)
    grad_vp = results[3].reshape(rows_here + WINDOW, local_width)
    grad_kg = results[4].reshape(glob_count, local_width)
    grad_vg = results[5].reshape(glob_count, local_width)
    back = from_behind(
        jnp.concatenate([grad_kp[:WINDOW], grad_vp[:WINDOW]], 1).astype(jnp.bfloat16), "tm", -1
    )
    back_keys, back_values = back[:, :local_width], back[:, local_width:]
    grad_keys = grad_kp[WINDOW:].at[rows_here - WINDOW :].add(back_keys.astype(jnp.float32))
    grad_values = grad_vp[WINDOW:].at[rows_here - WINDOW :].add(back_values.astype(jnp.float32))
    grad_cat = jnp.concatenate(
        [grad_queries, grad_keys.astype(jnp.bfloat16), grad_values.astype(jnp.bfloat16)], 1
    )
    glob_grads = jnp.concatenate([grad_kg, grad_vg], 1)
    local_features = jnp.einsum(
        "gkc,kfc->gf",
        glob_grads.reshape(glob_count, 2, local_width),
        stacked[1:3].astype(jnp.float32),
        precision=PRECISE,
    )
    glob_cols = to_positions(glob_normed).astype(jnp.float32)
    inner = lax.dot_general(
        to_positions(normed), grad_cat, (((0,), (0,)), ((), ())), preferred_element_type=jnp.float32
    )
    glob_term = lax.dot_general(glob_cols, glob_grads, (((0,), (0,)), ((), ())), precision=PRECISE)
    inner = inner + jnp.concatenate([jnp.zeros((width, local_width), jnp.float32), glob_term], 1)
    last_term = lax.dot_general(
        to_positions(cotangent), attended, (((0,), (0,)), ((), ())), preferred_element_type=jnp.float32
    )
    weight_parts = jnp.concatenate(
        [inner.reshape(width, 3, local_width), last_term.reshape(width, 1, local_width)], 1
    )
    weight_rows, tm_features = butterfly(
        weight_parts.reshape(width, 4 * local_width), local_features, shard_index
    )
    grad_weights = weight_rows.reshape(width // shard_total, 4, local_width)
    tm_rounded = tm_features.astype(jnp.bfloat16)
    summary_features = tm_rounded.astype(jnp.float32) + lax.ppermute(
        tm_rounded, "mp", [(0, 1), (1, 0)]
    ).astype(jnp.float32)
    grad_summary = norm_back(summary_features, glob_unit, glob_inv)
    pool_grads = lax.dot_general(
        owned_mask, grad_summary, (((0,), (0,)), ((), ())), precision=PRECISE
    )
    mean_grads = norm_back(pool_grads, pool_unit, pool_inv) / rows_here
    half_rows = rows_here // mp_total
    start_row = mp_index * half_rows
    other_row = (1 - mp_index) * half_rows
    feature_all = product("tkc,kfc->tf", grad_cat.reshape(rows_here, 3, local_width), stacked[:3])
    mine = lax.dynamic_slice_in_dim(feature_all, start_row, half_rows, 0)
    theirs = lax.dynamic_slice_in_dim(feature_all, other_row, half_rows, 0).astype(jnp.bfloat16)
    received = lax.ppermute(theirs, "mp", [(0, 1), (1, 0)])
    feature_grads = mine + received.astype(jnp.float32)
    my_unit = lax.dynamic_slice_in_dim(unit_rows, start_row, half_rows, 0)
    my_inverse = lax.dynamic_slice_in_dim(inverse, start_row, half_rows, 0)
    my_cotangent = lax.dynamic_slice_in_dim(cotangent, start_row, half_rows, 0).astype(jnp.float32)
    grad_frames = (
        my_cotangent + norm_back(feature_grads, my_unit, my_inverse) + mean_grads
    ).astype(jnp.bfloat16)
    return (grad_frames, grad_weights, grad_summary)


def solution(mesh):
    in_specs = (P("tm", None), P("tm", None), P(None, None, "mp"), P(), P())
    out_specs = (P(("tm", "mp"), None), P("tm", None, "mp"), P())
    return jax.shard_map(shards, mesh=mesh, in_specs=in_specs, out_specs=out_specs, check_vma=False)
```
